128 devices in a mesh: req: 32 (over z, x, core), mlp: 4 (over y).
Axes of the slice: x: 4, y: 4, z: 4, core: 2. Of those that a mesh axis runs over, the one named last changes fastest.
Arguments:
- tokens: bfloat16 [12288, 2048], P(('req', 'mlp')), may hold values from -6 to 6
- lengths: int32 [4], replicated, may hold values from 1 to 6144, 12288 in all
- in_gain: float32 [2048], replicated, may hold values from 0.5 to 1.5
- w_query: bfloat16 [2048, 2048], P(None, 'mlp'), may hold values from -0.125 to 0.125
- w_key: bfloat16 [2048, 2048], P(None, 'mlp'), may hold values from -1 to 1
- w_value: bfloat16 [2048, 4096], P(None, 'mlp'), may hold values from -0.125 to 0.125
- w_gate: bfloat16 [2048, 4096], P(None, 'mlp'), may hold values from -0.125 to 0.125
- w_beta: bfloat16 [2048, 16], P(None, 'mlp'), may hold values from -0.125 to 0.125
- w_decay: bfloat16 [2048, 16], P(None, 'mlp'), may hold values from -0.125 to 0.125
- decay_log: float32 [16], P('mlp'), may hold values from -11 to 0
- decay_bias: float32 [16], P('mlp'), may hold values from -3 to 1
- conv_query: float32 [4, 2048], P(None, 'mlp'), may hold values from -2.5 to 2.5
- conv_key: float32 [4, 2048], P(None, 'mlp'), may hold values from -2.5 to 2.5
- conv_value: float32 [4, 4096], P(None, 'mlp'), may hold values from -2.5 to 2.5
- head_gain: float32 [256], replicated, may hold values from 0.5 to 1.5
- w_out: bfloat16 [4096, 2048], P('mlp'), may hold values from -0.09375 to 0.09375
- mlp_gain: float32 [2048], replicated, may hold values from 0.5 to 1.5
- w_up_gate: bfloat16 [2048, 5632], P('req', 'mlp'), may hold values from -0.125 to 0.125
- w_up: bfloat16 [2048, 5632], P('req', 'mlp'), may hold values from -0.125 to 0.125
- w_down: bfloat16 [5632, 2048], P('mlp', 'req'), may hold values from -0.078125 to 0.078125
Outputs:
- layer_out: bfloat16 [12288, 2048], P(('req', 'mlp'))
The draws below stay inside these ranges and needn't reach their ends.
Inputs may be any that keep to these rules, and one draw needn't show every extreme that they name: The 4 prompts lie end to end in the order given and their lengths sum to 12288; the longest has exactly 6144 tokens.
All inputs are finite; a program needn't handle non-finite values.
Results may differ from the reference program's by a relative error of at most 0.017.
Values may be sent and summed in bfloat16 or wider, within the bound.
No kernel may reach another device: no remote copies, remote signals or barrier semaphores. Data moves between devices by JAX's collectives and lax.ppermute only.
A program may use at most 128 MiB of HBM per device.

```python
import math
import jax
import jax.numpy as jnp
import numpy as np
from jax import lax

D = 2048
HEADS = 16
DK = 128
DV = 256
FF = 5632
CONV = 4
GROUP = 64
PROMPTS = 4
TOKENS = 12288
LONGEST = 6144


def slow_heads(key, slow_count):
    ranking = jax.random.permutation(jax.random.fold_in(key, 101), HEADS)
    return ranking < slow_count


def draw_decay_log(key, part):
    slow_count = HEADS // 2
    lower_factor = 1.0
    upper_factor = 4.0
    slow_mask = slow_heads(key, slow_count)
    reach_factor = jax.random.uniform(jax.random.fold_in(key, 102), (HEADS,), jnp.float32, lower_factor, upper_factor)
    slow_value = jnp.log(reach_factor / LONGEST)
    fast_value = jax.random.uniform(jax.random.fold_in(key, 103), (HEADS,), jnp.float32, -3.0, 0.0)
    return jnp.where(slow_mask, slow_value, fast_value).astype(jnp.float32)


def draw_decay_bias(key, part):
    slow_count = HEADS // 2
    slow_mask = slow_heads(key, slow_count)
    slow_value = jax.random.uniform(jax.random.fold_in(key, 104), (HEADS,), jnp.float32, -3.0, -2.0)
    fast_value = jax.random.uniform(jax.random.fold_in(key, 105), (HEADS,), jnp.float32, -1.0, 1.0)
    return jnp.where(slow_mask, slow_value, fast_value).astype(jnp.float32)


def draw_w_key(key, part):
    column_scale = jnp.exp(jax.random.uniform(jax.random.fold_in(key, 111), (HEADS * DK,), jnp.float32, -3.0, 0.0))
    entries = jax.random.truncated_normal(jax.random.fold_in(key, 112), -6.0, 6.0, (D, HEADS * DK), jnp.float32)
    return (entries * D ** (-0.5) * column_scale[None, :]).astype(jnp.bfloat16)


def block_levels(own_key, extent, shards, least, largest):
    def one(dim, shards_of):
        steps = jax.random.uniform(jax.random.fold_in(jax.random.fold_in(own_key, 6), dim), (shards_of,), jnp.float32, least / len(shards), largest / len(shards))
        return jnp.repeat(jnp.exp(steps), extent[dim] // shards_of).reshape((-1,) + (1,) * (len(extent) - dim - 1))

    level = one(*shards[0])
    for cut in shards[1:]:
        level = level * one(*cut)
    return level


def length_profile(count, total, limit, slope):
    loads = [(1 << 20) // math.isqrt(rank ** slope) + 1 for rank in range(2, count + 1)]
    rest, counts = total - limit - (count - 1), [1] * (count - 1)
    while rest > 0:
        candidates = [i for i in range(count - 1) if counts[i] < limit]
        whole, budget = sum([loads[i] for i in candidates]), rest
        for i in candidates:
            more = min(limit - counts[i], max(1, budget * loads[i] // whole), rest)
            counts[i] = counts[i] + more
            rest = rest - more
    return np.array([limit] + counts)


def ragged(stream_key, count, total, limit, skew):
    if count == 2:
        one = jax.random.randint(stream_key, (), max(1, total - limit), min(limit, total - 1) + 1)
        return jnp.stack([one, total - one])
    tallies = jnp.asarray(length_profile(count, total, limit, skew), jnp.int32)
    couples = (count - 1) // 2
    giver, receiver = tallies[1:1 + 2 * couples:2], tallies[2:2 + 2 * couples:2]
    margin = jnp.minimum(giver - 1, limit - receiver)
    passed = jax.random.randint(jax.random.fold_in(stream_key, 1), (couples,), 0, 1 << 20) % (margin + 1)
    tallies = tallies.at[1:1 + 2 * couples:2].set(giver - passed).at[2:2 + 2 * couples:2].set(receiver + passed)
    return tallies[jax.random.permutation(jax.random.fold_in(stream_key, 2), count)]


def normal_values(own_key, shape, deviation, most, cuts=(), held_as=jnp.bfloat16):
    factor_of = block_levels(own_key, shape, cuts, -0.22, 0.18) if cuts else 1.0
    array = jax.random.normal(own_key, shape, jnp.float32) * deviation * factor_of
    return jnp.minimum(jnp.maximum(array, -most), most).astype(held_as)


def setup_inputs(seed: int = 0) -> dict:
    keys = jax.random.split(jax.random.key(seed), 21)
    tokens = normal_values(keys[0], (TOKENS, D), 1.0, 6.0, ((0, 128),))
    lengths = ragged(keys[1], PROMPTS, TOKENS, LONGEST, 2).astype(jnp.int32)
    in_gain = jnp.clip(1.0 + 0.1 * jax.random.normal(keys[2], (D,), jnp.float32), 0.5, 1.5)
    w_query = normal_values(keys[3], (D, HEADS * DK), D ** -0.5, 0.125, ((1, 4),))
    w_key = draw_w_key(jax.random.fold_in(keys[20], 71), 0)
    w_value = normal_values(keys[5], (D, HEADS * DV), D ** -0.5, 0.125, ((1, 4),))
    w_gate = normal_values(keys[6], (D, HEADS * DV), D ** -0.5, 0.125, ((1, 4),))
    w_beta = normal_values(keys[7], (D, HEADS), D ** -0.5, 0.125, ((1, 4),))
    w_decay = normal_values(keys[8], (D, HEADS), D ** -0.5, 0.125, ((1, 4),))
    decay_log = draw_decay_log(jax.random.fold_in(keys[20], 71), 0)
    decay_bias = draw_decay_bias(jax.random.fold_in(keys[20], 71), 0)
    conv_query = normal_values(keys[11], (CONV, HEADS * DK), 0.5, 2.5, ((1, 4),), jnp.float32)
    conv_key = normal_values(keys[12], (CONV, HEADS * DK), 0.5, 2.5, ((1, 4),), jnp.float32)
    conv_value = normal_values(keys[13], (CONV, HEADS * DV), 0.5, 2.5, ((1, 4),), jnp.float32)
    head_gain = jnp.clip(1.0 + 0.1 * jax.random.normal(keys[14], (DV,), jnp.float32), 0.5, 1.5)
    w_out = normal_values(keys[15], (HEADS * DV, D), (HEADS * DV) ** -0.5, 0.09375, ((0, 4),))
    mlp_gain = jnp.clip(1.0 + 0.1 * jax.random.normal(keys[16], (D,), jnp.float32), 0.5, 1.5)
    w_up_gate = normal_values(keys[17], (D, FF), D ** -0.5, 0.125, ((0, 32), (1, 4)))
    w_up = normal_values(keys[18], (D, FF), D ** -0.5, 0.125, ((0, 32), (1, 4)))
    w_down = normal_values(keys[19], (FF, D), FF ** -0.5, 0.078125, ((0, 4), (1, 32)))
    return {"tokens": tokens, "lengths": lengths, "in_gain": in_gain, "w_query": w_query, "w_key": w_key, "w_value": w_value, "w_gate": w_gate, "w_beta": w_beta, "w_decay": w_decay, "decay_log": decay_log, "decay_bias": decay_bias, "conv_query": conv_query, "conv_key": conv_key, "conv_value": conv_value, "head_gain": head_gain, "w_out": w_out, "mlp_gain": mlp_gain, "w_up_gate": w_up_gate, "w_up": w_up, "w_down": w_down}


maximal_matmul_accuracy = lax.Precision.HIGHEST

def rms_scale(values, gain):
    mean_square = lax.optimization_barrier(jnp.mean(values * values, axis=-1, keepdims=True))
    return values / jnp.sqrt(mean_square + 1e-06) * gain

def unit_norm(values):
    return values / jnp.sqrt(lax.optimization_barrier(jnp.sum(values * values, axis=-1, keepdims=True)) + 1e-06)

def segment_of(positions, lengths):
    bounds = jnp.cumsum(lengths).astype(jnp.int32)[:-1]
    return lax.optimization_barrier(jnp.sum((positions[:, None] >= bounds[None, :]).astype(jnp.int32), axis=1)).astype(jnp.int32)

def causal_conv(projected, rim_rows, kernel, segment_ids, rim_segments):
    taps_count = kernel.shape[0]
    row_count = projected.shape[0]
    extended = jnp.concatenate([rim_rows, projected], axis=0).astype(jnp.float32)
    extended_ids = jnp.concatenate([rim_segments, segment_ids], axis=0)
    accumulated = jnp.zeros(projected.shape, jnp.float32)
    for offset in range(taps_count):
        window = lax.slice_in_dim(extended, offset, offset + row_count, axis=0)
        window_ids = lax.slice_in_dim(extended_ids, offset, offset + row_count, axis=0)
        same_doc = (window_ids == segment_ids)[:, None]
        accumulated = accumulated + kernel[offset][None, :] * jnp.where(same_doc, window, 0.0)
    return accumulated

def group_parts(query_vecs, key_vecs, value_vecs, beta_vals, log_decay, segment_ids, prior_segment):
    group_rows = query_vecs.shape[0]
    value_dim = value_vecs.shape[-1]
    cumulative = jnp.cumsum(log_decay, axis=0)
    row_index = jnp.arange(group_rows)[:, None]
    col_index = jnp.arange(group_rows)[None, :]
    same_doc = segment_ids[:, None] == segment_ids[None, :]
    keep_mask = ((row_index >= col_index) & same_doc)[None, :, :]
    strict_mask = (row_index > col_index)[None, :, :]
    head_cumul = jnp.transpose(cumulative)
    gaps = head_cumul[:, :, None] - head_cumul[:, None, :]
    weights = jnp.where(keep_mask, jnp.exp(jnp.where(keep_mask, gaps, 0.0)), 0.0)
    open_mask = (segment_ids == prior_segment).astype(query_vecs.dtype)
    start_decay = jnp.exp(cumulative) * open_mask[:, None]
    key_dots = jnp.einsum('ihd,jhd->hij', key_vecs, key_vecs, precision=maximal_matmul_accuracy)
    coupling = jnp.where(strict_mask, jnp.transpose(beta_vals)[:, :, None] * weights * key_dots, 0.0)
    system = coupling + jnp.eye(group_rows, dtype=query_vecs.dtype)[None]
    targets = jnp.concatenate([beta_vals[:, :, None] * value_vecs, (beta_vals * start_decay)[:, :, None] * key_vecs], axis=-1)
    solved = jax.scipy.linalg.solve_triangular(system, jnp.transpose(targets, (1, 0, 2)), lower=True, unit_diagonal=True)
    starting_value_rows = solved[:, :, :value_dim]
    delta_correction = solved[:, :, value_dim:]
    query_dots = weights * jnp.einsum('ihd,jhd->hij', query_vecs, key_vecs, precision=maximal_matmul_accuracy)
    query_begin_offset = query_vecs * start_decay[:, :, None]
    final_key_rows = key_vecs * jnp.transpose(weights[:, -1, :])[:, :, None]
    carried_decay_factor = start_decay[-1]
    return (starting_value_rows, delta_correction, query_dots, query_begin_offset, final_key_rows, carried_decay_factor)

def group_step(running_state, parts):
    starting_value_rows, delta_correction, query_dots, query_begin_offset, final_key_rows, carried_decay_factor = parts
    fresh_state_update = starting_value_rows - jnp.einsum('mxf,mft->mxt', delta_correction, running_state, precision=maximal_matmul_accuracy)
    output_rows = jnp.einsum('fob,obt->fot', query_begin_offset, running_state, precision=maximal_matmul_accuracy)
    output_rows = output_rows + jnp.einsum('hij,hjv->ihv', query_dots, fresh_state_update, precision=maximal_matmul_accuracy)
    updated_state = carried_decay_factor[:, None, None] * running_state + jnp.einsum('new,enr->ewr', final_key_rows, fresh_state_update, precision=maximal_matmul_accuracy)
    return (updated_state, output_rows)

def reference(tokens, lengths, in_gain, w_query, w_key, w_value, w_gate, w_beta, w_decay, decay_log, decay_bias, conv_query, conv_key, conv_value, head_gain, w_out, mlp_gain, w_up_gate, w_up, w_down):
    token_rows = tokens.astype(jnp.float32)
    normed = rms_scale(token_rows, in_gain).astype(jnp.bfloat16)
    positions = jnp.arange(TOKENS, dtype=jnp.int32)
    segment_ids = segment_of(positions, lengths)
    taps_count = conv_query.shape[0]
    rim_segments = segment_of(jnp.arange(taps_count - 1, dtype=jnp.int32) - (taps_count - 1), lengths)

    def convolved(weight, kernel):
        projected = jnp.dot(normed.astype(jnp.float32), weight.astype(jnp.float32), preferred_element_type=jnp.float32).astype(jnp.bfloat16)
        rim_rows = jnp.zeros((taps_count - 1, projected.shape[1]), jnp.bfloat16)
        return jax.nn.silu(causal_conv(projected, rim_rows, kernel, segment_ids, rim_segments))
    query_vecs = unit_norm(convolved(w_query, conv_query).reshape(TOKENS, HEADS, DK)) * DK ** (-0.5)
    key_vecs = unit_norm(convolved(w_key, conv_key).reshape(TOKENS, HEADS, DK))
    value_vecs = convolved(w_value, conv_value).reshape(TOKENS, HEADS, DV)
    gate_lin = jnp.dot(normed.astype(jnp.float32), w_gate.astype(jnp.float32), preferred_element_type=jnp.float32).astype(jnp.bfloat16)
    beta_vals = jax.nn.sigmoid(jnp.dot(normed.astype(jnp.float32), w_beta.astype(jnp.float32), preferred_element_type=jnp.float32))
    log_decay = -jnp.exp(decay_log) * jax.nn.softplus(jnp.dot(normed.astype(jnp.float32), w_decay.astype(jnp.float32), preferred_element_type=jnp.float32) + decay_bias)
    group_total = TOKENS // GROUP

    def shaped(values):
        return values.reshape((group_total, GROUP) + values.shape[1:])
    prior_ids = segment_of(jnp.arange(group_total, dtype=jnp.int32) * GROUP - 1, lengths)

    def advance(running_state, inputs_one):
        return group_step(running_state, group_parts(*inputs_one))
    initial = jnp.zeros((HEADS, DK, DV), jnp.float32)
    _, output_rows = lax.scan(advance, initial, (shaped(query_vecs), shaped(key_vecs), shaped(value_vecs), shaped(beta_vals), shaped(log_decay), shaped(segment_ids), prior_ids))
    output_rows = output_rows.reshape(TOKENS, HEADS, DV)
    gate_vals = jax.nn.silu(gate_lin.astype(jnp.float32)).reshape(TOKENS, HEADS, DV)
    head_out = (rms_scale(output_rows, head_gain) * gate_vals).reshape(TOKENS, HEADS * DV).astype(jnp.bfloat16)
    resid = token_rows + jnp.dot(head_out.astype(jnp.float32), w_out.astype(jnp.float32), preferred_element_type=jnp.float32)
    mlp_in = rms_scale(resid, mlp_gain).astype(jnp.bfloat16)
    gate_acc = jnp.dot(mlp_in.astype(jnp.float32), w_up_gate.astype(jnp.float32), preferred_element_type=jnp.float32)
    up_acc = jnp.dot(mlp_in.astype(jnp.float32), w_up.astype(jnp.float32), preferred_element_type=jnp.float32)
    hidden = (jax.nn.silu(gate_acc) * up_acc).astype(jnp.bfloat16)
    return (resid + jnp.dot(hidden.astype(jnp.float32), w_down.astype(jnp.float32), preferred_element_type=jnp.float32)).astype(jnp.bfloat16)
```

```python
import jax
import jax.numpy as jnp
from jax import lax
from jax.sharding import PartitionSpec as P

GROUP = 64


maximal_matmul_accuracy = lax.Precision.HIGHEST


def shifted(value, axis, steps):
    count = lax.axis_size(axis)
    first, last = (max(0, -steps), min(count, count - steps))
    return lax.ppermute(value, axis, [(source, source + steps) for source in range(first, last)])


def carried_in(shard, axis, combine, identity):
    length, index = (lax.axis_size(axis), lax.axis_index(axis))
    everything = jax.tree.map(
        lambda part, kind: lax.all_gather(part.astype(kind), axis),
        shard,
        jax.tree.map(lambda a: jnp.bfloat16 if a.dtype == jnp.float32 else a.dtype, shard),
    )
    start = jax.tree.map(
        lambda part, zero: jnp.broadcast_to(jnp.asarray(zero, part.dtype), part.shape),
        shard,
        identity,
    )

    def step(k, before):
        reached = k < index
        new = combine(
            before, jax.tree.map(lambda part, own: part[k].astype(own.dtype), everything, shard)
        )
        return jax.tree.map(lambda a, b: jnp.where(reached, a, b), new, before)

    return lax.fori_loop(0, length, step, start)


def prefix_state(piece_map, eye_block):
    index, count = lax.axis_index("req"), lax.axis_size("req")
    linear, additive = piece_map
    opened = index >= 1
    linear = jnp.where(opened, shifted(linear, "req", 1), eye_block)
    additive = jnp.where(opened, shifted(additive, "req", 1), 0.0)
    reach = 1
    while reach < count:
        reached = index >= reach
        if 2 * reach >= count:
            got_add = shifted(additive, "req", reach)
            additive = jnp.where(
                reached,
                jnp.einsum("baf,bfu->bau", linear, got_add, precision=maximal_matmul_accuracy)
                + additive,
                additive,
            )
        else:
            got_lin, got_add = shifted((linear, additive), "req", reach)
            new_lin, new_add = combine_maps((got_lin, got_add), (linear, additive))
            linear = jnp.where(reached, new_lin, linear)
            additive = jnp.where(reached, new_add, additive)
        reach *= 2
    return additive


def gather_rows(share, axis):
    count, index = lax.axis_size(axis), lax.axis_index(axis)
    pieces = [share] + [
        lax.ppermute(share, axis, [(j, (j - s) % count) for j in range(count)])
        for s in range(1, count)
    ]
    return jnp.roll(jnp.stack(pieces), index, axis=0).reshape((-1,) + share.shape[1:])


def scatter_sum(full, axis):
    count, index = lax.axis_size(axis), lax.axis_index(axis)
    rows = full.shape[0] // count
    total = lax.dynamic_slice_in_dim(full, index * rows, rows, 0).astype(jnp.float32)
    for s in range(1, count):
        part = lax.dynamic_slice_in_dim(full, ((index + s) % count) * rows, rows, 0)
        got = lax.ppermute(part, axis, [(j, (j + s) % count) for j in range(count)])
        total = total + got.astype(jnp.float32)
    return total


def rms_scale(values, gain):
    mean_square = jnp.mean(values * values, axis=-1, keepdims=True)
    return values / jnp.sqrt(mean_square + 1e-06) * gain


def unit_norm(values):
    return values / jnp.sqrt(jnp.sum(values * values, axis=-1, keepdims=True) + 1e-06)


def segment_of(positions, lengths):
    bounds = jnp.cumsum(lengths)[:-1]
    return jnp.sum((positions[:, None] >= bounds[None, :]).astype(jnp.int32), axis=1)


def causal_conv(projected, rim_rows, kernel, segment_ids, rim_segments):
    taps_count = kernel.shape[0]
    row_count = projected.shape[0]
    extended = jnp.concatenate([rim_rows, projected], axis=0).astype(jnp.float32)
    extended_ids = jnp.concatenate([rim_segments, segment_ids], axis=0)
    accumulated = jnp.zeros(projected.shape, jnp.float32)
    for offset in range(taps_count):
        window = lax.slice_in_dim(extended, offset, offset + row_count, axis=0)
        window_ids = lax.slice_in_dim(extended_ids, offset, offset + row_count, axis=0)
        same_doc = (window_ids == segment_ids)[:, None]
        accumulated = accumulated + kernel[offset][None, :] * jnp.where(same_doc, window, 0.0)
    return accumulated


def unit_lower_inverse(system):
    size = system.shape[-1]
    rows = jnp.arange(size)[:, None]
    cols = jnp.arange(size)[None, :]
    inverse = jnp.broadcast_to(jnp.eye(size, dtype=system.dtype), system.shape)
    block = 1
    while block < size:
        lower_left = (
            (rows // (2 * block) == cols // (2 * block))
            & ((rows // block) % 2 == 1)
            & ((cols // block) % 2 == 0)
        )
        coupling = jnp.where(lower_left, system, 0.0)
        joined = jnp.einsum(
            "hij,hjk->hik",
            jnp.einsum("hij,hjk->hik", inverse, coupling, precision=maximal_matmul_accuracy),
            inverse,
            precision=maximal_matmul_accuracy,
        )
        inverse = inverse - joined
        block *= 2
    return inverse


def group_parts(query_vecs, key_vecs, value_vecs, beta_vals, log_decay, segment_ids, prior_segment):
    group_rows = query_vecs.shape[0]
    value_dim = value_vecs.shape[-1]
    cumulative = jnp.cumsum(log_decay, axis=0)
    row_index = jnp.arange(group_rows)[:, None]
    col_index = jnp.arange(group_rows)[None, :]
    same_doc = segment_ids[:, None] == segment_ids[None, :]
    keep_mask = ((row_index >= col_index) & same_doc)[None, :, :]
    strict_mask = (row_index > col_index)[None, :, :]
    head_cumul = jnp.transpose(cumulative)
    gaps = head_cumul[:, :, None] - head_cumul[:, None, :]
    weights = jnp.where(keep_mask, jnp.exp(jnp.where(keep_mask, gaps, 0.0)), 0.0)
    open_mask = (segment_ids == prior_segment).astype(query_vecs.dtype)
    start_decay = jnp.exp(cumulative) * open_mask[:, None]
    key_dots = jnp.einsum("ihd,jhd->hij", key_vecs, key_vecs, precision=maximal_matmul_accuracy)
    coupling = jnp.where(
        strict_mask, jnp.transpose(beta_vals)[:, :, None] * weights * key_dots, 0.0
    )
    system = coupling + jnp.eye(group_rows, dtype=query_vecs.dtype)[None]
    targets = jnp.concatenate(
        [beta_vals[:, :, None] * value_vecs, (beta_vals * start_decay)[:, :, None] * key_vecs],
        axis=-1,
    )
    solved = jnp.einsum(
        "hij,hjc->hic",
        unit_lower_inverse(system),
        jnp.transpose(targets, (1, 0, 2)),
        precision=maximal_matmul_accuracy,
    )
    starting_value_rows = solved[:, :, :value_dim]
    delta_correction = solved[:, :, value_dim:]
    query_dots = weights * jnp.einsum(
        "ihd,jhd->hij", query_vecs, key_vecs, precision=maximal_matmul_accuracy
    )
    query_begin_offset = query_vecs * start_decay[:, :, None]
    final_key_rows = key_vecs * jnp.transpose(weights[:, -1, :])[:, :, None]
    carried_decay_factor = start_decay[-1]
    return (
        starting_value_rows,
        delta_correction,
        query_dots,
        query_begin_offset,
        final_key_rows,
        carried_decay_factor,
    )


def group_step(running_state, parts):
    (
        starting_value_rows,
        delta_correction,
        query_dots,
        query_begin_offset,
        final_key_rows,
        carried_decay_factor,
    ) = parts
    fresh_state_update = starting_value_rows - jnp.einsum(
        "mxf,mft->mxt", delta_correction, running_state, precision=maximal_matmul_accuracy
    )
    output_rows = jnp.einsum(
        "fob,obt->fot", query_begin_offset, running_state, precision=maximal_matmul_accuracy
    )
    output_rows = output_rows + jnp.einsum(
        "hij,hjv->ihv", query_dots, fresh_state_update, precision=maximal_matmul_accuracy
    )
    updated_state = carried_decay_factor[:, None, None] * running_state + jnp.einsum(
        "new,enr->ewr", final_key_rows, fresh_state_update, precision=maximal_matmul_accuracy
    )
    return (updated_state, output_rows)


def combine_maps(earlier, later):
    earlier_map, preceding_additive = earlier
    following_linear_map, following_additive = later
    joined_map = jnp.einsum(
        "hkl,hlm->hkm", following_linear_map, earlier_map, precision=maximal_matmul_accuracy
    )
    joined_add = (
        jnp.einsum(
            "baf,bfu->bau",
            following_linear_map,
            preceding_additive,
            precision=maximal_matmul_accuracy,
        )
        + following_additive
    )
    return (joined_map, joined_add)


def per_device(
    tokens,
    lengths,
    in_gain,
    w_query,
    w_key,
    w_value,
    w_gate,
    w_beta,
    w_decay,
    decay_log,
    decay_bias,
    conv_query,
    conv_key,
    conv_value,
    head_gain,
    w_out,
    mlp_gain,
    w_up_gate,
    w_up,
    w_down,
):
    share_rows = tokens.shape[0]
    gathered = gather_rows(tokens, "mlp")
    piece_len = gathered.shape[0]
    head_count = w_beta.shape[1]
    key_dim = w_query.shape[1] // head_count
    value_dim = w_value.shape[1] // head_count
    taps_count = conv_query.shape[0]
    group_count = piece_len // GROUP
    piece_start = lax.axis_index("req") * piece_len
    positions = piece_start + jnp.arange(piece_len, dtype=jnp.int32)
    segment_ids = segment_of(positions, lengths)
    rim_segments = segment_of(
        piece_start - (taps_count - 1) + jnp.arange(taps_count - 1, dtype=jnp.int32), lengths
    )
    token_rows = gathered.astype(jnp.float32)
    normed = rms_scale(token_rows, in_gain).astype(jnp.bfloat16)
    proj_query = jnp.dot(normed, w_query, preferred_element_type=jnp.float32).astype(jnp.bfloat16)
    proj_key = jnp.dot(normed, w_key, preferred_element_type=jnp.float32).astype(jnp.bfloat16)
    proj_value = jnp.dot(normed, w_value, preferred_element_type=jnp.float32).astype(jnp.bfloat16)
    edge_rows = jnp.concatenate(
        [
            proj_query[piece_len - taps_count + 1 :],
            proj_key[piece_len - taps_count + 1 :],
            proj_value[piece_len - taps_count + 1 :],
        ],
        axis=1,
    )
    rim_all = shifted(edge_rows, "req", 1)
    query_width = proj_query.shape[1]
    key_width = proj_key.shape[1]
    rim_query = rim_all[:, :query_width]
    rim_key = rim_all[:, query_width : query_width + key_width]
    rim_value = rim_all[:, query_width + key_width :]
    conv_q = jax.nn.silu(causal_conv(proj_query, rim_query, conv_query, segment_ids, rim_segments))
    conv_k = jax.nn.silu(causal_conv(proj_key, rim_key, conv_key, segment_ids, rim_segments))
    conv_v = jax.nn.silu(causal_conv(proj_value, rim_value, conv_value, segment_ids, rim_segments))
    query_vecs = unit_norm(conv_q.reshape(piece_len, head_count, key_dim)) * key_dim ** (-0.5)
    key_vecs = unit_norm(conv_k.reshape(piece_len, head_count, key_dim))
    value_vecs = conv_v.reshape(piece_len, head_count, value_dim)
    gate_lin = jnp.dot(normed, w_gate, preferred_element_type=jnp.float32).astype(jnp.bfloat16)
    beta_vals = jax.nn.sigmoid(jnp.dot(normed, w_beta, preferred_element_type=jnp.float32))
    log_decay = -jnp.exp(decay_log) * jax.nn.softplus(
        jnp.dot(normed, w_decay, preferred_element_type=jnp.float32) + decay_bias
    )

    def shaped(values):
        return values.reshape((group_count, GROUP) + values.shape[1:])

    prior_ids = segment_of(
        piece_start + jnp.arange(group_count, dtype=jnp.int32) * GROUP - 1, lengths
    )
    parts = jax.vmap(group_parts)(
        shaped(query_vecs),
        shaped(key_vecs),
        shaped(value_vecs),
        shaped(beta_vals),
        shaped(log_decay),
        shaped(segment_ids),
        prior_ids,
    )
    eye_block = jnp.broadcast_to(
        jnp.eye(key_dim, dtype=jnp.float32), (head_count, key_dim, key_dim)
    )
    zero_state = jnp.zeros((head_count, key_dim, value_dim), jnp.float32)

    def compose(carried, parts_one):
        (
            starting_value_rows,
            delta_correction,
            query_dots,
            query_begin_offset,
            final_key_rows,
            carried_decay_factor,
        ) = parts_one
        local_map = carried_decay_factor[:, None, None] * eye_block - jnp.einsum(
            "chk,hcl->hkl", final_key_rows, delta_correction, precision=maximal_matmul_accuracy
        )
        within_piece_additive = jnp.einsum(
            "new,enr->ewr", final_key_rows, starting_value_rows, precision=maximal_matmul_accuracy
        )
        return (combine_maps(carried, (local_map, within_piece_additive)), None)

    piece_maps, _ = lax.scan(compose, (eye_block, zero_state), parts)
    incoming = prefix_state(piece_maps, eye_block)
    _, output_rows = lax.scan(group_step, incoming, parts)
    output_rows = output_rows.reshape(piece_len, head_count, value_dim)
    gate_vals = jax.nn.silu(gate_lin.astype(jnp.float32)).reshape(piece_len, head_count, value_dim)
    head_out = (
        (rms_scale(output_rows, head_gain) * gate_vals)
        .reshape(piece_len, head_count * value_dim)
        .astype(jnp.bfloat16)
    )
    partial_out = jnp.dot(head_out, w_out, preferred_element_type=jnp.float32)
    attn_mine = scatter_sum(partial_out.astype(jnp.bfloat16), "mlp")
    resid_mine = tokens.astype(jnp.float32) + attn_mine
    mlp_in = gather_rows(rms_scale(resid_mine, mlp_gain).astype(jnp.bfloat16), "mlp")

    def add_rows(piece):
        return jnp.dot(mlp_in, piece, preferred_element_type=jnp.float32)

    gate_acc = add_rows(lax.all_gather(w_up_gate, "req", axis=0, tiled=True))
    up_acc = add_rows(lax.all_gather(w_up, "req", axis=0, tiled=True))
    hidden = (jax.nn.silu(gate_acc) * up_acc).astype(jnp.bfloat16)
    down_terms = jnp.dot(
        hidden,
        lax.all_gather(w_down, "req", axis=1, tiled=True),
        preferred_element_type=jnp.float32,
    )
    mlp_share = scatter_sum(down_terms.astype(jnp.bfloat16), "mlp")
    return (resid_mine + mlp_share).astype(jnp.bfloat16)


def solution(mesh):
    placed = (
        P(("req", "mlp"), None),
        P(),
        P(),
        P(None, "mlp"),
        P(None, "mlp"),
        P(None, "mlp"),
        P(None, "mlp"),
        P(None, "mlp"),
        P(None, "mlp"),
        P("mlp"),
        P("mlp"),
        P(None, "mlp"),
        P(None, "mlp"),
        P(None, "mlp"),
        P(),
        P("mlp", None),
        P(),
        P("req", "mlp"),
        P("req", "mlp"),
        P("mlp", "req"),
    )
    return jax.shard_map(
        per_device, mesh=mesh, in_specs=placed, out_specs=P(("req", "mlp"), None), check_vma=False
    )
```

```python
import jax
import jax.numpy as jnp
from jax import lax
from jax.sharding import PartitionSpec as P

GROUP = 64


maximal_matmul_accuracy = lax.Precision.HIGHEST


def shifted(value, axis, steps):
    count = lax.axis_size(axis)
    first, last = (max(0, -steps), min(count, count - steps))
    return lax.ppermute(value, axis, [(source, source + steps) for source in range(first, last)])


def carried_in(shard, axis, combine, identity):
    length, index = (lax.axis_size(axis), lax.axis_index(axis))
    everything = jax.tree.map(
        lambda part, kind: lax.all_gather(part.astype(kind), axis),
        shard,
        jax.tree.map(lambda a: jnp.bfloat16 if a.dtype == jnp.float32 else a.dtype, shard),
    )
    start = jax.tree.map(
        lambda part, zero: jnp.broadcast_to(jnp.asarray(zero, part.dtype), part.shape),
        shard,
        identity,
    )

    def step(k, before):
        reached = k < index
        new = combine(
            before, jax.tree.map(lambda part, own: part[k].astype(own.dtype), everything, shard)
        )
        return jax.tree.map(lambda a, b: jnp.where(reached, a, b), new, before)

    return lax.fori_loop(0, length, step, start)


def prefix_state(piece_map, eye_block):
    index, count = lax.axis_index("req"), lax.axis_size("req")
    core, across, down = index % 2, (index // 2) % 4, index // 8
    ident = (eye_block, jnp.zeros_like(piece_map[1]))

    def pick(flag, a, b):
        return jax.tree.map(lambda u, v: jnp.where(flag, u, v), a, b)

    def sent(value, pairs, kind):
        got = lax.ppermute(jax.tree.map(lambda a: a.astype(kind), value), "req", pairs)
        return jax.tree.map(lambda a: a.astype(jnp.float32), got)

    other = sent(piece_map, [(r, r ^ 1) for r in range(count)], jnp.float32)
    first = core == 0
    chip_total = pick(first, combine_maps(piece_map, other), combine_maps(other, piece_map))
    in_chip = pick(first, ident, other)

    def row_of(r):
        return (r // 8, (r // 2) % 4, r % 2)

    row_got = [chip_total]
    for s in range(1, 4):
        pairs = []
        for r in range(count):
            z, x, c = row_of(r)
            pairs.append((r, z * 8 + ((x + s) % 4) * 2 + c))
        row_got.append(sent(chip_total, pairs, jnp.bfloat16))
    row_total = None
    in_row = ident
    for place in range(4):
        value = jax.tree.map(
            lambda *parts: jnp.stack(parts)[(across - place) % 4], *row_got
        )
        row_total = value if row_total is None else combine_maps(row_total, value)
        if place < 3:
            in_row = pick(place < across, combine_maps(in_row, value), in_row)

    below = ident
    for s in (3, 2, 1):
        pairs = []
        for r in range(count):
            z, x, c = row_of(r)
            if z + s < count // 8:
                pairs.append((r, r + 8 * s))
        value = sent(row_total, pairs, jnp.bfloat16)
        below = pick(down >= s, combine_maps(below, value), below)

    linear, additive = combine_maps(below, in_row)
    return (
        jnp.einsum("baf,bfu->bau", in_chip[0], additive, precision=maximal_matmul_accuracy)
        + in_chip[1]
    )


def gather_rows(share, axis):
    count, index = lax.axis_size(axis), lax.axis_index(axis)
    pieces = [share] + [
        lax.ppermute(share, axis, [(j, (j - s) % count) for j in range(count)])
        for s in range(1, count)
    ]
    return jnp.roll(jnp.stack(pieces), index, axis=0).reshape((-1,) + share.shape[1:])


def scatter_sum(full, axis):
    count, index = lax.axis_size(axis), lax.axis_index(axis)
    rows = full.shape[0] // count
    total = lax.dynamic_slice_in_dim(full, index * rows, rows, 0).astype(jnp.float32)
    for s in range(1, count):
        part = lax.dynamic_slice_in_dim(full, ((index + s) % count) * rows, rows, 0)
        got = lax.ppermute(part, axis, [(j, (j + s) % count) for j in range(count)])
        total = total + got.astype(jnp.float32)
    return total


def rms_scale(values, gain):
    mean_square = jnp.mean(values * values, axis=-1, keepdims=True)
    return values / jnp.sqrt(mean_square + 1e-06) * gain


def unit_norm(values):
    return values / jnp.sqrt(jnp.sum(values * values, axis=-1, keepdims=True) + 1e-06)


def segment_of(positions, lengths):
    bounds = jnp.cumsum(lengths)[:-1]
    return jnp.sum((positions[:, None] >= bounds[None, :]).astype(jnp.int32), axis=1)


def causal_conv(projected, rim_rows, kernel, segment_ids, rim_segments):
    taps_count = kernel.shape[0]
    row_count = projected.shape[0]
    extended = jnp.concatenate([rim_rows, projected], axis=0).astype(jnp.float32)
    extended_ids = jnp.concatenate([rim_segments, segment_ids], axis=0)
    accumulated = jnp.zeros(projected.shape, jnp.float32)
    for offset in range(taps_count):
        window = lax.slice_in_dim(extended, offset, offset + row_count, axis=0)
        window_ids = lax.slice_in_dim(extended_ids, offset, offset + row_count, axis=0)
        same_doc = (window_ids == segment_ids)[:, None]
        accumulated = accumulated + kernel[offset][None, :] * jnp.where(same_doc, window, 0.0)
    return accumulated


def unit_lower_inverse(system):
    size = system.shape[-1]
    rows = jnp.arange(size)[:, None]
    cols = jnp.arange(size)[None, :]
    inverse = jnp.broadcast_to(jnp.eye(size, dtype=system.dtype), system.shape)
    block = 1
    while block < size:
        lower_left = (
            (rows // (2 * block) == cols // (2 * block))
            & ((rows // block) % 2 == 1)
            & ((cols // block) % 2 == 0)
        )
        coupling = jnp.where(lower_left, system, 0.0)
        joined = jnp.einsum(
            "hij,hjk->hik",
            jnp.einsum("hij,hjk->hik", inverse, coupling, precision=maximal_matmul_accuracy),
            inverse,
            precision=maximal_matmul_accuracy,
        )
        inverse = inverse - joined
        block *= 2
    return inverse


def group_parts(query_vecs, key_vecs, value_vecs, beta_vals, log_decay, segment_ids, prior_segment):
    group_rows = query_vecs.shape[0]
    value_dim = value_vecs.shape[-1]
    cumulative = jnp.cumsum(log_decay, axis=0)
    row_index = jnp.arange(group_rows)[:, None]
    col_index = jnp.arange(group_rows)[None, :]
    same_doc = segment_ids[:, None] == segment_ids[None, :]
    keep_mask = ((row_index >= col_index) & same_doc)[None, :, :]
    strict_mask = (row_index > col_index)[None, :, :]
    head_cumul = jnp.transpose(cumulative)
    gaps = head_cumul[:, :, None] - head_cumul[:, None, :]
    weights = jnp.where(keep_mask, jnp.exp(jnp.where(keep_mask, gaps, 0.0)), 0.0)
    open_mask = (segment_ids == prior_segment).astype(query_vecs.dtype)
    start_decay = jnp.exp(cumulative) * open_mask[:, None]
    key_dots = jnp.einsum("ihd,jhd->hij", key_vecs, key_vecs, precision=maximal_matmul_accuracy)
    coupling = jnp.where(
        strict_mask, jnp.transpose(beta_vals)[:, :, None] * weights * key_dots, 0.0
    )
    system = coupling + jnp.eye(group_rows, dtype=query_vecs.dtype)[None]
    targets = jnp.concatenate(
        [beta_vals[:, :, None] * value_vecs, (beta_vals * start_decay)[:, :, None] * key_vecs],
        axis=-1,
    )
    solved = jnp.einsum(
        "hij,hjc->hic",
        unit_lower_inverse(system),
        jnp.transpose(targets, (1, 0, 2)),
        precision=maximal_matmul_accuracy,
    )
    starting_value_rows = solved[:, :, :value_dim]
    delta_correction = solved[:, :, value_dim:]
    query_dots = weights * jnp.einsum(
        "ihd,jhd->hij", query_vecs, key_vecs, precision=maximal_matmul_accuracy
    )
    query_begin_offset = query_vecs * start_decay[:, :, None]
    final_key_rows = key_vecs * jnp.transpose(weights[:, -1, :])[:, :, None]
    carried_decay_factor = start_decay[-1]
    return (
        starting_value_rows,
        delta_correction,
        query_dots,
        query_begin_offset,
        final_key_rows,
        carried_decay_factor,
    )


def group_step(running_state, parts):
    (
        starting_value_rows,
        delta_correction,
        query_dots,
        query_begin_offset,
        final_key_rows,
        carried_decay_factor,
    ) = parts
    fresh_state_update = starting_value_rows - jnp.einsum(
        "mxf,mft->mxt", delta_correction, running_state, precision=maximal_matmul_accuracy
    )
    output_rows = jnp.einsum(
        "fob,obt->fot", query_begin_offset, running_state, precision=maximal_matmul_accuracy
    )
    output_rows = output_rows + jnp.einsum(
        "hij,hjv->ihv", query_dots, fresh_state_update, precision=maximal_matmul_accuracy
    )
    updated_state = carried_decay_factor[:, None, None] * running_state + jnp.einsum(
        "new,enr->ewr", final_key_rows, fresh_state_update, precision=maximal_matmul_accuracy
    )
    return (updated_state, output_rows)


def combine_maps(earlier, later):
    earlier_map, preceding_additive = earlier
    following_linear_map, following_additive = later
    joined_map = jnp.einsum(
        "hkl,hlm->hkm", following_linear_map, earlier_map, precision=maximal_matmul_accuracy
    )
    joined_add = (
        jnp.einsum(
            "baf,bfu->bau",
            following_linear_map,
            preceding_additive,
            precision=maximal_matmul_accuracy,
        )
        + following_additive
    )
    return (joined_map, joined_add)


def per_device(
    tokens,
    lengths,
    in_gain,
    w_query,
    w_key,
    w_value,
    w_gate,
    w_beta,
    w_decay,
    decay_log,
    decay_bias,
    conv_query,
    conv_key,
    conv_value,
    head_gain,
    w_out,
    mlp_gain,
    w_up_gate,
    w_up,
    w_down,
):
    share_rows = tokens.shape[0]
    gathered = gather_rows(tokens, "mlp")
    piece_len = gathered.shape[0]
    head_count = w_beta.shape[1]
    key_dim = w_query.shape[1] // head_count
    value_dim = w_value.shape[1] // head_count
    taps_count = conv_query.shape[0]
    group_count = piece_len // GROUP
    piece_start = lax.axis_index("req") * piece_len
    positions = piece_start + jnp.arange(piece_len, dtype=jnp.int32)
    segment_ids = segment_of(positions, lengths)
    rim_segments = segment_of(
        piece_start - (taps_count - 1) + jnp.arange(taps_count - 1, dtype=jnp.int32), lengths
    )
    token_rows = gathered.astype(jnp.float32)
    normed = rms_scale(token_rows, in_gain).astype(jnp.bfloat16)
    proj_query = jnp.dot(normed, w_query, preferred_element_type=jnp.float32).astype(jnp.bfloat16)
    proj_key = jnp.dot(normed, w_key, preferred_element_type=jnp.float32).astype(jnp.bfloat16)
    proj_value = jnp.dot(normed, w_value, preferred_element_type=jnp.float32).astype(jnp.bfloat16)
    edge_rows = jnp.concatenate(
        [
            proj_query[piece_len - taps_count + 1 :],
            proj_key[piece_len - taps_count + 1 :],
            proj_value[piece_len - taps_count + 1 :],
        ],
        axis=1,
    )
    rim_all = shifted(edge_rows, "req", 1)
    query_width = proj_query.shape[1]
    key_width = proj_key.shape[1]
    rim_query = rim_all[:, :query_width]
    rim_key = rim_all[:, query_width : query_width + key_width]
    rim_value = rim_all[:, query_width + key_width :]
    conv_q = jax.nn.silu(causal_conv(proj_query, rim_query, conv_query, segment_ids, rim_segments))
    conv_k = jax.nn.silu(causal_conv(proj_key, rim_key, conv_key, segment_ids, rim_segments))
    conv_v = jax.nn.silu(causal_conv(proj_value, rim_value, conv_value, segment_ids, rim_segments))
    query_vecs = unit_norm(conv_q.reshape(piece_len, head_count, key_dim)) * key_dim ** (-0.5)
    key_vecs = unit_norm(conv_k.reshape(piece_len, head_count, key_dim))
    value_vecs = conv_v.reshape(piece_len, head_count, value_dim)
    gate_lin = jnp.dot(normed, w_gate, preferred_element_type=jnp.float32).astype(jnp.bfloat16)
    beta_vals = jax.nn.sigmoid(jnp.dot(normed, w_beta, preferred_element_type=jnp.float32))
    log_decay = -jnp.exp(decay_log) * jax.nn.softplus(
        jnp.dot(normed, w_decay, preferred_element_type=jnp.float32) + decay_bias
    )

    def shaped(values):
        return values.reshape((group_count, GROUP) + values.shape[1:])

    prior_ids = segment_of(
        piece_start + jnp.arange(group_count, dtype=jnp.int32) * GROUP - 1, lengths
    )
    parts = jax.vmap(group_parts)(
        shaped(query_vecs),
        shaped(key_vecs),
        shaped(value_vecs),
        shaped(beta_vals),
        shaped(log_decay),
        shaped(segment_ids),
        prior_ids,
    )
    eye_block = jnp.broadcast_to(
        jnp.eye(key_dim, dtype=jnp.float32), (head_count, key_dim, key_dim)
    )
    zero_state = jnp.zeros((head_count, key_dim, value_dim), jnp.float32)

    (
        starting_value_rows,
        delta_correction,
        query_dots,
        query_begin_offset,
        final_key_rows,
        carried_decay_factor,
    ) = parts
    local_maps = carried_decay_factor[:, :, None, None] * eye_block - jnp.einsum(
        "gchk,ghcl->ghkl", final_key_rows, delta_correction, precision=maximal_matmul_accuracy
    )
    local_adds = jnp.einsum(
        "gnew,genr->gewr", final_key_rows, starting_value_rows, precision=maximal_matmul_accuracy
    )
    before = [(eye_block, zero_state)]
    for g in range(group_count):
        before.append(combine_maps(before[-1], (local_maps[g], local_adds[g])))
    start_linear = jnp.stack([m[0] for m in before[:-1]])
    start_additive = jnp.stack([m[1] for m in before[:-1]])
    state_query = query_begin_offset - jnp.einsum(
        "ghij,ghjk->gihk", query_dots, delta_correction, precision=maximal_matmul_accuracy
    )
    inner_rows = jnp.einsum(
        "ghij,ghjv->gihv", query_dots, starting_value_rows, precision=maximal_matmul_accuracy
    ) + jnp.einsum(
        "gihk,ghkv->gihv", state_query, start_additive, precision=maximal_matmul_accuracy
    )
    entry_query = jnp.einsum(
        "gihk,ghkl->gihl", state_query, start_linear, precision=maximal_matmul_accuracy
    )
    incoming = prefix_state(before[-1], eye_block)
    output_rows = inner_rows + jnp.einsum(
        "gihk,hkv->gihv", entry_query, incoming, precision=maximal_matmul_accuracy
    )
    output_rows = output_rows.reshape(piece_len, head_count, value_dim)
    gate_vals = jax.nn.silu(gate_lin.astype(jnp.float32)).reshape(piece_len, head_count, value_dim)
    head_out = (
        (rms_scale(output_rows, head_gain) * gate_vals)
        .reshape(piece_len, head_count * value_dim)
        .astype(jnp.bfloat16)
    )
    partial_out = jnp.dot(head_out, w_out, preferred_element_type=jnp.float32)
    attn_mine = scatter_sum(partial_out.astype(jnp.bfloat16), "mlp")
    resid_mine = tokens.astype(jnp.float32) + attn_mine
    mlp_in = gather_rows(rms_scale(resid_mine, mlp_gain).astype(jnp.bfloat16), "mlp")

    def add_rows(piece):
        return jnp.dot(mlp_in, piece, preferred_element_type=jnp.float32)

    gate_acc = add_rows(lax.all_gather(w_up_gate, "req", axis=0, tiled=True))
    up_acc = add_rows(lax.all_gather(w_up, "req", axis=0, tiled=True))
    hidden = (jax.nn.silu(gate_acc) * up_acc).astype(jnp.bfloat16)
    down_terms = jnp.dot(
        hidden,
        lax.all_gather(w_down, "req", axis=1, tiled=True),
        preferred_element_type=jnp.float32,
    )
    mlp_share = scatter_sum(down_terms.astype(jnp.bfloat16), "mlp")
    return (resid_mine + mlp_share).astype(jnp.bfloat16)


def solution(mesh):
    placed = (
        P(("req", "mlp"), None),
        P(),
        P(),
        P(None, "mlp"),
        P(None, "mlp"),
        P(None, "mlp"),
        P(None, "mlp"),
        P(None, "mlp"),
        P(None, "mlp"),
        P("mlp"),
        P("mlp"),
        P(None, "mlp"),
        P(None, "mlp"),
        P(None, "mlp"),
        P(),
        P("mlp", None),
        P(),
        P("req", "mlp"),
        P("req", "mlp"),
        P("mlp", "req"),
    )
    return jax.shard_map(
        per_device, mesh=mesh, in_specs=placed, out_specs=P(("req", "mlp"), None), check_vma=False
    )
```

```python
import jax
import jax.numpy as jnp
from jax import lax
from jax.sharding import PartitionSpec as P

GROUP = 64


maximal_matmul_accuracy = lax.Precision.HIGHEST


def shifted(value, axis, steps):
    count = lax.axis_size(axis)
    first, last = (max(0, -steps), min(count, count - steps))
    return lax.ppermute(value, axis, [(source, source + steps) for source in range(first, last)])


def carried_in(shard, axis, combine, identity):
    length, index = (lax.axis_size(axis), lax.axis_index(axis))
    everything = jax.tree.map(
        lambda part, kind: lax.all_gather(part.astype(kind), axis),
        shard,
        jax.tree.map(lambda a: jnp.bfloat16 if a.dtype == jnp.float32 else a.dtype, shard),
    )
    start = jax.tree.map(
        lambda part, zero: jnp.broadcast_to(jnp.asarray(zero, part.dtype), part.shape),
        shard,
        identity,
    )

    def step(k, before):
        reached = k < index
        new = combine(
            before, jax.tree.map(lambda part, own: part[k].astype(own.dtype), everything, shard)
        )
        return jax.tree.map(lambda a, b: jnp.where(reached, a, b), new, before)

    return lax.fori_loop(0, length, step, start)


def prefix_state(piece_map, eye_block):
    index, count = lax.axis_index("req"), lax.axis_size("req")
    core, across, down = index % 2, (index // 2) % 4, index // 8
    ident = (eye_block, jnp.zeros_like(piece_map[1]))

    def pick(flag, a, b):
        return jax.tree.map(lambda u, v: jnp.where(flag, u, v), a, b)

    def sent(value, pairs, kind):
        got = lax.ppermute(jax.tree.map(lambda a: a.astype(kind), value), "req", pairs)
        return jax.tree.map(lambda a: a.astype(jnp.float32), got)

    other = sent(piece_map, [(r, r ^ 1) for r in range(count)], jnp.float32)
    first = core == 0
    chip_total = pick(first, combine_maps(piece_map, other), combine_maps(other, piece_map))
    in_chip = pick(first, ident, other)

    def row_of(r):
        return (r // 8, (r // 2) % 4, r % 2)

    row_got = [chip_total]
    for s in range(1, 4):
        pairs = []
        for r in range(count):
            z, x, c = row_of(r)
            pairs.append((r, z * 8 + ((x + s) % 4) * 2 + c))
        row_got.append(sent(chip_total, pairs, jnp.bfloat16))
    row_total = None
    in_row = ident
    for place in range(4):
        value = jax.tree.map(
            lambda *parts: jnp.stack(parts)[(across - place) % 4], *row_got
        )
        row_total = value if row_total is None else combine_maps(row_total, value)
        if place < 3:
            in_row = pick(place < across, combine_maps(in_row, value), in_row)

    below = ident
    for s in (3, 2, 1):
        pairs = []
        for r in range(count):
            z, x, c = row_of(r)
            if z + s < count // 8:
                pairs.append((r, r + 8 * s))
        value = sent(row_total, pairs, jnp.bfloat16)
        below = pick(down >= s, combine_maps(below, value), below)

    linear, additive = combine_maps(below, in_row)
    return (
        jnp.einsum("baf,bfu->bau", in_chip[0], additive, precision=maximal_matmul_accuracy)
        + in_chip[1]
    )


def gather_rows(share, axis):
    count, index = lax.axis_size(axis), lax.axis_index(axis)
    pieces = [share] + [
        lax.ppermute(share, axis, [(j, (j - s) % count) for j in range(count)])
        for s in range(1, count)
    ]
    return jnp.roll(jnp.stack(pieces), index, axis=0).reshape((-1,) + share.shape[1:])


def scatter_sum(full, axis):
    count, index = lax.axis_size(axis), lax.axis_index(axis)
    rows = full.shape[0] // count
    total = lax.dynamic_slice_in_dim(full, index * rows, rows, 0).astype(jnp.float32)
    for s in range(1, count):
        part = lax.dynamic_slice_in_dim(full, ((index + s) % count) * rows, rows, 0)
        got = lax.ppermute(part, axis, [(j, (j + s) % count) for j in range(count)])
        total = total + got.astype(jnp.float32)
    return total


def rms_scale(values, gain):
    mean_square = jnp.mean(values * values, axis=-1, keepdims=True)
    return values / jnp.sqrt(mean_square + 1e-06) * gain


def unit_norm(values):
    return values / jnp.sqrt(jnp.sum(values * values, axis=-1, keepdims=True) + 1e-06)


def segment_of(positions, lengths):
    bounds = jnp.cumsum(lengths)[:-1]
    return jnp.sum((positions[:, None] >= bounds[None, :]).astype(jnp.int32), axis=1)


def causal_conv(projected, rim_rows, kernel, segment_ids, rim_segments):
    taps_count = kernel.shape[0]
    row_count = projected.shape[0]
    extended = jnp.concatenate([rim_rows, projected], axis=0).astype(jnp.float32)
    extended_ids = jnp.concatenate([rim_segments, segment_ids], axis=0)
    accumulated = jnp.zeros(projected.shape, jnp.float32)
    for offset in range(taps_count):
        window = lax.slice_in_dim(extended, offset, offset + row_count, axis=0)
        window_ids = lax.slice_in_dim(extended_ids, offset, offset + row_count, axis=0)
        same_doc = (window_ids == segment_ids)[:, None]
        accumulated = accumulated + kernel[offset][None, :] * jnp.where(same_doc, window, 0.0)
    return accumulated


def unit_lower_inverse(system):
    size = system.shape[-1]
    rows = jnp.arange(size)[:, None]
    cols = jnp.arange(size)[None, :]
    inverse = jnp.broadcast_to(jnp.eye(size, dtype=system.dtype), system.shape)
    block = 1
    while block < size:
        lower_left = (
            (rows // (2 * block) == cols // (2 * block))
            & ((rows // block) % 2 == 1)
            & ((cols // block) % 2 == 0)
        )
        coupling = jnp.where(lower_left, system, 0.0)
        joined = jnp.einsum(
            "hij,hjk->hik",
            jnp.einsum("hij,hjk->hik", inverse, coupling, precision=maximal_matmul_accuracy),
            inverse,
            precision=maximal_matmul_accuracy,
        )
        inverse = inverse - joined
        block *= 2
    return inverse


def group_parts(query_vecs, key_vecs, value_vecs, beta_vals, log_decay, segment_ids, prior_segment):
    group_rows = query_vecs.shape[0]
    value_dim = value_vecs.shape[-1]
    cumulative = jnp.cumsum(log_decay, axis=0)
    row_index = jnp.arange(group_rows)[:, None]
    col_index = jnp.arange(group_rows)[None, :]
    same_doc = segment_ids[:, None] == segment_ids[None, :]
    keep_mask = ((row_index >= col_index) & same_doc)[None, :, :]
    strict_mask = (row_index > col_index)[None, :, :]
    head_cumul = jnp.transpose(cumulative)
    gaps = head_cumul[:, :, None] - head_cumul[:, None, :]
    weights = jnp.where(keep_mask, jnp.exp(jnp.where(keep_mask, gaps, 0.0)), 0.0)
    open_mask = (segment_ids == prior_segment).astype(query_vecs.dtype)
    start_decay = jnp.exp(cumulative) * open_mask[:, None]
    key_dots = jnp.einsum("ihd,jhd->hij", key_vecs, key_vecs, precision=maximal_matmul_accuracy)
    coupling = jnp.where(
        strict_mask, jnp.transpose(beta_vals)[:, :, None] * weights * key_dots, 0.0
    )
    system = coupling + jnp.eye(group_rows, dtype=query_vecs.dtype)[None]
    targets = jnp.concatenate(
        [beta_vals[:, :, None] * value_vecs, (beta_vals * start_decay)[:, :, None] * key_vecs],
        axis=-1,
    )
    solved = jnp.einsum(
        "hij,hjc->hic",
        unit_lower_inverse(system),
        jnp.transpose(targets, (1, 0, 2)),
        precision=maximal_matmul_accuracy,
    )
    starting_value_rows = solved[:, :, :value_dim]
    delta_correction = solved[:, :, value_dim:]
    query_dots = weights * jnp.einsum(
        "ihd,jhd->hij", query_vecs, key_vecs, precision=maximal_matmul_accuracy
    )
    query_begin_offset = query_vecs * start_decay[:, :, None]
    final_key_rows = key_vecs * jnp.transpose(weights[:, -1, :])[:, :, None]
    carried_decay_factor = start_decay[-1]
    return (
        starting_value_rows,
        delta_correction,
        query_dots,
        query_begin_offset,
        final_key_rows,
        carried_decay_factor,
    )


def group_step(running_state, parts):
    (
        starting_value_rows,
        delta_correction,
        query_dots,
        query_begin_offset,
        final_key_rows,
        carried_decay_factor,
    ) = parts
    fresh_state_update = starting_value_rows - jnp.einsum(
        "mxf,mft->mxt", delta_correction, running_state, precision=maximal_matmul_accuracy
    )
    output_rows = jnp.einsum(
        "fob,obt->fot", query_begin_offset, running_state, precision=maximal_matmul_accuracy
    )
    output_rows = output_rows + jnp.einsum(
        "hij,hjv->ihv", query_dots, fresh_state_update, precision=maximal_matmul_accuracy
    )
    updated_state = carried_decay_factor[:, None, None] * running_state + jnp.einsum(
        "new,enr->ewr", final_key_rows, fresh_state_update, precision=maximal_matmul_accuracy
    )
    return (updated_state, output_rows)


def combine_maps(earlier, later):
    earlier_map, preceding_additive = earlier
    following_linear_map, following_additive = later
    joined_map = jnp.einsum(
        "hkl,hlm->hkm", following_linear_map, earlier_map, precision=maximal_matmul_accuracy
    )
    joined_add = (
        jnp.einsum(
            "baf,bfu->bau",
            following_linear_map,
            preceding_additive,
            precision=maximal_matmul_accuracy,
        )
        + following_additive
    )
    return (joined_map, joined_add)


def per_device(
    tokens,
    lengths,
    in_gain,
    w_query,
    w_key,
    w_value,
    w_gate,
    w_beta,
    w_decay,
    decay_log,
    decay_bias,
    conv_query,
    conv_key,
    conv_value,
    head_gain,
    w_out,
    mlp_gain,
    w_up_gate,
    w_up,
    w_down,
):
    share_rows = tokens.shape[0]
    gathered = gather_rows(tokens, "mlp")
    piece_len = gathered.shape[0]
    head_count = w_beta.shape[1]
    key_dim = w_query.shape[1] // head_count
    value_dim = w_value.shape[1] // head_count
    taps_count = conv_query.shape[0]
    group_count = piece_len // GROUP
    piece_start = lax.axis_index("req") * piece_len
    positions = piece_start + jnp.arange(piece_len, dtype=jnp.int32)
    segment_ids = segment_of(positions, lengths)
    rim_segments = segment_of(
        piece_start - (taps_count - 1) + jnp.arange(taps_count - 1, dtype=jnp.int32), lengths
    )
    token_rows = gathered.astype(jnp.float32)
    normed = rms_scale(token_rows, in_gain).astype(jnp.bfloat16)
    proj_query = jnp.dot(normed, w_query, preferred_element_type=jnp.float32).astype(jnp.bfloat16)
    proj_key = jnp.dot(normed, w_key, preferred_element_type=jnp.float32).astype(jnp.bfloat16)
    proj_value = jnp.dot(normed, w_value, preferred_element_type=jnp.float32).astype(jnp.bfloat16)
    edge_rows = jnp.concatenate(
        [
            proj_query[piece_len - taps_count + 1 :],
            proj_key[piece_len - taps_count + 1 :],
            proj_value[piece_len - taps_count + 1 :],
        ],
        axis=1,
    )
    rim_all = shifted(edge_rows, "req", 1)
    query_width = proj_query.shape[1]
    key_width = proj_key.shape[1]
    rim_query = rim_all[:, :query_width]
    rim_key = rim_all[:, query_width : query_width + key_width]
    rim_value = rim_all[:, query_width + key_width :]
    conv_q = jax.nn.silu(causal_conv(proj_query, rim_query, conv_query, segment_ids, rim_segments))
    conv_k = jax.nn.silu(causal_conv(proj_key, rim_key, conv_key, segment_ids, rim_segments))
    conv_v = jax.nn.silu(causal_conv(proj_value, rim_value, conv_value, segment_ids, rim_segments))
    query_vecs = unit_norm(conv_q.reshape(piece_len, head_count, key_dim)) * key_dim ** (-0.5)
    key_vecs = unit_norm(conv_k.reshape(piece_len, head_count, key_dim))
    value_vecs = conv_v.reshape(piece_len, head_count, value_dim)
    gate_lin = jnp.dot(normed, w_gate, preferred_element_type=jnp.float32).astype(jnp.bfloat16)
    beta_vals = jax.nn.sigmoid(jnp.dot(normed, w_beta, preferred_element_type=jnp.float32))
    log_decay = -jnp.exp(decay_log) * jax.nn.softplus(
        jnp.dot(normed, w_decay, preferred_element_type=jnp.float32) + decay_bias
    )

    def shaped(values):
        return values.reshape((group_count, GROUP) + values.shape[1:])

    prior_ids = segment_of(
        piece_start + jnp.arange(group_count, dtype=jnp.int32) * GROUP - 1, lengths
    )
    parts = jax.vmap(group_parts)(
        shaped(query_vecs),
        shaped(key_vecs),
        shaped(value_vecs),
        shaped(beta_vals),
        shaped(log_decay),
        shaped(segment_ids),
        prior_ids,
    )
    eye_block = jnp.broadcast_to(
        jnp.eye(key_dim, dtype=jnp.float32), (head_count, key_dim, key_dim)
    )
    zero_state = jnp.zeros((head_count, key_dim, value_dim), jnp.float32)

    (
        starting_value_rows,
        delta_correction,
        query_dots,
        query_begin_offset,
        final_key_rows,
        carried_decay_factor,
    ) = parts
    local_maps = carried_decay_factor[:, :, None, None] * eye_block - jnp.einsum(
        "gchk,ghcl->ghkl", final_key_rows, delta_correction, precision=maximal_matmul_accuracy
    )
    local_adds = jnp.einsum(
        "gnew,genr->gewr", final_key_rows, starting_value_rows, precision=maximal_matmul_accuracy
    )
    before = [(eye_block, zero_state)]
    for g in range(group_count):
        before.append(combine_maps(before[-1], (local_maps[g], local_adds[g])))
    start_linear = jnp.stack([m[0] for m in before[:-1]])
    start_additive = jnp.stack([m[1] for m in before[:-1]])
    state_query = query_begin_offset - jnp.einsum(
        "ghij,ghjk->gihk", query_dots, delta_correction, precision=maximal_matmul_accuracy
    )
    inner_rows = jnp.einsum(
        "ghij,ghjv->gihv", query_dots, starting_value_rows, precision=maximal_matmul_accuracy
    ) + jnp.einsum(
        "gihk,ghkv->gihv", state_query, start_additive, precision=maximal_matmul_accuracy
    )
    entry_query = jnp.einsum(
        "gihk,ghkl->gihl", state_query, start_linear, precision=maximal_matmul_accuracy
    )
    incoming = prefix_state(before[-1], eye_block)
    w_down, incoming = lax.optimization_barrier((w_down, incoming))
    output_rows = inner_rows + jnp.einsum(
        "gihk,hkv->gihv", entry_query, incoming, precision=maximal_matmul_accuracy
    )
    output_rows = output_rows.reshape(piece_len, head_count, value_dim)
    gate_vals = jax.nn.silu(gate_lin.astype(jnp.float32)).reshape(piece_len, head_count, value_dim)
    head_out = (
        (rms_scale(output_rows, head_gain) * gate_vals)
        .reshape(piece_len, head_count * value_dim)
        .astype(jnp.bfloat16)
    )
    partial_out = jnp.dot(head_out, w_out, preferred_element_type=jnp.float32)
    attn_mine = scatter_sum(partial_out.astype(jnp.bfloat16), "mlp")
    resid_mine = tokens.astype(jnp.float32) + attn_mine
    own_in = rms_scale(resid_mine, mlp_gain).astype(jnp.bfloat16)
    gate_full = lax.all_gather(w_up_gate, "req", axis=0, tiled=True)
    up_full = lax.all_gather(w_up, "req", axis=0, tiled=True)
    down_full = lax.all_gather(w_down, "req", axis=1, tiled=True)

    def mlp_rows(rows):
        gate_acc = jnp.dot(rows, gate_full, preferred_element_type=jnp.float32)
        up_acc = jnp.dot(rows, up_full, preferred_element_type=jnp.float32)
        hidden = (jax.nn.silu(gate_acc) * up_acc).astype(jnp.bfloat16)
        return jnp.dot(hidden, down_full, preferred_element_type=jnp.float32)

    count = lax.axis_size("mlp")
    total = resid_mine + mlp_rows(own_in)
    for s in range(1, count):
        got = lax.ppermute(own_in, "mlp", [(j, (j - s) % count) for j in range(count)])
        back = lax.ppermute(
            mlp_rows(got).astype(jnp.bfloat16), "mlp", [(j, (j + s) % count) for j in range(count)]
        )
        total = total + back.astype(jnp.float32)
    return total.astype(jnp.bfloat16)


def solution(mesh):
    placed = (
        P(("req", "mlp"), None),
        P(),
        P(),
        P(None, "mlp"),
        P(None, "mlp"),
        P(None, "mlp"),
        P(None, "mlp"),
        P(None, "mlp"),
        P(None, "mlp"),
        P("mlp"),
        P("mlp"),
        P(None, "mlp"),
        P(None, "mlp"),
        P(None, "mlp"),
        P(),
        P("mlp", None),
        P(),
        P("req", "mlp"),
        P("req", "mlp"),
        P("mlp", "req"),
    )
    return jax.shard_map(
        per_device, mesh=mesh, in_specs=placed, out_specs=P(("req", "mlp"), None), check_vma=False
    )
```

```python
import jax
import jax.numpy as jnp
from jax import lax
from jax.sharding import PartitionSpec as P

GROUP = 64


maximal_matmul_accuracy = lax.Precision.HIGH


def shifted(value, axis, steps):
    count = lax.axis_size(axis)
    first, last = (max(0, -steps), min(count, count - steps))
    return lax.ppermute(value, axis, [(source, source + steps) for source in range(first, last)])


def carried_in(shard, axis, combine, identity):
    length, index = (lax.axis_size(axis), lax.axis_index(axis))
    everything = jax.tree.map(
        lambda part, kind: lax.all_gather(part.astype(kind), axis),
        shard,
        jax.tree.map(lambda a: jnp.bfloat16 if a.dtype == jnp.float32 else a.dtype, shard),
    )
    start = jax.tree.map(
        lambda part, zero: jnp.broadcast_to(jnp.asarray(zero, part.dtype), part.shape),
        shard,
        identity,
    )

    def step(k, before):
        reached = k < index
        new = combine(
            before, jax.tree.map(lambda part, own: part[k].astype(own.dtype), everything, shard)
        )
        return jax.tree.map(lambda a, b: jnp.where(reached, a, b), new, before)

    return lax.fori_loop(0, length, step, start)


def prefix_state(piece_map, eye_block):
    index, count = lax.axis_index("req"), lax.axis_size("req")
    core, across, down = index % 2, (index // 2) % 4, index // 8
    ident = (eye_block, jnp.zeros_like(piece_map[1]))

    def pick(flag, a, b):
        return jax.tree.map(lambda u, v: jnp.where(flag, u, v), a, b)

    def sent(value, pairs, kind):
        got = lax.ppermute(jax.tree.map(lambda a: a.astype(kind), value), "req", pairs)
        return jax.tree.map(lambda a: a.astype(jnp.float32), got)

    other = sent(piece_map, [(r, r ^ 1) for r in range(count)], jnp.float32)
    first = core == 0
    chip_total = pick(first, combine_maps(piece_map, other), combine_maps(other, piece_map))
    in_chip = pick(first, ident, other)

    def row_of(r):
        return (r // 8, (r // 2) % 4, r % 2)

    row_got = [chip_total]
    for s in range(1, 4):
        pairs = []
        for r in range(count):
            z, x, c = row_of(r)
            pairs.append((r, z * 8 + ((x + s) % 4) * 2 + c))
        row_got.append(sent(chip_total, pairs, jnp.bfloat16))
    row_total = None
    in_row = ident
    for place in range(4):
        value = jax.tree.map(
            lambda *parts: jnp.stack(parts)[(across - place) % 4], *row_got
        )
        row_total = value if row_total is None else combine_maps(row_total, value)
        if place < 3:
            in_row = pick(place < across, combine_maps(in_row, value), in_row)

    below = ident
    for s in (3, 2, 1):
        pairs = []
        for r in range(count):
            z, x, c = row_of(r)
            if z + s < count // 8:
                pairs.append((r, r + 8 * s))
        value = sent(row_total, pairs, jnp.bfloat16)
        below = pick(down >= s, combine_maps(below, value), below)

    linear, additive = combine_maps(below, in_row)
    return (
        jnp.einsum("baf,bfu->bau", in_chip[0], additive, precision=maximal_matmul_accuracy)
        + in_chip[1]
    )


def gather_rows(share, axis):
    count, index = lax.axis_size(axis), lax.axis_index(axis)
    pieces = [share] + [
        lax.ppermute(share, axis, [(j, (j - s) % count) for j in range(count)])
        for s in range(1, count)
    ]
    return jnp.roll(jnp.stack(pieces), index, axis=0).reshape((-1,) + share.shape[1:])


def scatter_sum(full, axis):
    count, index = lax.axis_size(axis), lax.axis_index(axis)
    rows = full.shape[0] // count
    total = lax.dynamic_slice_in_dim(full, index * rows, rows, 0).astype(jnp.float32)
    for s in range(1, count):
        part = lax.dynamic_slice_in_dim(full, ((index + s) % count) * rows, rows, 0)
        got = lax.ppermute(part, axis, [(j, (j + s) % count) for j in range(count)])
        total = total + got.astype(jnp.float32)
    return total


def rms_scale(values, gain):
    mean_square = jnp.mean(values * values, axis=-1, keepdims=True)
    return values / jnp.sqrt(mean_square + 1e-06) * gain


def unit_norm(values):
    return values / jnp.sqrt(jnp.sum(values * values, axis=-1, keepdims=True) + 1e-06)


def segment_of(positions, lengths):
    bounds = jnp.cumsum(lengths)[:-1]
    return jnp.sum((positions[:, None] >= bounds[None, :]).astype(jnp.int32), axis=1)


def causal_conv(projected, rim_rows, kernel, segment_ids, rim_segments):
    taps_count = kernel.shape[0]
    row_count = projected.shape[0]
    extended = jnp.concatenate([rim_rows, projected], axis=0).astype(jnp.float32)
    extended_ids = jnp.concatenate([rim_segments, segment_ids], axis=0)
    accumulated = jnp.zeros(projected.shape, jnp.float32)
    for offset in range(taps_count):
        window = lax.slice_in_dim(extended, offset, offset + row_count, axis=0)
        window_ids = lax.slice_in_dim(extended_ids, offset, offset + row_count, axis=0)
        same_doc = (window_ids == segment_ids)[:, None]
        accumulated = accumulated + kernel[offset][None, :] * jnp.where(same_doc, window, 0.0)
    return accumulated


def unit_lower_inverse(system):
    size = system.shape[-1]
    rows = jnp.arange(size)[:, None]
    cols = jnp.arange(size)[None, :]
    inverse = jnp.broadcast_to(jnp.eye(size, dtype=system.dtype), system.shape)
    block = 1
    while block < size:
        lower_left = (
            (rows // (2 * block) == cols // (2 * block))
            & ((rows // block) % 2 == 1)
            & ((cols // block) % 2 == 0)
        )
        coupling = jnp.where(lower_left, system, 0.0)
        joined = jnp.einsum(
            "hij,hjk->hik",
            jnp.einsum("hij,hjk->hik", inverse, coupling, precision=maximal_matmul_accuracy),
            inverse,
            precision=maximal_matmul_accuracy,
        )
        inverse = inverse - joined
        block *= 2
    return inverse


def group_parts(query_vecs, key_vecs, value_vecs, beta_vals, log_decay, segment_ids, prior_segment):
    group_rows = query_vecs.shape[0]
    value_dim = value_vecs.shape[-1]
    cumulative = jnp.cumsum(log_decay, axis=0)
    row_index = jnp.arange(group_rows)[:, None]
    col_index = jnp.arange(group_rows)[None, :]
    same_doc = segment_ids[:, None] == segment_ids[None, :]
    keep_mask = ((row_index >= col_index) & same_doc)[None, :, :]
    strict_mask = (row_index > col_index)[None, :, :]
    head_cumul = jnp.transpose(cumulative)
    gaps = head_cumul[:, :, None] - head_cumul[:, None, :]
    weights = jnp.where(keep_mask, jnp.exp(jnp.where(keep_mask, gaps, 0.0)), 0.0)
    open_mask = (segment_ids == prior_segment).astype(query_vecs.dtype)
    start_decay = jnp.exp(cumulative) * open_mask[:, None]
    key_dots = jnp.einsum("ihd,jhd->hij", key_vecs, key_vecs, precision=maximal_matmul_accuracy)
    coupling = jnp.where(
        strict_mask, jnp.transpose(beta_vals)[:, :, None] * weights * key_dots, 0.0
    )
    system = coupling + jnp.eye(group_rows, dtype=query_vecs.dtype)[None]
    targets = jnp.concatenate(
        [beta_vals[:, :, None] * value_vecs, (beta_vals * start_decay)[:, :, None] * key_vecs],
        axis=-1,
    )
    solved = jnp.einsum(
        "hij,hjc->hic",
        unit_lower_inverse(system),
        jnp.transpose(targets, (1, 0, 2)),
        precision=maximal_matmul_accuracy,
    )
    starting_value_rows = solved[:, :, :value_dim]
    delta_correction = solved[:, :, value_dim:]
    query_dots = weights * jnp.einsum(
        "ihd,jhd->hij", query_vecs, key_vecs, precision=maximal_matmul_accuracy
    )
    query_begin_offset = query_vecs * start_decay[:, :, None]
    final_key_rows = key_vecs * jnp.transpose(weights[:, -1, :])[:, :, None]
    carried_decay_factor = start_decay[-1]
    return (
        starting_value_rows,
        delta_correction,
        query_dots,
        query_begin_offset,
        final_key_rows,
        carried_decay_factor,
    )


def group_step(running_state, parts):
    (
        starting_value_rows,
        delta_correction,
        query_dots,
        query_begin_offset,
        final_key_rows,
        carried_decay_factor,
    ) = parts
    fresh_state_update = starting_value_rows - jnp.einsum(
        "mxf,mft->mxt", delta_correction, running_state, precision=maximal_matmul_accuracy
    )
    output_rows = jnp.einsum(
        "fob,obt->fot", query_begin_offset, running_state, precision=maximal_matmul_accuracy
    )
    output_rows = output_rows + jnp.einsum(
        "hij,hjv->ihv", query_dots, fresh_state_update, precision=maximal_matmul_accuracy
    )
    updated_state = carried_decay_factor[:, None, None] * running_state + jnp.einsum(
        "new,enr->ewr", final_key_rows, fresh_state_update, precision=maximal_matmul_accuracy
    )
    return (updated_state, output_rows)


def combine_maps(earlier, later):
    earlier_map, preceding_additive = earlier
    following_linear_map, following_additive = later
    joined_map = jnp.einsum(
        "hkl,hlm->hkm", following_linear_map, earlier_map, precision=maximal_matmul_accuracy
    )
    joined_add = (
        jnp.einsum(
            "baf,bfu->bau",
            following_linear_map,
            preceding_additive,
            precision=maximal_matmul_accuracy,
        )
        + following_additive
    )
    return (joined_map, joined_add)


def per_device(
    tokens,
    lengths,
    in_gain,
    w_query,
    w_key,
    w_value,
    w_gate,
    w_beta,
    w_decay,
    decay_log,
    decay_bias,
    conv_query,
    conv_key,
    conv_value,
    head_gain,
    w_out,
    mlp_gain,
    w_up_gate,
    w_up,
    w_down,
):
    share_rows = tokens.shape[0]
    gathered = gather_rows(tokens, "mlp")
    piece_len = gathered.shape[0]
    head_count = w_beta.shape[1]
    key_dim = w_query.shape[1] // head_count
    value_dim = w_value.shape[1] // head_count
    taps_count = conv_query.shape[0]
    group_count = piece_len // GROUP
    piece_start = lax.axis_index("req") * piece_len
    positions = piece_start + jnp.arange(piece_len, dtype=jnp.int32)
    segment_ids = segment_of(positions, lengths)
    rim_segments = segment_of(
        piece_start - (taps_count - 1) + jnp.arange(taps_count - 1, dtype=jnp.int32), lengths
    )
    token_rows = gathered.astype(jnp.float32)
    normed = rms_scale(token_rows, in_gain).astype(jnp.bfloat16)
    proj_query = jnp.dot(normed, w_query, preferred_element_type=jnp.float32).astype(jnp.bfloat16)
    proj_key = jnp.dot(normed, w_key, preferred_element_type=jnp.float32).astype(jnp.bfloat16)
    proj_value = jnp.dot(normed, w_value, preferred_element_type=jnp.float32).astype(jnp.bfloat16)
    edge_rows = jnp.concatenate(
        [
            proj_query[piece_len - taps_count + 1 :],
            proj_key[piece_len - taps_count + 1 :],
            proj_value[piece_len - taps_count + 1 :],
        ],
        axis=1,
    )
    rim_all = shifted(edge_rows, "req", 1)
    query_width = proj_query.shape[1]
    key_width = proj_key.shape[1]
    rim_query = rim_all[:, :query_width]
    rim_key = rim_all[:, query_width : query_width + key_width]
    rim_value = rim_all[:, query_width + key_width :]
    conv_q = jax.nn.silu(causal_conv(proj_query, rim_query, conv_query, segment_ids, rim_segments))
    conv_k = jax.nn.silu(causal_conv(proj_key, rim_key, conv_key, segment_ids, rim_segments))
    conv_v = jax.nn.silu(causal_conv(proj_value, rim_value, conv_value, segment_ids, rim_segments))
    query_vecs = unit_norm(conv_q.reshape(piece_len, head_count, key_dim)) * key_dim ** (-0.5)
    key_vecs = unit_norm(conv_k.reshape(piece_len, head_count, key_dim))
    value_vecs = conv_v.reshape(piece_len, head_count, value_dim)
    gate_lin = jnp.dot(normed, w_gate, preferred_element_type=jnp.float32).astype(jnp.bfloat16)
    beta_vals = jax.nn.sigmoid(jnp.dot(normed, w_beta, preferred_element_type=jnp.float32))
    log_decay = -jnp.exp(decay_log) * jax.nn.softplus(
        jnp.dot(normed, w_decay, preferred_element_type=jnp.float32) + decay_bias
    )

    def shaped(values):
        return values.reshape((group_count, GROUP) + values.shape[1:])

    prior_ids = segment_of(
        piece_start + jnp.arange(group_count, dtype=jnp.int32) * GROUP - 1, lengths
    )
    parts = jax.vmap(group_parts)(
        shaped(query_vecs),
        shaped(key_vecs),
        shaped(value_vecs),
        shaped(beta_vals),
        shaped(log_decay),
        shaped(segment_ids),
        prior_ids,
    )
    eye_block = jnp.broadcast_to(
        jnp.eye(key_dim, dtype=jnp.float32), (head_count, key_dim, key_dim)
    )
    zero_state = jnp.zeros((head_count, key_dim, value_dim), jnp.float32)

    (
        starting_value_rows,
        delta_correction,
        query_dots,
        query_begin_offset,
        final_key_rows,
        carried_decay_factor,
    ) = parts
    local_maps = carried_decay_factor[:, :, None, None] * eye_block - jnp.einsum(
        "gchk,ghcl->ghkl", final_key_rows, delta_correction, precision=maximal_matmul_accuracy
    )
    local_adds = jnp.einsum(
        "gnew,genr->gewr", final_key_rows, starting_value_rows, precision=maximal_matmul_accuracy
    )
    before = [(eye_block, zero_state)]
    for g in range(group_count):
        before.append(combine_maps(before[-1], (local_maps[g], local_adds[g])))
    start_linear = jnp.stack([m[0] for m in before[:-1]])
    start_additive = jnp.stack([m[1] for m in before[:-1]])
    state_query = query_begin_offset - jnp.einsum(
        "ghij,ghjk->gihk", query_dots, delta_correction, precision=maximal_matmul_accuracy
    )
    inner_rows = jnp.einsum(
        "ghij,ghjv->gihv", query_dots, starting_value_rows, precision=maximal_matmul_accuracy
    ) + jnp.einsum(
        "gihk,ghkv->gihv", state_query, start_additive, precision=maximal_matmul_accuracy
    )
    entry_query = jnp.einsum(
        "gihk,ghkl->gihl", state_query, start_linear, precision=maximal_matmul_accuracy
    )
    incoming = prefix_state(before[-1], eye_block)
    w_down, incoming = lax.optimization_barrier((w_down, incoming))
    output_rows = inner_rows + jnp.einsum(
        "gihk,hkv->gihv", entry_query, incoming, precision=maximal_matmul_accuracy
    )
    output_rows = output_rows.reshape(piece_len, head_count, value_dim)
    gate_vals = jax.nn.silu(gate_lin.astype(jnp.float32)).reshape(piece_len, head_count, value_dim)
    head_out = (
        (rms_scale(output_rows, head_gain) * gate_vals)
        .reshape(piece_len, head_count * value_dim)
        .astype(jnp.bfloat16)
    )
    partial_out = jnp.dot(head_out, w_out, preferred_element_type=jnp.float32)
    attn_mine = scatter_sum(partial_out.astype(jnp.bfloat16), "mlp")
    resid_mine = tokens.astype(jnp.float32) + attn_mine
    mlp_in = gather_rows(rms_scale(resid_mine, mlp_gain).astype(jnp.bfloat16), "mlp")

    def add_rows(piece):
        return jnp.dot(mlp_in, piece, preferred_element_type=jnp.float32)

    gate_acc = add_rows(lax.all_gather(w_up_gate, "req", axis=0, tiled=True))
    up_acc = add_rows(lax.all_gather(w_up, "req", axis=0, tiled=True))
    hidden = (jax.nn.silu(gate_acc) * up_acc).astype(jnp.bfloat16)
    down_terms = jnp.dot(
        hidden,
        lax.all_gather(w_down, "req", axis=1, tiled=True),
        preferred_element_type=jnp.float32,
    )
    mlp_share = scatter_sum(down_terms.astype(jnp.bfloat16), "mlp")
    return (resid_mine + mlp_share).astype(jnp.bfloat16)


def solution(mesh):
    placed = (
        P(("req", "mlp"), None),
        P(),
        P(),
        P(None, "mlp"),
        P(None, "mlp"),
        P(None, "mlp"),
        P(None, "mlp"),
        P(None, "mlp"),
        P(None, "mlp"),
        P("mlp"),
        P("mlp"),
        P(None, "mlp"),
        P(None, "mlp"),
        P(None, "mlp"),
        P(),
        P("mlp", None),
        P(),
        P("req", "mlp"),
        P("req", "mlp"),
        P("mlp", "req"),
    )
    return jax.shard_map(
        per_device, mesh=mesh, in_specs=placed, out_specs=P(("req", "mlp"), None), check_vma=False
    )
```

```python
import jax
import jax.numpy as jnp
from jax import lax
from jax.sharding import PartitionSpec as P

GROUP = 64


maximal_matmul_accuracy = lax.Precision.HIGH


def shifted(value, axis, steps):
    count = lax.axis_size(axis)
    first, last = (max(0, -steps), min(count, count - steps))
    return lax.ppermute(value, axis, [(source, source + steps) for source in range(first, last)])


def carried_in(shard, axis, combine, identity):
    length, index = (lax.axis_size(axis), lax.axis_index(axis))
    everything = jax.tree.map(
        lambda part, kind: lax.all_gather(part.astype(kind), axis),
        shard,
        jax.tree.map(lambda a: jnp.bfloat16 if a.dtype == jnp.float32 else a.dtype, shard),
    )
    start = jax.tree.map(
        lambda part, zero: jnp.broadcast_to(jnp.asarray(zero, part.dtype), part.shape),
        shard,
        identity,
    )

    def step(k, before):
        reached = k < index
        new = combine(
            before, jax.tree.map(lambda part, own: part[k].astype(own.dtype), everything, shard)
        )
        return jax.tree.map(lambda a, b: jnp.where(reached, a, b), new, before)

    return lax.fori_loop(0, length, step, start)


def join_maps(earlier, later):
    width = later.shape[-2]
    joined = jnp.einsum(
        "hkl,hlm->hkm", later[..., :width], earlier, precision=maximal_matmul_accuracy
    )
    return joined.at[..., width:].add(later[..., width:])


def prefix_state(piece_map, ident):
    index, count = lax.axis_index("req"), lax.axis_size("req")
    core, across, down = index % 2, (index // 2) % 4, index // 8
    width = piece_map.shape[-2]

    def sent(value, pairs, kind):
        return lax.ppermute(value.astype(kind), "req", pairs).astype(jnp.float32)

    other = sent(piece_map, [(r, r ^ 1) for r in range(count)], jnp.float32)
    first = core == 0
    chip_total = jnp.where(first, join_maps(piece_map, other), join_maps(other, piece_map))
    in_chip = jnp.where(first, ident, other)

    row_got = [chip_total]
    for s in range(1, 4):
        pairs = []
        for r in range(count):
            z, x, c = r // 8, (r // 2) % 4, r % 2
            pairs.append((r, z * 8 + ((x + s) % 4) * 2 + c))
        row_got.append(sent(chip_total, pairs, jnp.bfloat16))
    stacked = jnp.stack(row_got)
    row_total = None
    in_row = ident
    for place in range(4):
        value = stacked[(across - place) % 4]
        row_total = value if row_total is None else join_maps(row_total, value)
        if place < 3:
            in_row = jnp.where(place < across, join_maps(in_row, value), in_row)

    below = jnp.zeros_like(piece_map[..., width:])
    for s in (3, 2, 1):
        pairs = [(r, r + 8 * s) for r in range(count) if r // 8 + s < count // 8]
        value = sent(row_total, pairs, jnp.bfloat16)
        below = jnp.where(
            down >= s,
            jnp.einsum(
                "baf,bfu->bau", value[..., :width], below, precision=maximal_matmul_accuracy
            )
            + value[..., width:],
            below,
        )

    row_part = (
        jnp.einsum("baf,bfu->bau", in_row[..., :width], below, precision=maximal_matmul_accuracy)
        + in_row[..., width:]
    )
    return (
        jnp.einsum("baf,bfu->bau", in_chip[..., :width], row_part, precision=maximal_matmul_accuracy)
        + in_chip[..., width:]
    )


def gather_rows(share, axis):
    count, index = lax.axis_size(axis), lax.axis_index(axis)
    pieces = [share] + [
        lax.ppermute(share, axis, [(j, (j - s) % count) for j in range(count)])
        for s in range(1, count)
    ]
    return jnp.roll(jnp.stack(pieces), index, axis=0).reshape((-1,) + share.shape[1:])


def scatter_sum(full, axis):
    count, index = lax.axis_size(axis), lax.axis_index(axis)
    rows = full.shape[0] // count
    total = lax.dynamic_slice_in_dim(full, index * rows, rows, 0).astype(jnp.float32)
    for s in range(1, count):
        part = lax.dynamic_slice_in_dim(full, ((index + s) % count) * rows, rows, 0)
        got = lax.ppermute(part, axis, [(j, (j + s) % count) for j in range(count)])
        total = total + got.astype(jnp.float32)
    return total


def rms_scale(values, gain):
    mean_square = jnp.mean(values * values, axis=-1, keepdims=True)
    return values / jnp.sqrt(mean_square + 1e-06) * gain


def unit_norm(values):
    return values / jnp.sqrt(jnp.sum(values * values, axis=-1, keepdims=True) + 1e-06)


def segment_of(positions, lengths):
    bounds = jnp.cumsum(lengths)[:-1]
    return jnp.sum((positions[:, None] >= bounds[None, :]).astype(jnp.int32), axis=1)


def causal_conv(projected, rim_rows, kernel, segment_ids, rim_segments):
    taps_count = kernel.shape[0]
    row_count = projected.shape[0]
    extended = jnp.concatenate([rim_rows, projected], axis=0).astype(jnp.float32)
    extended_ids = jnp.concatenate([rim_segments, segment_ids], axis=0)
    accumulated = jnp.zeros(projected.shape, jnp.float32)
    for offset in range(taps_count):
        window = lax.slice_in_dim(extended, offset, offset + row_count, axis=0)
        window_ids = lax.slice_in_dim(extended_ids, offset, offset + row_count, axis=0)
        same_doc = (window_ids == segment_ids)[:, None]
        accumulated = accumulated + kernel[offset][None, :] * jnp.where(same_doc, window, 0.0)
    return accumulated


def unit_lower_inverse(system):
    size = system.shape[-1]
    rows = jnp.arange(size)[:, None]
    cols = jnp.arange(size)[None, :]
    inverse = jnp.broadcast_to(jnp.eye(size, dtype=system.dtype), system.shape)
    block = 1
    while block < size:
        lower_left = (
            (rows // (2 * block) == cols // (2 * block))
            & ((rows // block) % 2 == 1)
            & ((cols // block) % 2 == 0)
        )
        coupling = jnp.where(lower_left, system, 0.0)
        joined = jnp.einsum(
            "hij,hjk->hik",
            jnp.einsum("hij,hjk->hik", inverse, coupling, precision=maximal_matmul_accuracy),
            inverse,
            precision=maximal_matmul_accuracy,
        )
        inverse = inverse - joined
        block *= 2
    return inverse


def group_parts(query_vecs, key_vecs, value_vecs, beta_vals, log_decay, segment_ids, prior_segment):
    group_rows = query_vecs.shape[0]
    value_dim = value_vecs.shape[-1]
    cumulative = jnp.cumsum(log_decay, axis=0)
    row_index = jnp.arange(group_rows)[:, None]
    col_index = jnp.arange(group_rows)[None, :]
    same_doc = segment_ids[:, None] == segment_ids[None, :]
    keep_mask = ((row_index >= col_index) & same_doc)[None, :, :]
    strict_mask = (row_index > col_index)[None, :, :]
    head_cumul = jnp.transpose(cumulative)
    gaps = head_cumul[:, :, None] - head_cumul[:, None, :]
    weights = jnp.where(keep_mask, jnp.exp(jnp.where(keep_mask, gaps, 0.0)), 0.0)
    open_mask = (segment_ids == prior_segment).astype(query_vecs.dtype)
    start_decay = jnp.exp(cumulative) * open_mask[:, None]
    key_dots = jnp.einsum("ihd,jhd->hij", key_vecs, key_vecs, precision=maximal_matmul_accuracy)
    coupling = jnp.where(
        strict_mask, jnp.transpose(beta_vals)[:, :, None] * weights * key_dots, 0.0
    )
    system = coupling + jnp.eye(group_rows, dtype=query_vecs.dtype)[None]
    targets = jnp.concatenate(
        [beta_vals[:, :, None] * value_vecs, (beta_vals * start_decay)[:, :, None] * key_vecs],
        axis=-1,
    )
    solved = jnp.einsum(
        "hij,hjc->hic",
        unit_lower_inverse(system),
        jnp.transpose(targets, (1, 0, 2)),
        precision=maximal_matmul_accuracy,
    )
    starting_value_rows = solved[:, :, :value_dim]
    delta_correction = solved[:, :, value_dim:]
    query_dots = weights * jnp.einsum(
        "ihd,jhd->hij", query_vecs, key_vecs, precision=maximal_matmul_accuracy
    )
    query_begin_offset = query_vecs * start_decay[:, :, None]
    final_key_rows = key_vecs * jnp.transpose(weights[:, -1, :])[:, :, None]
    carried_decay_factor = start_decay[-1]
    return (
        starting_value_rows,
        delta_correction,
        query_dots,
        query_begin_offset,
        final_key_rows,
        carried_decay_factor,
    )


def group_step(running_state, parts):
    (
        starting_value_rows,
        delta_correction,
        query_dots,
        query_begin_offset,
        final_key_rows,
        carried_decay_factor,
    ) = parts
    fresh_state_update = starting_value_rows - jnp.einsum(
        "mxf,mft->mxt", delta_correction, running_state, precision=maximal_matmul_accuracy
    )
    output_rows = jnp.einsum(
        "fob,obt->fot", query_begin_offset, running_state, precision=maximal_matmul_accuracy
    )
    output_rows = output_rows + jnp.einsum(
        "hij,hjv->ihv", query_dots, fresh_state_update, precision=maximal_matmul_accuracy
    )
    updated_state = carried_decay_factor[:, None, None] * running_state + jnp.einsum(
        "new,enr->ewr", final_key_rows, fresh_state_update, precision=maximal_matmul_accuracy
    )
    return (updated_state, output_rows)


def combine_maps(earlier, later):
    earlier_map, preceding_additive = earlier
    following_linear_map, following_additive = later
    joined_map = jnp.einsum(
        "hkl,hlm->hkm", following_linear_map, earlier_map, precision=maximal_matmul_accuracy
    )
    joined_add = (
        jnp.einsum(
            "baf,bfu->bau",
            following_linear_map,
            preceding_additive,
            precision=maximal_matmul_accuracy,
        )
        + following_additive
    )
    return (joined_map, joined_add)


def per_device(
    tokens,
    lengths,
    in_gain,
    w_query,
    w_key,
    w_value,
    w_gate,
    w_beta,
    w_decay,
    decay_log,
    decay_bias,
    conv_query,
    conv_key,
    conv_value,
    head_gain,
    w_out,
    mlp_gain,
    w_up_gate,
    w_up,
    w_down,
):
    share_rows = tokens.shape[0]
    gathered = gather_rows(tokens, "mlp")
    piece_len = gathered.shape[0]
    head_count = w_beta.shape[1]
    key_dim = w_query.shape[1] // head_count
    value_dim = w_value.shape[1] // head_count
    taps_count = conv_query.shape[0]
    group_count = piece_len // GROUP
    piece_start = lax.axis_index("req") * piece_len
    positions = piece_start + jnp.arange(piece_len, dtype=jnp.int32)
    segment_ids = segment_of(positions, lengths)
    rim_segments = segment_of(
        piece_start - (taps_count - 1) + jnp.arange(taps_count - 1, dtype=jnp.int32), lengths
    )
    token_rows = gathered.astype(jnp.float32)
    normed = rms_scale(token_rows, in_gain).astype(jnp.bfloat16)
    proj_query = jnp.dot(normed, w_query, preferred_element_type=jnp.float32).astype(jnp.bfloat16)
    proj_key = jnp.dot(normed, w_key, preferred_element_type=jnp.float32).astype(jnp.bfloat16)
    proj_value = jnp.dot(normed, w_value, preferred_element_type=jnp.float32).astype(jnp.bfloat16)
    edge_rows = jnp.concatenate(
        [
            proj_query[piece_len - taps_count + 1 :],
            proj_key[piece_len - taps_count + 1 :],
            proj_value[piece_len - taps_count + 1 :],
        ],
        axis=1,
    )
    rim_all = shifted(edge_rows, "req", 1)
    query_width = proj_query.shape[1]
    key_width = proj_key.shape[1]
    rim_query = rim_all[:, :query_width]
    rim_key = rim_all[:, query_width : query_width + key_width]
    rim_value = rim_all[:, query_width + key_width :]
    conv_q = jax.nn.silu(causal_conv(proj_query, rim_query, conv_query, segment_ids, rim_segments))
    conv_k = jax.nn.silu(causal_conv(proj_key, rim_key, conv_key, segment_ids, rim_segments))
    conv_v = jax.nn.silu(causal_conv(proj_value, rim_value, conv_value, segment_ids, rim_segments))
    query_vecs = unit_norm(conv_q.reshape(piece_len, head_count, key_dim)) * key_dim ** (-0.5)
    key_vecs = unit_norm(conv_k.reshape(piece_len, head_count, key_dim))
    value_vecs = conv_v.reshape(piece_len, head_count, value_dim)
    gate_lin = jnp.dot(normed, w_gate, preferred_element_type=jnp.float32).astype(jnp.bfloat16)
    beta_vals = jax.nn.sigmoid(jnp.dot(normed, w_beta, preferred_element_type=jnp.float32))
    log_decay = -jnp.exp(decay_log) * jax.nn.softplus(
        jnp.dot(normed, w_decay, preferred_element_type=jnp.float32) + decay_bias
    )

    def shaped(values):
        return values.reshape((group_count, GROUP) + values.shape[1:])

    prior_ids = segment_of(
        piece_start + jnp.arange(group_count, dtype=jnp.int32) * GROUP - 1, lengths
    )
    parts = jax.vmap(group_parts)(
        shaped(query_vecs),
        shaped(key_vecs),
        shaped(value_vecs),
        shaped(beta_vals),
        shaped(log_decay),
        shaped(segment_ids),
        prior_ids,
    )
    eye_block = jnp.broadcast_to(
        jnp.eye(key_dim, dtype=jnp.float32), (head_count, key_dim, key_dim)
    )
    zero_state = jnp.zeros((head_count, key_dim, value_dim), jnp.float32)

    (
        starting_value_rows,
        delta_correction,
        query_dots,
        query_begin_offset,
        final_key_rows,
        carried_decay_factor,
    ) = parts
    local_maps = carried_decay_factor[:, :, None, None] * eye_block - jnp.einsum(
        "gchk,ghcl->ghkl", final_key_rows, delta_correction, precision=maximal_matmul_accuracy
    )
    local_adds = jnp.einsum(
        "gnew,genr->gewr", final_key_rows, starting_value_rows, precision=maximal_matmul_accuracy
    )
    ident = jnp.concatenate([eye_block, zero_state], axis=-1)
    local_joint = jnp.concatenate([local_maps, local_adds], axis=-1)
    before = [ident]
    for g in range(group_count):
        before.append(join_maps(before[-1], local_joint[g]))
    start_joint = jnp.stack(before[:-1])
    start_linear = start_joint[..., :key_dim]
    start_additive = start_joint[..., key_dim:]
    state_query = query_begin_offset - jnp.einsum(
        "ghij,ghjk->gihk", query_dots, delta_correction, precision=maximal_matmul_accuracy
    )
    inner_rows = jnp.einsum(
        "ghij,ghjv->gihv", query_dots, starting_value_rows, precision=maximal_matmul_accuracy
    ) + jnp.einsum(
        "gihk,ghkv->gihv", state_query, start_additive, precision=maximal_matmul_accuracy
    )
    entry_query = jnp.einsum(
        "gihk,ghkl->gihl", state_query, start_linear, precision=maximal_matmul_accuracy
    )
    incoming = prefix_state(before[-1], ident)
    w_down, incoming = lax.optimization_barrier((w_down, incoming))
    output_rows = inner_rows + jnp.einsum(
        "gihk,hkv->gihv", entry_query, incoming, precision=maximal_matmul_accuracy
    )
    output_rows = output_rows.reshape(piece_len, head_count, value_dim)
    gate_vals = jax.nn.silu(gate_lin.astype(jnp.float32)).reshape(piece_len, head_count, value_dim)
    head_out = (
        (rms_scale(output_rows, head_gain) * gate_vals)
        .reshape(piece_len, head_count * value_dim)
        .astype(jnp.bfloat16)
    )
    partial_out = jnp.dot(head_out, w_out, preferred_element_type=jnp.float32)
    attn_mine = scatter_sum(partial_out.astype(jnp.bfloat16), "mlp")
    resid_mine = tokens.astype(jnp.float32) + attn_mine
    mlp_in = gather_rows(rms_scale(resid_mine, mlp_gain).astype(jnp.bfloat16), "mlp")

    def add_rows(piece):
        return jnp.dot(mlp_in, piece, preferred_element_type=jnp.float32)

    gate_acc = add_rows(lax.all_gather(w_up_gate, "req", axis=0, tiled=True))
    up_acc = add_rows(lax.all_gather(w_up, "req", axis=0, tiled=True))
    hidden = (jax.nn.silu(gate_acc) * up_acc).astype(jnp.bfloat16)
    down_terms = jnp.dot(
        hidden,
        lax.all_gather(w_down, "req", axis=1, tiled=True),
        preferred_element_type=jnp.float32,
    )
    mlp_share = scatter_sum(down_terms.astype(jnp.bfloat16), "mlp")
    return (resid_mine + mlp_share).astype(jnp.bfloat16)


def solution(mesh):
    placed = (
        P(("req", "mlp"), None),
        P(),
        P(),
        P(None, "mlp"),
        P(None, "mlp"),
        P(None, "mlp"),
        P(None, "mlp"),
        P(None, "mlp"),
        P(None, "mlp"),
        P("mlp"),
        P("mlp"),
        P(None, "mlp"),
        P(None, "mlp"),
        P(None, "mlp"),
        P(),
        P("mlp", None),
        P(),
        P("req", "mlp"),
        P("req", "mlp"),
        P("mlp", "req"),
    )
    return jax.shard_map(
        per_device, mesh=mesh, in_specs=placed, out_specs=P(("req", "mlp"), None), check_vma=False
    )
```

```python
import jax
import jax.numpy as jnp
from jax import lax
from jax.sharding import PartitionSpec as P

GROUP = 64
REQ = ("z", "x", "core")


maximal_matmul_accuracy = lax.Precision.HIGH


def shifted(value, axis, steps):
    count = lax.axis_size(axis)
    first, last = (max(0, -steps), min(count, count - steps))
    return lax.ppermute(value, axis, [(source, source + steps) for source in range(first, last)])


def carried_in(shard, axis, combine, identity):
    length, index = (lax.axis_size(axis), lax.axis_index(axis))
    everything = jax.tree.map(
        lambda part, kind: lax.all_gather(part.astype(kind), axis),
        shard,
        jax.tree.map(lambda a: jnp.bfloat16 if a.dtype == jnp.float32 else a.dtype, shard),
    )
    start = jax.tree.map(
        lambda part, zero: jnp.broadcast_to(jnp.asarray(zero, part.dtype), part.shape),
        shard,
        identity,
    )

    def step(k, before):
        reached = k < index
        new = combine(
            before, jax.tree.map(lambda part, own: part[k].astype(own.dtype), everything, shard)
        )
        return jax.tree.map(lambda a, b: jnp.where(reached, a, b), new, before)

    return lax.fori_loop(0, length, step, start)


def prefix_state(piece_map, eye_block):
    index, count = lax.axis_index(REQ), req_count()
    core, across, down = index % 2, (index // 2) % 4, index // 8
    ident = (eye_block, jnp.zeros_like(piece_map[1]))

    def pick(flag, a, b):
        return jax.tree.map(lambda u, v: jnp.where(flag, u, v), a, b)

    def sent(value, pairs, kind):
        got = lax.ppermute(jax.tree.map(lambda a: a.astype(kind), value), REQ, pairs)
        return jax.tree.map(lambda a: a.astype(jnp.float32), got)

    other = sent(piece_map, [(r, r ^ 1) for r in range(count)], jnp.float32)
    first = core == 0
    chip_total = pick(first, combine_maps(piece_map, other), combine_maps(other, piece_map))
    in_chip = pick(first, ident, other)

    def row_of(r):
        return (r // 8, (r // 2) % 4, r % 2)

    row_got = [chip_total]
    for s in range(1, 4):
        pairs = []
        for r in range(count):
            z, x, c = row_of(r)
            pairs.append((r, z * 8 + ((x + s) % 4) * 2 + c))
        row_got.append(sent(chip_total, pairs, jnp.bfloat16))
    row_total = None
    in_row = ident
    for place in range(4):
        value = jax.tree.map(
            lambda *parts: jnp.stack(parts)[(across - place) % 4], *row_got
        )
        row_total = value if row_total is None else combine_maps(row_total, value)
        if place < 3:
            in_row = pick(place < across, combine_maps(in_row, value), in_row)

    below = ident
    for s in (3, 2, 1):
        pairs = []
        for r in range(count):
            z, x, c = row_of(r)
            if z + s < count // 8:
                pairs.append((r, r + 8 * s))
        value = sent(row_total, pairs, jnp.bfloat16)
        below = pick(down >= s, combine_maps(below, value), below)

    linear, additive = combine_maps(below, in_row)
    return (
        jnp.einsum("baf,bfu->bau", in_chip[0], additive, precision=maximal_matmul_accuracy)
        + in_chip[1]
    )


def gather_rows(share, axis):
    count, index = lax.axis_size(axis), lax.axis_index(axis)
    pieces = [share] + [
        lax.ppermute(share, axis, [(j, (j - s) % count) for j in range(count)])
        for s in range(1, count)
    ]
    return jnp.roll(jnp.stack(pieces), index, axis=0).reshape((-1,) + share.shape[1:])


def scatter_sum(full, axis):
    count, index = lax.axis_size(axis), lax.axis_index(axis)
    rows = full.shape[0] // count
    total = lax.dynamic_slice_in_dim(full, index * rows, rows, 0).astype(jnp.float32)
    for s in range(1, count):
        part = lax.dynamic_slice_in_dim(full, ((index + s) % count) * rows, rows, 0)
        got = lax.ppermute(part, axis, [(j, (j + s) % count) for j in range(count)])
        total = total + got.astype(jnp.float32)
    return total


def req_count():
    return lax.axis_size("z") * lax.axis_size("x") * lax.axis_size("core")


def rms_scale(values, gain):
    mean_square = jnp.mean(values * values, axis=-1, keepdims=True)
    return values / jnp.sqrt(mean_square + 1e-06) * gain


def unit_norm(values):
    return values / jnp.sqrt(jnp.sum(values * values, axis=-1, keepdims=True) + 1e-06)


def segment_of(positions, lengths):
    bounds = jnp.cumsum(lengths)[:-1]
    return jnp.sum((positions[:, None] >= bounds[None, :]).astype(jnp.int32), axis=1)


def causal_conv(projected, rim_rows, kernel, segment_ids, rim_segments):
    taps_count = kernel.shape[0]
    row_count = projected.shape[0]
    extended = jnp.concatenate([rim_rows, projected], axis=0).astype(jnp.float32)
    extended_ids = jnp.concatenate([rim_segments, segment_ids], axis=0)
    accumulated = jnp.zeros(projected.shape, jnp.float32)
    for offset in range(taps_count):
        window = lax.slice_in_dim(extended, offset, offset + row_count, axis=0)
        window_ids = lax.slice_in_dim(extended_ids, offset, offset + row_count, axis=0)
        same_doc = (window_ids == segment_ids)[:, None]
        accumulated = accumulated + kernel[offset][None, :] * jnp.where(same_doc, window, 0.0)
    return accumulated


def unit_lower_inverse(system):
    size = system.shape[-1]
    rows = jnp.arange(size)[:, None]
    cols = jnp.arange(size)[None, :]
    inverse = jnp.broadcast_to(jnp.eye(size, dtype=system.dtype), system.shape)
    block = 1
    while block < size:
        lower_left = (
            (rows // (2 * block) == cols // (2 * block))
            & ((rows // block) % 2 == 1)
            & ((cols // block) % 2 == 0)
        )
        coupling = jnp.where(lower_left, system, 0.0)
        joined = jnp.einsum(
            "hij,hjk->hik",
            jnp.einsum("hij,hjk->hik", inverse, coupling, precision=maximal_matmul_accuracy),
            inverse,
            precision=maximal_matmul_accuracy,
        )
        inverse = inverse - joined
        block *= 2
    return inverse


def group_parts(query_vecs, key_vecs, value_vecs, beta_vals, log_decay, segment_ids, prior_segment):
    group_rows = query_vecs.shape[0]
    value_dim = value_vecs.shape[-1]
    cumulative = jnp.cumsum(log_decay, axis=0)
    row_index = jnp.arange(group_rows)[:, None]
    col_index = jnp.arange(group_rows)[None, :]
    same_doc = segment_ids[:, None] == segment_ids[None, :]
    keep_mask = ((row_index >= col_index) & same_doc)[None, :, :]
    strict_mask = (row_index > col_index)[None, :, :]
    head_cumul = jnp.transpose(cumulative)
    gaps = head_cumul[:, :, None] - head_cumul[:, None, :]
    weights = jnp.where(keep_mask, jnp.exp(jnp.where(keep_mask, gaps, 0.0)), 0.0)
    open_mask = (segment_ids == prior_segment).astype(query_vecs.dtype)
    start_decay = jnp.exp(cumulative) * open_mask[:, None]
    key_dots = jnp.einsum("ihd,jhd->hij", key_vecs, key_vecs, precision=maximal_matmul_accuracy)
    coupling = jnp.where(
        strict_mask, jnp.transpose(beta_vals)[:, :, None] * weights * key_dots, 0.0
    )
    system = coupling + jnp.eye(group_rows, dtype=query_vecs.dtype)[None]
    targets = jnp.concatenate(
        [beta_vals[:, :, None] * value_vecs, (beta_vals * start_decay)[:, :, None] * key_vecs],
        axis=-1,
    )
    solved = jnp.einsum(
        "hij,hjc->hic",
        unit_lower_inverse(system),
        jnp.transpose(targets, (1, 0, 2)),
        precision=maximal_matmul_accuracy,
    )
    starting_value_rows = solved[:, :, :value_dim]
    delta_correction = solved[:, :, value_dim:]
    query_dots = weights * jnp.einsum(
        "ihd,jhd->hij", query_vecs, key_vecs, precision=maximal_matmul_accuracy
    )
    query_begin_offset = query_vecs * start_decay[:, :, None]
    final_key_rows = key_vecs * jnp.transpose(weights[:, -1, :])[:, :, None]
    carried_decay_factor = start_decay[-1]
    return (
        starting_value_rows,
        delta_correction,
        query_dots,
        query_begin_offset,
        final_key_rows,
        carried_decay_factor,
    )


def group_step(running_state, parts):
    (
        starting_value_rows,
        delta_correction,
        query_dots,
        query_begin_offset,
        final_key_rows,
        carried_decay_factor,
    ) = parts
    fresh_state_update = starting_value_rows - jnp.einsum(
        "mxf,mft->mxt", delta_correction, running_state, precision=maximal_matmul_accuracy
    )
    output_rows = jnp.einsum(
        "fob,obt->fot", query_begin_offset, running_state, precision=maximal_matmul_accuracy
    )
    output_rows = output_rows + jnp.einsum(
        "hij,hjv->ihv", query_dots, fresh_state_update, precision=maximal_matmul_accuracy
    )
    updated_state = carried_decay_factor[:, None, None] * running_state + jnp.einsum(
        "new,enr->ewr", final_key_rows, fresh_state_update, precision=maximal_matmul_accuracy
    )
    return (updated_state, output_rows)


def combine_maps(earlier, later):
    earlier_map, preceding_additive = earlier
    following_linear_map, following_additive = later
    joined_map = jnp.einsum(
        "hkl,hlm->hkm", following_linear_map, earlier_map, precision=maximal_matmul_accuracy
    )
    joined_add = (
        jnp.einsum(
            "baf,bfu->bau",
            following_linear_map,
            preceding_additive,
            precision=maximal_matmul_accuracy,
        )
        + following_additive
    )
    return (joined_map, joined_add)


def per_device(
    tokens,
    lengths,
    in_gain,
    w_query,
    w_key,
    w_value,
    w_gate,
    w_beta,
    w_decay,
    decay_log,
    decay_bias,
    conv_query,
    conv_key,
    conv_value,
    head_gain,
    w_out,
    mlp_gain,
    w_up_gate,
    w_up,
    w_down,
):
    share_rows = tokens.shape[0]
    gathered = gather_rows(tokens, "mlp")
    piece_len = gathered.shape[0]
    head_count = w_beta.shape[1]
    key_dim = w_query.shape[1] // head_count
    value_dim = w_value.shape[1] // head_count
    taps_count = conv_query.shape[0]
    group_count = piece_len // GROUP
    piece_start = lax.axis_index(REQ) * piece_len
    positions = piece_start + jnp.arange(piece_len, dtype=jnp.int32)
    segment_ids = segment_of(positions, lengths)
    rim_segments = segment_of(
        piece_start - (taps_count - 1) + jnp.arange(taps_count - 1, dtype=jnp.int32), lengths
    )
    token_rows = gathered.astype(jnp.float32)
    normed = rms_scale(token_rows, in_gain).astype(jnp.bfloat16)
    proj_query = jnp.dot(normed, w_query, preferred_element_type=jnp.float32).astype(jnp.bfloat16)
    proj_key = jnp.dot(normed, w_key, preferred_element_type=jnp.float32).astype(jnp.bfloat16)
    proj_value = jnp.dot(normed, w_value, preferred_element_type=jnp.float32).astype(jnp.bfloat16)
    edge_rows = jnp.concatenate(
        [
            proj_query[piece_len - taps_count + 1 :],
            proj_key[piece_len - taps_count + 1 :],
            proj_value[piece_len - taps_count + 1 :],
        ],
        axis=1,
    )
    rim_all = lax.ppermute(edge_rows, REQ, [(r, r + 1) for r in range(req_count() - 1)])
    query_width = proj_query.shape[1]
    key_width = proj_key.shape[1]
    rim_query = rim_all[:, :query_width]
    rim_key = rim_all[:, query_width : query_width + key_width]
    rim_value = rim_all[:, query_width + key_width :]
    conv_q = jax.nn.silu(causal_conv(proj_query, rim_query, conv_query, segment_ids, rim_segments))
    conv_k = jax.nn.silu(causal_conv(proj_key, rim_key, conv_key, segment_ids, rim_segments))
    conv_v = jax.nn.silu(causal_conv(proj_value, rim_value, conv_value, segment_ids, rim_segments))
    query_vecs = unit_norm(conv_q.reshape(piece_len, head_count, key_dim)) * key_dim ** (-0.5)
    key_vecs = unit_norm(conv_k.reshape(piece_len, head_count, key_dim))
    value_vecs = conv_v.reshape(piece_len, head_count, value_dim)
    gate_lin = jnp.dot(normed, w_gate, preferred_element_type=jnp.float32).astype(jnp.bfloat16)
    beta_vals = jax.nn.sigmoid(jnp.dot(normed, w_beta, preferred_element_type=jnp.float32))
    log_decay = -jnp.exp(decay_log) * jax.nn.softplus(
        jnp.dot(normed, w_decay, preferred_element_type=jnp.float32) + decay_bias
    )

    def shaped(values):
        return values.reshape((group_count, GROUP) + values.shape[1:])

    prior_ids = segment_of(
        piece_start + jnp.arange(group_count, dtype=jnp.int32) * GROUP - 1, lengths
    )
    parts = jax.vmap(group_parts)(
        shaped(query_vecs),
        shaped(key_vecs),
        shaped(value_vecs),
        shaped(beta_vals),
        shaped(log_decay),
        shaped(segment_ids),
        prior_ids,
    )
    eye_block = jnp.broadcast_to(
        jnp.eye(key_dim, dtype=jnp.float32), (head_count, key_dim, key_dim)
    )
    zero_state = jnp.zeros((head_count, key_dim, value_dim), jnp.float32)

    (
        starting_value_rows,
        delta_correction,
        query_dots,
        query_begin_offset,
        final_key_rows,
        carried_decay_factor,
    ) = parts
    local_maps = carried_decay_factor[:, :, None, None] * eye_block - jnp.einsum(
        "gchk,ghcl->ghkl", final_key_rows, delta_correction, precision=maximal_matmul_accuracy
    )
    local_adds = jnp.einsum(
        "gnew,genr->gewr", final_key_rows, starting_value_rows, precision=maximal_matmul_accuracy
    )
    before = [(eye_block, zero_state)]
    for g in range(group_count):
        before.append(combine_maps(before[-1], (local_maps[g], local_adds[g])))
    start_linear = jnp.stack([m[0] for m in before[:-1]])
    start_additive = jnp.stack([m[1] for m in before[:-1]])
    state_query = query_begin_offset - jnp.einsum(
        "ghij,ghjk->gihk", query_dots, delta_correction, precision=maximal_matmul_accuracy
    )
    inner_rows = jnp.einsum(
        "ghij,ghjv->gihv", query_dots, starting_value_rows, precision=maximal_matmul_accuracy
    ) + jnp.einsum(
        "gihk,ghkv->gihv", state_query, start_additive, precision=maximal_matmul_accuracy
    )
    entry_query = jnp.einsum(
        "gihk,ghkl->gihl", state_query, start_linear, precision=maximal_matmul_accuracy
    )
    incoming = prefix_state(before[-1], eye_block)
    w_down, incoming = lax.optimization_barrier((w_down, incoming))
    output_rows = inner_rows + jnp.einsum(
        "gihk,hkv->gihv", entry_query, incoming, precision=maximal_matmul_accuracy
    )
    output_rows = output_rows.reshape(piece_len, head_count, value_dim)
    gate_vals = jax.nn.silu(gate_lin.astype(jnp.float32)).reshape(piece_len, head_count, value_dim)
    head_out = (
        (rms_scale(output_rows, head_gain) * gate_vals)
        .reshape(piece_len, head_count * value_dim)
        .astype(jnp.bfloat16)
    )
    partial_out = jnp.dot(head_out, w_out, preferred_element_type=jnp.float32)
    attn_mine = scatter_sum(partial_out.astype(jnp.bfloat16), "mlp")
    resid_mine = tokens.astype(jnp.float32) + attn_mine
    mlp_in = gather_rows(rms_scale(resid_mine, mlp_gain).astype(jnp.bfloat16), "mlp")

    rows = mlp_in.shape[0]
    chips = req_count() // 2
    block = mlp_in.shape[1] // (2 * chips)
    mlp_in = mlp_in.reshape(rows, chips, 2, block).transpose(0, 2, 1, 3).reshape(rows, -1)

    def gathered(weight, axis):
        half = lax.all_gather(weight, ("z", "x"), axis=axis, tiled=True)
        return lax.all_gather(half, "core", axis=axis, tiled=True)

    def add_rows(piece):
        return jnp.dot(mlp_in, piece, preferred_element_type=jnp.float32)

    gate_acc = add_rows(gathered(w_up_gate, 0))
    up_acc = add_rows(gathered(w_up, 0))
    hidden = (jax.nn.silu(gate_acc) * up_acc).astype(jnp.bfloat16)
    down_terms = jnp.dot(hidden, gathered(w_down, 1), preferred_element_type=jnp.float32)
    down_terms = (
        down_terms.reshape(rows, 2, chips, block).transpose(0, 2, 1, 3).reshape(rows, -1)
    )
    mlp_share = scatter_sum(down_terms.astype(jnp.bfloat16), "mlp")
    return (resid_mine + mlp_share).astype(jnp.bfloat16)


def solution(mesh):
    rows = ("z", "x", "core", "mlp")
    req_devices = mesh.shape["req"]
    split = jax.sharding.Mesh(
        mesh.devices.reshape(req_devices // 8, 4, 2, mesh.shape["mlp"]), rows
    )
    placed = (
        P(rows, None),
        P(),
        P(),
        P(None, "mlp"),
        P(None, "mlp"),
        P(None, "mlp"),
        P(None, "mlp"),
        P(None, "mlp"),
        P(None, "mlp"),
        P("mlp"),
        P("mlp"),
        P(None, "mlp"),
        P(None, "mlp"),
        P(None, "mlp"),
        P(),
        P("mlp", None),
        P(),
        P(REQ, "mlp"),
        P(REQ, "mlp"),
        P("mlp", REQ),
    )
    return jax.shard_map(
        per_device, mesh=split, in_specs=placed, out_specs=P(rows, None), check_vma=False
    )
```

```python
import jax
import jax.numpy as jnp
from jax import lax
from jax.sharding import PartitionSpec as P

GROUP = 64


maximal_matmul_accuracy = lax.Precision.DEFAULT


def shifted(value, axis, steps):
    count = lax.axis_size(axis)
    first, last = (max(0, -steps), min(count, count - steps))
    return lax.ppermute(value, axis, [(source, source + steps) for source in range(first, last)])


def carried_in(shard, axis, combine, identity):
    length, index = (lax.axis_size(axis), lax.axis_index(axis))
    everything = jax.tree.map(
        lambda part, kind: lax.all_gather(part.astype(kind), axis),
        shard,
        jax.tree.map(lambda a: jnp.bfloat16 if a.dtype == jnp.float32 else a.dtype, shard),
    )
    start = jax.tree.map(
        lambda part, zero: jnp.broadcast_to(jnp.asarray(zero, part.dtype), part.shape),
        shard,
        identity,
    )

    def step(k, before):
        reached = k < index
        new = combine(
            before, jax.tree.map(lambda part, own: part[k].astype(own.dtype), everything, shard)
        )
        return jax.tree.map(lambda a, b: jnp.where(reached, a, b), new, before)

    return lax.fori_loop(0, length, step, start)


def prefix_state(piece_map, eye_block):
    index, count = lax.axis_index("req"), lax.axis_size("req")
    core, across, down = index % 2, (index // 2) % 4, index // 8
    ident = (eye_block, jnp.zeros_like(piece_map[1]))

    def pick(flag, a, b):
        return jax.tree.map(lambda u, v: jnp.where(flag, u, v), a, b)

    def sent(value, pairs, kind):
        got = lax.ppermute(jax.tree.map(lambda a: a.astype(kind), value), "req", pairs)
        return jax.tree.map(lambda a: a.astype(jnp.float32), got)

    other = sent(piece_map, [(r, r ^ 1) for r in range(count)], jnp.float32)
    first = core == 0
    chip_total = pick(first, combine_maps(piece_map, other), combine_maps(other, piece_map))
    in_chip = pick(first, ident, other)

    def row_of(r):
        return (r // 8, (r // 2) % 4, r % 2)

    row_got = [chip_total]
    for s in range(1, 4):
        pairs = []
        for r in range(count):
            z, x, c = row_of(r)
            pairs.append((r, z * 8 + ((x + s) % 4) * 2 + c))
        row_got.append(sent(chip_total, pairs, jnp.bfloat16))
    row_total = None
    in_row = ident
    for place in range(4):
        value = jax.tree.map(
            lambda *parts: jnp.stack(parts)[(across - place) % 4], *row_got
        )
        row_total = value if row_total is None else combine_maps(row_total, value)
        if place < 3:
            in_row = pick(place < across, combine_maps(in_row, value), in_row)

    below = ident
    for s in (3, 2, 1):
        pairs = []
        for r in range(count):
            z, x, c = row_of(r)
            if z + s < count // 8:
                pairs.append((r, r + 8 * s))
        value = sent(row_total, pairs, jnp.bfloat16)
        below = pick(down >= s, combine_maps(below, value), below)

    linear, additive = combine_maps(below, in_row)
    return (
        jnp.einsum("baf,bfu->bau", in_chip[0], additive, precision=maximal_matmul_accuracy)
        + in_chip[1]
    )


def gather_rows(share, axis):
    count, index = lax.axis_size(axis), lax.axis_index(axis)
    pieces = [share] + [
        lax.ppermute(share, axis, [(j, (j - s) % count) for j in range(count)])
        for s in range(1, count)
    ]
    return jnp.roll(jnp.stack(pieces), index, axis=0).reshape((-1,) + share.shape[1:])


def scatter_sum(full, axis):
    count, index = lax.axis_size(axis), lax.axis_index(axis)
    rows = full.shape[0] // count
    total = lax.dynamic_slice_in_dim(full, index * rows, rows, 0).astype(jnp.float32)
    for s in range(1, count):
        part = lax.dynamic_slice_in_dim(full, ((index + s) % count) * rows, rows, 0)
        got = lax.ppermute(part, axis, [(j, (j + s) % count) for j in range(count)])
        total = total + got.astype(jnp.float32)
    return total


def rms_scale(values, gain):
    mean_square = jnp.mean(values * values, axis=-1, keepdims=True)
    return values / jnp.sqrt(mean_square + 1e-06) * gain


def unit_norm(values):
    return values / jnp.sqrt(jnp.sum(values * values, axis=-1, keepdims=True) + 1e-06)


def segment_of(positions, lengths):
    bounds = jnp.cumsum(lengths)[:-1]
    return jnp.sum((positions[:, None] >= bounds[None, :]).astype(jnp.int32), axis=1)


def causal_conv(projected, rim_rows, kernel, segment_ids, rim_segments):
    taps_count = kernel.shape[0]
    row_count = projected.shape[0]
    extended = jnp.concatenate([rim_rows, projected], axis=0).astype(jnp.float32)
    extended_ids = jnp.concatenate([rim_segments, segment_ids], axis=0)
    accumulated = jnp.zeros(projected.shape, jnp.float32)
    for offset in range(taps_count):
        window = lax.slice_in_dim(extended, offset, offset + row_count, axis=0)
        window_ids = lax.slice_in_dim(extended_ids, offset, offset + row_count, axis=0)
        same_doc = (window_ids == segment_ids)[:, None]
        accumulated = accumulated + kernel[offset][None, :] * jnp.where(same_doc, window, 0.0)
    return accumulated


def unit_lower_inverse(system):
    size = system.shape[-1]
    rows = jnp.arange(size)[:, None]
    cols = jnp.arange(size)[None, :]
    inverse = jnp.broadcast_to(jnp.eye(size, dtype=system.dtype), system.shape)
    block = 1
    while block < size:
        lower_left = (
            (rows // (2 * block) == cols // (2 * block))
            & ((rows // block) % 2 == 1)
            & ((cols // block) % 2 == 0)
        )
        coupling = jnp.where(lower_left, system, 0.0)
        joined = jnp.einsum(
            "hij,hjk->hik",
            jnp.einsum("hij,hjk->hik", inverse, coupling, precision=maximal_matmul_accuracy),
            inverse,
            precision=maximal_matmul_accuracy,
        )
        inverse = inverse - joined
        block *= 2
    return inverse


def group_parts(query_vecs, key_vecs, value_vecs, beta_vals, log_decay, segment_ids, prior_segment):
    group_rows = query_vecs.shape[0]
    value_dim = value_vecs.shape[-1]
    cumulative = jnp.cumsum(log_decay, axis=0)
    row_index = jnp.arange(group_rows)[:, None]
    col_index = jnp.arange(group_rows)[None, :]
    same_doc = segment_ids[:, None] == segment_ids[None, :]
    keep_mask = ((row_index >= col_index) & same_doc)[None, :, :]
    strict_mask = (row_index > col_index)[None, :, :]
    head_cumul = jnp.transpose(cumulative)
    gaps = head_cumul[:, :, None] - head_cumul[:, None, :]
    weights = jnp.where(keep_mask, jnp.exp(jnp.where(keep_mask, gaps, 0.0)), 0.0)
    open_mask = (segment_ids == prior_segment).astype(query_vecs.dtype)
    start_decay = jnp.exp(cumulative) * open_mask[:, None]
    key_dots = jnp.einsum("ihd,jhd->hij", key_vecs, key_vecs, precision=maximal_matmul_accuracy)
    coupling = jnp.where(
        strict_mask, jnp.transpose(beta_vals)[:, :, None] * weights * key_dots, 0.0
    )
    system = coupling + jnp.eye(group_rows, dtype=query_vecs.dtype)[None]
    targets = jnp.concatenate(
        [beta_vals[:, :, None] * value_vecs, (beta_vals * start_decay)[:, :, None] * key_vecs],
        axis=-1,
    )
    solved = jnp.einsum(
        "hij,hjc->hic",
        unit_lower_inverse(system),
        jnp.transpose(targets, (1, 0, 2)),
        precision=maximal_matmul_accuracy,
    )
    starting_value_rows = solved[:, :, :value_dim]
    delta_correction = solved[:, :, value_dim:]
    query_dots = weights * jnp.einsum(
        "ihd,jhd->hij", query_vecs, key_vecs, precision=maximal_matmul_accuracy
    )
    query_begin_offset = query_vecs * start_decay[:, :, None]
    final_key_rows = key_vecs * jnp.transpose(weights[:, -1, :])[:, :, None]
    carried_decay_factor = start_decay[-1]
    return (
        starting_value_rows,
        delta_correction,
        query_dots,
        query_begin_offset,
        final_key_rows,
        carried_decay_factor,
    )


def group_step(running_state, parts):
    (
        starting_value_rows,
        delta_correction,
        query_dots,
        query_begin_offset,
        final_key_rows,
        carried_decay_factor,
    ) = parts
    fresh_state_update = starting_value_rows - jnp.einsum(
        "mxf,mft->mxt", delta_correction, running_state, precision=maximal_matmul_accuracy
    )
    output_rows = jnp.einsum(
        "fob,obt->fot", query_begin_offset, running_state, precision=maximal_matmul_accuracy
    )
    output_rows = output_rows + jnp.einsum(
        "hij,hjv->ihv", query_dots, fresh_state_update, precision=maximal_matmul_accuracy
    )
    updated_state = carried_decay_factor[:, None, None] * running_state + jnp.einsum(
        "new,enr->ewr", final_key_rows, fresh_state_update, precision=maximal_matmul_accuracy
    )
    return (updated_state, output_rows)


def combine_maps(earlier, later):
    earlier_map, preceding_additive = earlier
    following_linear_map, following_additive = later
    joined_map = jnp.einsum(
        "hkl,hlm->hkm", following_linear_map, earlier_map, precision=maximal_matmul_accuracy
    )
    joined_add = (
        jnp.einsum(
            "baf,bfu->bau",
            following_linear_map,
            preceding_additive,
            precision=maximal_matmul_accuracy,
        )
        + following_additive
    )
    return (joined_map, joined_add)


def per_device(
    tokens,
    lengths,
    in_gain,
    w_query,
    w_key,
    w_value,
    w_gate,
    w_beta,
    w_decay,
    decay_log,
    decay_bias,
    conv_query,
    conv_key,
    conv_value,
    head_gain,
    w_out,
    mlp_gain,
    w_up_gate,
    w_up,
    w_down,
):
    share_rows = tokens.shape[0]
    gathered = gather_rows(tokens, "mlp")
    piece_len = gathered.shape[0]
    head_count = w_beta.shape[1]
    key_dim = w_query.shape[1] // head_count
    value_dim = w_value.shape[1] // head_count
    taps_count = conv_query.shape[0]
    group_count = piece_len // GROUP
    piece_start = lax.axis_index("req") * piece_len
    positions = piece_start + jnp.arange(piece_len, dtype=jnp.int32)
    segment_ids = segment_of(positions, lengths)
    rim_segments = segment_of(
        piece_start - (taps_count - 1) + jnp.arange(taps_count - 1, dtype=jnp.int32), lengths
    )
    token_rows = gathered.astype(jnp.float32)
    normed = rms_scale(token_rows, in_gain).astype(jnp.bfloat16)
    proj_query = jnp.dot(normed, w_query, preferred_element_type=jnp.float32).astype(jnp.bfloat16)
    proj_key = jnp.dot(normed, w_key, preferred_element_type=jnp.float32).astype(jnp.bfloat16)
    proj_value = jnp.dot(normed, w_value, preferred_element_type=jnp.float32).astype(jnp.bfloat16)
    edge_rows = jnp.concatenate(
        [
            proj_query[piece_len - taps_count + 1 :],
            proj_key[piece_len - taps_count + 1 :],
            proj_value[piece_len - taps_count + 1 :],
        ],
        axis=1,
    )
    rim_all = shifted(edge_rows, "req", 1)
    query_width = proj_query.shape[1]
    key_width = proj_key.shape[1]
    rim_query = rim_all[:, :query_width]
    rim_key = rim_all[:, query_width : query_width + key_width]
    rim_value = rim_all[:, query_width + key_width :]
    conv_q = jax.nn.silu(causal_conv(proj_query, rim_query, conv_query, segment_ids, rim_segments))
    conv_k = jax.nn.silu(causal_conv(proj_key, rim_key, conv_key, segment_ids, rim_segments))
    conv_v = jax.nn.silu(causal_conv(proj_value, rim_value, conv_value, segment_ids, rim_segments))
    query_vecs = unit_norm(conv_q.reshape(piece_len, head_count, key_dim)) * key_dim ** (-0.5)
    key_vecs = unit_norm(conv_k.reshape(piece_len, head_count, key_dim))
    value_vecs = conv_v.reshape(piece_len, head_count, value_dim)
    gate_lin = jnp.dot(normed, w_gate, preferred_element_type=jnp.float32).astype(jnp.bfloat16)
    beta_vals = jax.nn.sigmoid(jnp.dot(normed, w_beta, preferred_element_type=jnp.float32))
    log_decay = -jnp.exp(decay_log) * jax.nn.softplus(
        jnp.dot(normed, w_decay, preferred_element_type=jnp.float32) + decay_bias
    )

    def shaped(values):
        return values.reshape((group_count, GROUP) + values.shape[1:])

    prior_ids = segment_of(
        piece_start + jnp.arange(group_count, dtype=jnp.int32) * GROUP - 1, lengths
    )
    parts = jax.vmap(group_parts)(
        shaped(query_vecs),
        shaped(key_vecs),
        shaped(value_vecs),
        shaped(beta_vals),
        shaped(log_decay),
        shaped(segment_ids),
        prior_ids,
    )
    eye_block = jnp.broadcast_to(
        jnp.eye(key_dim, dtype=jnp.float32), (head_count, key_dim, key_dim)
    )
    zero_state = jnp.zeros((head_count, key_dim, value_dim), jnp.float32)

    (
        starting_value_rows,
        delta_correction,
        query_dots,
        query_begin_offset,
        final_key_rows,
        carried_decay_factor,
    ) = parts
    local_maps = carried_decay_factor[:, :, None, None] * eye_block - jnp.einsum(
        "gchk,ghcl->ghkl", final_key_rows, delta_correction, precision=maximal_matmul_accuracy
    )
    local_adds = jnp.einsum(
        "gnew,genr->gewr", final_key_rows, starting_value_rows, precision=maximal_matmul_accuracy
    )
    before = [(eye_block, zero_state)]
    for g in range(group_count):
        before.append(combine_maps(before[-1], (local_maps[g], local_adds[g])))
    start_linear = jnp.stack([m[0] for m in before[:-1]])
    start_additive = jnp.stack([m[1] for m in before[:-1]])
    state_query = query_begin_offset - jnp.einsum(
        "ghij,ghjk->gihk", query_dots, delta_correction, precision=maximal_matmul_accuracy
    )
    inner_rows = jnp.einsum(
        "ghij,ghjv->gihv", query_dots, starting_value_rows, precision=maximal_matmul_accuracy
    ) + jnp.einsum(
        "gihk,ghkv->gihv", state_query, start_additive, precision=maximal_matmul_accuracy
    )
    entry_query = jnp.einsum(
        "gihk,ghkl->gihl", state_query, start_linear, precision=maximal_matmul_accuracy
    )
    incoming = prefix_state(before[-1], eye_block)
    w_down, incoming = lax.optimization_barrier((w_down, incoming))
    output_rows = inner_rows + jnp.einsum(
        "gihk,hkv->gihv", entry_query, incoming, precision=maximal_matmul_accuracy
    )
    output_rows = output_rows.reshape(piece_len, head_count, value_dim)
    gate_vals = jax.nn.silu(gate_lin.astype(jnp.float32)).reshape(piece_len, head_count, value_dim)
    head_out = (
        (rms_scale(output_rows, head_gain) * gate_vals)
        .reshape(piece_len, head_count * value_dim)
        .astype(jnp.bfloat16)
    )
    partial_out = jnp.dot(head_out, w_out, preferred_element_type=jnp.float32)
    attn_mine = scatter_sum(partial_out.astype(jnp.bfloat16), "mlp")
    resid_mine = tokens.astype(jnp.float32) + attn_mine
    mlp_in = gather_rows(rms_scale(resid_mine, mlp_gain).astype(jnp.bfloat16), "mlp")

    def add_rows(piece):
        return jnp.dot(mlp_in, piece, preferred_element_type=jnp.float32)

    gate_acc = add_rows(lax.all_gather(w_up_gate, "req", axis=0, tiled=True))
    up_acc = add_rows(lax.all_gather(w_up, "req", axis=0, tiled=True))
    hidden = (jax.nn.silu(gate_acc) * up_acc).astype(jnp.bfloat16)
    down_terms = jnp.dot(
        hidden,
        lax.all_gather(w_down, "req", axis=1, tiled=True),
        preferred_element_type=jnp.float32,
    )
    mlp_share = scatter_sum(down_terms.astype(jnp.bfloat16), "mlp")
    return (resid_mine + mlp_share).astype(jnp.bfloat16)


def solution(mesh):
    placed = (
        P(("req", "mlp"), None),
        P(),
        P(),
        P(None, "mlp"),
        P(None, "mlp"),
        P(None, "mlp"),
        P(None, "mlp"),
        P(None, "mlp"),
        P(None, "mlp"),
        P("mlp"),
        P("mlp"),
        P(None, "mlp"),
        P(None, "mlp"),
        P(None, "mlp"),
        P(),
        P("mlp", None),
        P(),
        P("req", "mlp"),
        P("req", "mlp"),
        P("mlp", "req"),
    )
    return jax.shard_map(
        per_device, mesh=mesh, in_specs=placed, out_specs=P(("req", "mlp"), None), check_vma=False
    )
```

```python
import jax
import jax.numpy as jnp
from jax import lax
from jax.sharding import PartitionSpec as P

GROUP = 64


maximal_matmul_accuracy = lax.Precision.HIGH


def shifted(value, axis, steps):
    count = lax.axis_size(axis)
    first, last = (max(0, -steps), min(count, count - steps))
    return lax.ppermute(value, axis, [(source, source + steps) for source in range(first, last)])


def carried_in(shard, axis, combine, identity):
    length, index = (lax.axis_size(axis), lax.axis_index(axis))
    everything = jax.tree.map(
        lambda part, kind: lax.all_gather(part.astype(kind), axis),
        shard,
        jax.tree.map(lambda a: jnp.bfloat16 if a.dtype == jnp.float32 else a.dtype, shard),
    )
    start = jax.tree.map(
        lambda part, zero: jnp.broadcast_to(jnp.asarray(zero, part.dtype), part.shape),
        shard,
        identity,
    )

    def step(k, before):
        reached = k < index
        new = combine(
            before, jax.tree.map(lambda part, own: part[k].astype(own.dtype), everything, shard)
        )
        return jax.tree.map(lambda a, b: jnp.where(reached, a, b), new, before)

    return lax.fori_loop(0, length, step, start)


def prefix_state(piece_map, eye_block, riders):
    index, count = lax.axis_index("req"), lax.axis_size("req")
    core, across, down = index % 2, (index // 2) % 4, index // 8
    ident = (eye_block, jnp.zeros_like(piece_map[1]))

    def pick(flag, a, b):
        return jax.tree.map(lambda u, v: jnp.where(flag, u, v), a, b)

    def sent(value, pairs, kind):
        got = lax.ppermute(jax.tree.map(lambda a: a.astype(kind), value), "req", pairs)
        return jax.tree.map(lambda a: a.astype(jnp.float32), got)

    other = sent(piece_map, [(r, r ^ 1) for r in range(count)], jnp.float32)
    first = core == 0
    chip_total = pick(first, combine_maps(piece_map, other), combine_maps(other, piece_map))
    chip_total, riders = lax.optimization_barrier((chip_total, riders))
    in_chip = pick(first, ident, other)

    def row_of(r):
        return (r // 8, (r // 2) % 4, r % 2)

    row_got = [chip_total]
    for s in range(1, 4):
        pairs = []
        for r in range(count):
            z, x, c = row_of(r)
            pairs.append((r, z * 8 + ((x + s) % 4) * 2 + c))
        row_got.append(sent(chip_total, pairs, jnp.bfloat16))
    row_total = None
    in_row = ident
    for place in range(4):
        value = jax.tree.map(
            lambda *parts: jnp.stack(parts)[(across - place) % 4], *row_got
        )
        row_total = value if row_total is None else combine_maps(row_total, value)
        if place < 3:
            in_row = pick(place < across, combine_maps(in_row, value), in_row)

    below = ident
    for s in (3, 2, 1):
        pairs = []
        for r in range(count):
            z, x, c = row_of(r)
            if z + s < count // 8:
                pairs.append((r, r + 8 * s))
        value = sent(row_total, pairs, jnp.bfloat16)
        below = pick(down >= s, combine_maps(below, value), below)

    linear, additive = combine_maps(below, in_row)
    return (
        jnp.einsum("baf,bfu->bau", in_chip[0], additive, precision=maximal_matmul_accuracy)
        + in_chip[1]
    ), riders


def gather_rows(share, axis):
    count, index = lax.axis_size(axis), lax.axis_index(axis)
    pieces = [share] + [
        lax.ppermute(share, axis, [(j, (j - s) % count) for j in range(count)])
        for s in range(1, count)
    ]
    return jnp.roll(jnp.stack(pieces), index, axis=0).reshape((-1,) + share.shape[1:])


def scatter_sum(full, axis):
    count, index = lax.axis_size(axis), lax.axis_index(axis)
    rows = full.shape[0] // count
    total = lax.dynamic_slice_in_dim(full, index * rows, rows, 0).astype(jnp.float32)
    for s in range(1, count):
        part = lax.dynamic_slice_in_dim(full, ((index + s) % count) * rows, rows, 0)
        got = lax.ppermute(part, axis, [(j, (j + s) % count) for j in range(count)])
        total = total + got.astype(jnp.float32)
    return total


def rms_scale(values, gain):
    mean_square = jnp.mean(values * values, axis=-1, keepdims=True)
    return values / jnp.sqrt(mean_square + 1e-06) * gain


def unit_norm(values):
    return values / jnp.sqrt(jnp.sum(values * values, axis=-1, keepdims=True) + 1e-06)


def segment_of(positions, lengths):
    bounds = jnp.cumsum(lengths)[:-1]
    return jnp.sum((positions[:, None] >= bounds[None, :]).astype(jnp.int32), axis=1)


def causal_conv(projected, rim_rows, kernel, segment_ids, rim_segments):
    taps_count = kernel.shape[0]
    row_count = projected.shape[0]
    extended = jnp.concatenate([rim_rows, projected], axis=0).astype(jnp.float32)
    extended_ids = jnp.concatenate([rim_segments, segment_ids], axis=0)
    accumulated = jnp.zeros(projected.shape, jnp.float32)
    for offset in range(taps_count):
        window = lax.slice_in_dim(extended, offset, offset + row_count, axis=0)
        window_ids = lax.slice_in_dim(extended_ids, offset, offset + row_count, axis=0)
        same_doc = (window_ids == segment_ids)[:, None]
        accumulated = accumulated + kernel[offset][None, :] * jnp.where(same_doc, window, 0.0)
    return accumulated


def unit_lower_inverse(system):
    size = system.shape[-1]
    rows = jnp.arange(size)[:, None]
    cols = jnp.arange(size)[None, :]
    inverse = jnp.broadcast_to(jnp.eye(size, dtype=system.dtype), system.shape)
    block = 1
    while block < size:
        lower_left = (
            (rows // (2 * block) == cols // (2 * block))
            & ((rows // block) % 2 == 1)
            & ((cols // block) % 2 == 0)
        )
        coupling = jnp.where(lower_left, system, 0.0)
        joined = jnp.einsum(
            "hij,hjk->hik",
            jnp.einsum("hij,hjk->hik", inverse, coupling, precision=maximal_matmul_accuracy),
            inverse,
            precision=maximal_matmul_accuracy,
        )
        inverse = inverse - joined
        block *= 2
    return inverse


def group_parts(query_vecs, key_vecs, value_vecs, beta_vals, log_decay, segment_ids, prior_segment):
    group_rows = query_vecs.shape[0]
    value_dim = value_vecs.shape[-1]
    cumulative = jnp.cumsum(log_decay, axis=0)
    row_index = jnp.arange(group_rows)[:, None]
    col_index = jnp.arange(group_rows)[None, :]
    same_doc = segment_ids[:, None] == segment_ids[None, :]
    keep_mask = ((row_index >= col_index) & same_doc)[None, :, :]
    strict_mask = (row_index > col_index)[None, :, :]
    head_cumul = jnp.transpose(cumulative)
    gaps = head_cumul[:, :, None] - head_cumul[:, None, :]
    weights = jnp.where(keep_mask, jnp.exp(jnp.where(keep_mask, gaps, 0.0)), 0.0)
    open_mask = (segment_ids == prior_segment).astype(query_vecs.dtype)
    start_decay = jnp.exp(cumulative) * open_mask[:, None]
    key_dots = jnp.einsum("ihd,jhd->hij", key_vecs, key_vecs, precision=maximal_matmul_accuracy)
    coupling = jnp.where(
        strict_mask, jnp.transpose(beta_vals)[:, :, None] * weights * key_dots, 0.0
    )
    system = coupling + jnp.eye(group_rows, dtype=query_vecs.dtype)[None]
    targets = jnp.concatenate(
        [beta_vals[:, :, None] * value_vecs, (beta_vals * start_decay)[:, :, None] * key_vecs],
        axis=-1,
    )
    solved = jnp.einsum(
        "hij,hjc->hic",
        unit_lower_inverse(system),
        jnp.transpose(targets, (1, 0, 2)),
        precision=maximal_matmul_accuracy,
    )
    starting_value_rows = solved[:, :, :value_dim]
    delta_correction = solved[:, :, value_dim:]
    query_dots = weights * jnp.einsum(
        "ihd,jhd->hij", query_vecs, key_vecs, precision=maximal_matmul_accuracy
    )
    query_begin_offset = query_vecs * start_decay[:, :, None]
    final_key_rows = key_vecs * jnp.transpose(weights[:, -1, :])[:, :, None]
    carried_decay_factor = start_decay[-1]
    return (
        starting_value_rows,
        delta_correction,
        query_dots,
        query_begin_offset,
        final_key_rows,
        carried_decay_factor,
    )


def group_step(running_state, parts):
    (
        starting_value_rows,
        delta_correction,
        query_dots,
        query_begin_offset,
        final_key_rows,
        carried_decay_factor,
    ) = parts
    fresh_state_update = starting_value_rows - jnp.einsum(
        "mxf,mft->mxt", delta_correction, running_state, precision=maximal_matmul_accuracy
    )
    output_rows = jnp.einsum(
        "fob,obt->fot", query_begin_offset, running_state, precision=maximal_matmul_accuracy
    )
    output_rows = output_rows + jnp.einsum(
        "hij,hjv->ihv", query_dots, fresh_state_update, precision=maximal_matmul_accuracy
    )
    updated_state = carried_decay_factor[:, None, None] * running_state + jnp.einsum(
        "new,enr->ewr", final_key_rows, fresh_state_update, precision=maximal_matmul_accuracy
    )
    return (updated_state, output_rows)


def combine_maps(earlier, later):
    earlier_map, preceding_additive = earlier
    following_linear_map, following_additive = later
    joined_map = jnp.einsum(
        "hkl,hlm->hkm", following_linear_map, earlier_map, precision=maximal_matmul_accuracy
    )
    joined_add = (
        jnp.einsum(
            "baf,bfu->bau",
            following_linear_map,
            preceding_additive,
            precision=maximal_matmul_accuracy,
        )
        + following_additive
    )
    return (joined_map, joined_add)


def per_device(
    tokens,
    lengths,
    in_gain,
    w_query,
    w_key,
    w_value,
    w_gate,
    w_beta,
    w_decay,
    decay_log,
    decay_bias,
    conv_query,
    conv_key,
    conv_value,
    head_gain,
    w_out,
    mlp_gain,
    w_up_gate,
    w_up,
    w_down,
):
    share_rows = tokens.shape[0]
    gathered = gather_rows(tokens, "mlp")
    piece_len = gathered.shape[0]
    head_count = w_beta.shape[1]
    key_dim = w_query.shape[1] // head_count
    value_dim = w_value.shape[1] // head_count
    taps_count = conv_query.shape[0]
    group_count = piece_len // GROUP
    piece_start = lax.axis_index("req") * piece_len
    positions = piece_start + jnp.arange(piece_len, dtype=jnp.int32)
    segment_ids = segment_of(positions, lengths)
    rim_segments = segment_of(
        piece_start - (taps_count - 1) + jnp.arange(taps_count - 1, dtype=jnp.int32), lengths
    )
    token_rows = gathered.astype(jnp.float32)
    normed = rms_scale(token_rows, in_gain).astype(jnp.bfloat16)
    proj_query = jnp.dot(normed, w_query, preferred_element_type=jnp.float32).astype(jnp.bfloat16)
    proj_key = jnp.dot(normed, w_key, preferred_element_type=jnp.float32).astype(jnp.bfloat16)
    proj_value = jnp.dot(normed, w_value, preferred_element_type=jnp.float32).astype(jnp.bfloat16)
    edge_rows = jnp.concatenate(
        [
            proj_query[piece_len - taps_count + 1 :],
            proj_key[piece_len - taps_count + 1 :],
            proj_value[piece_len - taps_count + 1 :],
        ],
        axis=1,
    )
    rim_all = shifted(edge_rows, "req", 1)
    query_width = proj_query.shape[1]
    key_width = proj_key.shape[1]
    rim_query = rim_all[:, :query_width]
    rim_key = rim_all[:, query_width : query_width + key_width]
    rim_value = rim_all[:, query_width + key_width :]
    conv_q = jax.nn.silu(causal_conv(proj_query, rim_query, conv_query, segment_ids, rim_segments))
    conv_k = jax.nn.silu(causal_conv(proj_key, rim_key, conv_key, segment_ids, rim_segments))
    conv_v = jax.nn.silu(causal_conv(proj_value, rim_value, conv_value, segment_ids, rim_segments))
    query_vecs = unit_norm(conv_q.reshape(piece_len, head_count, key_dim)) * key_dim ** (-0.5)
    key_vecs = unit_norm(conv_k.reshape(piece_len, head_count, key_dim))
    value_vecs = conv_v.reshape(piece_len, head_count, value_dim)
    gate_lin = jnp.dot(normed, w_gate, preferred_element_type=jnp.float32).astype(jnp.bfloat16)
    beta_vals = jax.nn.sigmoid(jnp.dot(normed, w_beta, preferred_element_type=jnp.float32))
    log_decay = -jnp.exp(decay_log) * jax.nn.softplus(
        jnp.dot(normed, w_decay, preferred_element_type=jnp.float32) + decay_bias
    )

    def shaped(values):
        return values.reshape((group_count, GROUP) + values.shape[1:])

    prior_ids = segment_of(
        piece_start + jnp.arange(group_count, dtype=jnp.int32) * GROUP - 1, lengths
    )
    parts = jax.vmap(group_parts)(
        shaped(query_vecs),
        shaped(key_vecs),
        shaped(value_vecs),
        shaped(beta_vals),
        shaped(log_decay),
        shaped(segment_ids),
        prior_ids,
    )
    eye_block = jnp.broadcast_to(
        jnp.eye(key_dim, dtype=jnp.float32), (head_count, key_dim, key_dim)
    )
    zero_state = jnp.zeros((head_count, key_dim, value_dim), jnp.float32)

    (
        starting_value_rows,
        delta_correction,
        query_dots,
        query_begin_offset,
        final_key_rows,
        carried_decay_factor,
    ) = parts
    local_maps = carried_decay_factor[:, :, None, None] * eye_block - jnp.einsum(
        "gchk,ghcl->ghkl", final_key_rows, delta_correction, precision=maximal_matmul_accuracy
    )
    local_adds = jnp.einsum(
        "gnew,genr->gewr", final_key_rows, starting_value_rows, precision=maximal_matmul_accuracy
    )
    before = [(eye_block, zero_state)]
    for g in range(group_count):
        before.append(combine_maps(before[-1], (local_maps[g], local_adds[g])))
    start_linear = jnp.stack([m[0] for m in before[:-1]])
    start_additive = jnp.stack([m[1] for m in before[:-1]])
    state_query = query_begin_offset - jnp.einsum(
        "ghij,ghjk->gihk", query_dots, delta_correction, precision=maximal_matmul_accuracy
    )
    inner_rows = jnp.einsum(
        "ghij,ghjv->gihv", query_dots, starting_value_rows, precision=maximal_matmul_accuracy
    ) + jnp.einsum(
        "gihk,ghkv->gihv", state_query, start_additive, precision=maximal_matmul_accuracy
    )
    entry_query = jnp.einsum(
        "gihk,ghkl->gihl", state_query, start_linear, precision=maximal_matmul_accuracy
    )
    incoming, (inner_rows, entry_query) = prefix_state(before[-1], eye_block, (inner_rows, entry_query))
    w_down, incoming = lax.optimization_barrier((w_down, incoming))
    output_rows = inner_rows + jnp.einsum(
        "gihk,hkv->gihv", entry_query, incoming, precision=maximal_matmul_accuracy
    )
    output_rows = output_rows.reshape(piece_len, head_count, value_dim)
    gate_vals = jax.nn.silu(gate_lin.astype(jnp.float32)).reshape(piece_len, head_count, value_dim)
    head_out = (
        (rms_scale(output_rows, head_gain) * gate_vals)
        .reshape(piece_len, head_count * value_dim)
        .astype(jnp.bfloat16)
    )
    partial_out = jnp.dot(head_out, w_out, preferred_element_type=jnp.float32)
    attn_mine = scatter_sum(partial_out.astype(jnp.bfloat16), "mlp")
    resid_mine = tokens.astype(jnp.float32) + attn_mine
    mlp_in = gather_rows(rms_scale(resid_mine, mlp_gain).astype(jnp.bfloat16), "mlp")

    def add_rows(piece):
        return jnp.dot(mlp_in, piece, preferred_element_type=jnp.float32)

    gate_acc = add_rows(lax.all_gather(w_up_gate, "req", axis=0, tiled=True))
    up_acc = add_rows(lax.all_gather(w_up, "req", axis=0, tiled=True))
    hidden = (jax.nn.silu(gate_acc) * up_acc).astype(jnp.bfloat16)
    down_terms = jnp.dot(
        hidden,
        lax.all_gather(w_down, "req", axis=1, tiled=True),
        preferred_element_type=jnp.float32,
    )
    mlp_share = scatter_sum(down_terms.astype(jnp.bfloat16), "mlp")
    return (resid_mine + mlp_share).astype(jnp.bfloat16)


def solution(mesh):
    placed = (
        P(("req", "mlp"), None),
        P(),
        P(),
        P(None, "mlp"),
        P(None, "mlp"),
        P(None, "mlp"),
        P(None, "mlp"),
        P(None, "mlp"),
        P(None, "mlp"),
        P("mlp"),
        P("mlp"),
        P(None, "mlp"),
        P(None, "mlp"),
        P(None, "mlp"),
        P(),
        P("mlp", None),
        P(),
        P("req", "mlp"),
        P("req", "mlp"),
        P("mlp", "req"),
    )
    return jax.shard_map(
        per_device, mesh=mesh, in_specs=placed, out_specs=P(("req", "mlp"), None), check_vma=False
    )
```

```python
import jax
import jax.numpy as jnp
from jax import lax
from jax.sharding import PartitionSpec as P

GROUP = 64


maximal_matmul_accuracy = lax.Precision.HIGH


def shifted(value, axis, steps):
    count = lax.axis_size(axis)
    first, last = (max(0, -steps), min(count, count - steps))
    return lax.ppermute(value, axis, [(source, source + steps) for source in range(first, last)])


def carried_in(shard, axis, combine, identity):
    length, index = (lax.axis_size(axis), lax.axis_index(axis))
    everything = jax.tree.map(
        lambda part, kind: lax.all_gather(part.astype(kind), axis),
        shard,
        jax.tree.map(lambda a: jnp.bfloat16 if a.dtype == jnp.float32 else a.dtype, shard),
    )
    start = jax.tree.map(
        lambda part, zero: jnp.broadcast_to(jnp.asarray(zero, part.dtype), part.shape),
        shard,
        identity,
    )

    def step(k, before):
        reached = k < index
        new = combine(
            before, jax.tree.map(lambda part, own: part[k].astype(own.dtype), everything, shard)
        )
        return jax.tree.map(lambda a, b: jnp.where(reached, a, b), new, before)

    return lax.fori_loop(0, length, step, start)


def prefix_state(piece_map, eye_block):
    index, count = lax.axis_index("req"), lax.axis_size("req")
    core, across, down = index % 2, (index // 2) % 4, index // 8
    ident = (eye_block, jnp.zeros_like(piece_map[1]))

    def pick(flag, a, b):
        return jax.tree.map(lambda u, v: jnp.where(flag, u, v), a, b)

    def sent(value, pairs, kind):
        got = lax.ppermute(jax.tree.map(lambda a: a.astype(kind), value), "req", pairs)
        return jax.tree.map(lambda a: a.astype(jnp.float32), got)

    other = sent(piece_map, [(r, r ^ 1) for r in range(count)], jnp.float32)
    first = core == 0
    chip_total = pick(first, combine_maps(piece_map, other), combine_maps(other, piece_map))
    in_chip = pick(first, ident, other)

    def row_of(r):
        return (r // 8, (r // 2) % 4, r % 2)

    row_got = [chip_total]
    for s in range(1, 4):
        pairs = []
        for r in range(count):
            z, x, c = row_of(r)
            pairs.append((r, z * 8 + ((x + s) % 4) * 2 + c))
        row_got.append(sent(chip_total, pairs, jnp.bfloat16))
    row_total = None
    in_row = ident
    for place in range(4):
        value = jax.tree.map(
            lambda *parts: jnp.stack(parts)[(across - place) % 4], *row_got
        )
        row_total = value if row_total is None else combine_maps(row_total, value)
        if place < 3:
            in_row = pick(place < across, combine_maps(in_row, value), in_row)

    below = ident
    for s in (3, 2, 1):
        pairs = []
        for r in range(count):
            z, x, c = row_of(r)
            if z + s < count // 8:
                pairs.append((r, r + 8 * s))
        value = sent(row_total, pairs, jnp.bfloat16)
        below = pick(down >= s, combine_maps(below, value), below)

    linear, additive = combine_maps(below, in_row)
    return (
        jnp.einsum("baf,bfu->bau", in_chip[0], additive, precision=maximal_matmul_accuracy)
        + in_chip[1]
    )


def gather_rows(share, axis):
    count, index = lax.axis_size(axis), lax.axis_index(axis)
    pieces = [share] + [
        lax.ppermute(share, axis, [(j, (j - s) % count) for j in range(count)])
        for s in range(1, count)
    ]
    return jnp.roll(jnp.stack(pieces), index, axis=0).reshape((-1,) + share.shape[1:])


def scatter_sum(full, axis):
    count, index = lax.axis_size(axis), lax.axis_index(axis)
    rows = full.shape[0] // count
    total = lax.dynamic_slice_in_dim(full, index * rows, rows, 0).astype(jnp.float32)
    for s in range(1, count):
        part = lax.dynamic_slice_in_dim(full, ((index + s) % count) * rows, rows, 0)
        got = lax.ppermute(part, axis, [(j, (j + s) % count) for j in range(count)])
        total = total + got.astype(jnp.float32)
    return total


def rms_scale(values, gain):
    mean_square = jnp.mean(values * values, axis=-1, keepdims=True)
    return values / jnp.sqrt(mean_square + 1e-06) * gain


def unit_norm(values):
    return values / jnp.sqrt(jnp.sum(values * values, axis=-1, keepdims=True) + 1e-06)


def segment_of(positions, lengths):
    bounds = jnp.cumsum(lengths)[:-1]
    return jnp.sum((positions[:, None] >= bounds[None, :]).astype(jnp.int32), axis=1)


def causal_conv(projected, rim_rows, kernel, segment_ids, rim_segments):
    taps_count = kernel.shape[0]
    row_count = projected.shape[0]
    extended = jnp.concatenate([rim_rows, projected], axis=0).astype(jnp.float32)
    extended_ids = jnp.concatenate([rim_segments, segment_ids], axis=0)
    accumulated = jnp.zeros(projected.shape, jnp.float32)
    for offset in range(taps_count):
        window = lax.slice_in_dim(extended, offset, offset + row_count, axis=0)
        window_ids = lax.slice_in_dim(extended_ids, offset, offset + row_count, axis=0)
        same_doc = (window_ids == segment_ids)[:, None]
        accumulated = accumulated + kernel[offset][None, :] * jnp.where(same_doc, window, 0.0)
    return accumulated


def unit_lower_inverse(system):
    size = system.shape[-1]
    rows = jnp.arange(size)[:, None]
    cols = jnp.arange(size)[None, :]
    inverse = jnp.broadcast_to(jnp.eye(size, dtype=system.dtype), system.shape)
    block = 1
    while block < size:
        lower_left = (
            (rows // (2 * block) == cols // (2 * block))
            & ((rows // block) % 2 == 1)
            & ((cols // block) % 2 == 0)
        )
        coupling = jnp.where(lower_left, system, 0.0)
        joined = jnp.einsum(
            "hij,hjk->hik",
            jnp.einsum("hij,hjk->hik", inverse, coupling, precision=maximal_matmul_accuracy),
            inverse,
            precision=maximal_matmul_accuracy,
        )
        inverse = inverse - joined
        block *= 2
    return inverse


def group_parts(query_vecs, key_vecs, value_vecs, beta_vals, log_decay, segment_ids, prior_segment):
    group_rows = query_vecs.shape[0]
    value_dim = value_vecs.shape[-1]
    cumulative = jnp.cumsum(log_decay, axis=0)
    row_index = jnp.arange(group_rows)[:, None]
    col_index = jnp.arange(group_rows)[None, :]
    same_doc = segment_ids[:, None] == segment_ids[None, :]
    keep_mask = ((row_index >= col_index) & same_doc)[None, :, :]
    strict_mask = (row_index > col_index)[None, :, :]
    head_cumul = jnp.transpose(cumulative)
    gaps = head_cumul[:, :, None] - head_cumul[:, None, :]
    weights = jnp.where(keep_mask, jnp.exp(jnp.where(keep_mask, gaps, 0.0)), 0.0)
    open_mask = (segment_ids == prior_segment).astype(query_vecs.dtype)
    start_decay = jnp.exp(cumulative) * open_mask[:, None]
    key_dots = jnp.einsum("ihd,jhd->hij", key_vecs, key_vecs, precision=maximal_matmul_accuracy)
    coupling = jnp.where(
        strict_mask, jnp.transpose(beta_vals)[:, :, None] * weights * key_dots, 0.0
    )
    system = coupling + jnp.eye(group_rows, dtype=query_vecs.dtype)[None]
    targets = jnp.concatenate(
        [beta_vals[:, :, None] * value_vecs, (beta_vals * start_decay)[:, :, None] * key_vecs],
        axis=-1,
    )
    solved = jnp.einsum(
        "hij,hjc->hic",
        unit_lower_inverse(system),
        jnp.transpose(targets, (1, 0, 2)),
        precision=maximal_matmul_accuracy,
    )
    starting_value_rows = solved[:, :, :value_dim]
    delta_correction = solved[:, :, value_dim:]
    query_dots = weights * jnp.einsum(
        "ihd,jhd->hij", query_vecs, key_vecs, precision=maximal_matmul_accuracy
    )
    query_begin_offset = query_vecs * start_decay[:, :, None]
    final_key_rows = key_vecs * jnp.transpose(weights[:, -1, :])[:, :, None]
    carried_decay_factor = start_decay[-1]
    return (
        starting_value_rows,
        delta_correction,
        query_dots,
        query_begin_offset,
        final_key_rows,
        carried_decay_factor,
    )


def group_step(running_state, parts):
    (
        starting_value_rows,
        delta_correction,
        query_dots,
        query_begin_offset,
        final_key_rows,
        carried_decay_factor,
    ) = parts
    fresh_state_update = starting_value_rows - jnp.einsum(
        "mxf,mft->mxt", delta_correction, running_state, precision=maximal_matmul_accuracy
    )
    output_rows = jnp.einsum(
        "fob,obt->fot", query_begin_offset, running_state, precision=maximal_matmul_accuracy
    )
    output_rows = output_rows + jnp.einsum(
        "hij,hjv->ihv", query_dots, fresh_state_update, precision=maximal_matmul_accuracy
    )
    updated_state = carried_decay_factor[:, None, None] * running_state + jnp.einsum(
        "new,enr->ewr", final_key_rows, fresh_state_update, precision=maximal_matmul_accuracy
    )
    return (updated_state, output_rows)


def combine_maps(earlier, later):
    earlier_map, preceding_additive = earlier
    following_linear_map, following_additive = later
    joined_map = jnp.einsum(
        "hkl,hlm->hkm", following_linear_map, earlier_map, precision=maximal_matmul_accuracy
    )
    joined_add = (
        jnp.einsum(
            "baf,bfu->bau",
            following_linear_map,
            preceding_additive,
            precision=maximal_matmul_accuracy,
        )
        + following_additive
    )
    return (joined_map, joined_add)


def per_device(
    tokens,
    lengths,
    in_gain,
    w_query,
    w_key,
    w_value,
    w_gate,
    w_beta,
    w_decay,
    decay_log,
    decay_bias,
    conv_query,
    conv_key,
    conv_value,
    head_gain,
    w_out,
    mlp_gain,
    w_up_gate,
    w_up,
    w_down,
):
    share_rows = tokens.shape[0]
    gathered = gather_rows(tokens, "mlp")
    piece_len = gathered.shape[0]
    head_count = w_beta.shape[1]
    key_dim = w_query.shape[1] // head_count
    value_dim = w_value.shape[1] // head_count
    taps_count = conv_query.shape[0]
    group_count = piece_len // GROUP
    piece_start = lax.axis_index("req") * piece_len
    positions = piece_start + jnp.arange(piece_len, dtype=jnp.int32)
    segment_ids = segment_of(positions, lengths)
    rim_segments = segment_of(
        piece_start - (taps_count - 1) + jnp.arange(taps_count - 1, dtype=jnp.int32), lengths
    )
    token_rows = gathered.astype(jnp.float32)
    normed = rms_scale(token_rows, in_gain).astype(jnp.bfloat16)
    proj_query = jnp.dot(normed, w_query, preferred_element_type=jnp.float32).astype(jnp.bfloat16)
    proj_key = jnp.dot(normed, w_key, preferred_element_type=jnp.float32).astype(jnp.bfloat16)
    proj_value = jnp.dot(normed, w_value, preferred_element_type=jnp.float32).astype(jnp.bfloat16)
    edge_rows = jnp.concatenate(
        [
            proj_query[piece_len - taps_count + 1 :],
            proj_key[piece_len - taps_count + 1 :],
            proj_value[piece_len - taps_count + 1 :],
        ],
        axis=1,
    )
    rim_all = shifted(edge_rows, "req", 1)
    query_width = proj_query.shape[1]
    key_width = proj_key.shape[1]
    rim_query = rim_all[:, :query_width]
    rim_key = rim_all[:, query_width : query_width + key_width]
    rim_value = rim_all[:, query_width + key_width :]
    conv_q = jax.nn.silu(causal_conv(proj_query, rim_query, conv_query, segment_ids, rim_segments))
    conv_k = jax.nn.silu(causal_conv(proj_key, rim_key, conv_key, segment_ids, rim_segments))
    conv_v = jax.nn.silu(causal_conv(proj_value, rim_value, conv_value, segment_ids, rim_segments))
    query_vecs = unit_norm(conv_q.reshape(piece_len, head_count, key_dim)) * key_dim ** (-0.5)
    key_vecs = unit_norm(conv_k.reshape(piece_len, head_count, key_dim))
    value_vecs = conv_v.reshape(piece_len, head_count, value_dim)
    gate_lin = jnp.dot(normed, w_gate, preferred_element_type=jnp.float32).astype(jnp.bfloat16)
    beta_vals = jax.nn.sigmoid(jnp.dot(normed, w_beta, preferred_element_type=jnp.float32))
    log_decay = -jnp.exp(decay_log) * jax.nn.softplus(
        jnp.dot(normed, w_decay, preferred_element_type=jnp.float32) + decay_bias
    )

    def shaped(values):
        return values.reshape((group_count, GROUP) + values.shape[1:])

    prior_ids = segment_of(
        piece_start + jnp.arange(group_count, dtype=jnp.int32) * GROUP - 1, lengths
    )
    parts = jax.vmap(group_parts)(
        shaped(query_vecs),
        shaped(key_vecs),
        shaped(value_vecs),
        shaped(beta_vals),
        shaped(log_decay),
        shaped(segment_ids),
        prior_ids,
    )
    eye_block = jnp.broadcast_to(
        jnp.eye(key_dim, dtype=jnp.float32), (head_count, key_dim, key_dim)
    )
    zero_state = jnp.zeros((head_count, key_dim, value_dim), jnp.float32)

    (
        starting_value_rows,
        delta_correction,
        query_dots,
        query_begin_offset,
        final_key_rows,
        carried_decay_factor,
    ) = parts
    local_maps = carried_decay_factor[:, :, None, None] * eye_block - jnp.einsum(
        "gchk,ghcl->ghkl", final_key_rows, delta_correction, precision=maximal_matmul_accuracy
    )
    local_adds = jnp.einsum(
        "gnew,genr->gewr", final_key_rows, starting_value_rows, precision=maximal_matmul_accuracy
    )
    before = [(eye_block, zero_state)]
    for g in range(group_count):
        before.append(combine_maps(before[-1], (local_maps[g], local_adds[g])))
    start_linear = jnp.stack([m[0] for m in before[:-1]])
    start_additive = jnp.stack([m[1] for m in before[:-1]])
    state_query = query_begin_offset - jnp.einsum(
        "ghij,ghjk->gihk", query_dots, delta_correction, precision=maximal_matmul_accuracy
    )
    inner_rows = jnp.einsum(
        "ghij,ghjv->gihv", query_dots, starting_value_rows, precision=maximal_matmul_accuracy
    ) + jnp.einsum(
        "gihk,ghkv->gihv", state_query, start_additive, precision=maximal_matmul_accuracy
    )
    entry_query = jnp.einsum(
        "gihk,ghkl->gihl", state_query, start_linear, precision=maximal_matmul_accuracy
    )
    incoming = prefix_state(before[-1], eye_block)
    w_down, incoming = lax.optimization_barrier((w_down, incoming))
    output_rows = inner_rows + jnp.einsum(
        "gihk,hkv->gihv", entry_query, incoming, precision=maximal_matmul_accuracy
    )
    output_rows = output_rows.reshape(piece_len, head_count, value_dim)
    gate_vals = jax.nn.silu(gate_lin.astype(jnp.float32)).reshape(piece_len, head_count, value_dim)
    head_out = (
        (rms_scale(output_rows, head_gain) * gate_vals)
        .reshape(piece_len, head_count * value_dim)
        .astype(jnp.bfloat16)
    )
    head_out = lax.optimization_barrier(head_out)
    partial_out = jnp.dot(head_out, w_out, preferred_element_type=jnp.float32)
    attn_mine = scatter_sum(partial_out.astype(jnp.bfloat16), "mlp")
    resid_mine = tokens.astype(jnp.float32) + attn_mine
    mlp_in = gather_rows(rms_scale(resid_mine, mlp_gain).astype(jnp.bfloat16), "mlp")

    def add_rows(piece):
        return jnp.dot(mlp_in, piece, preferred_element_type=jnp.float32)

    gate_acc = add_rows(lax.all_gather(w_up_gate, "req", axis=0, tiled=True))
    up_acc = add_rows(lax.all_gather(w_up, "req", axis=0, tiled=True))
    hidden = lax.optimization_barrier((jax.nn.silu(gate_acc) * up_acc).astype(jnp.bfloat16))
    down_terms = jnp.dot(
        hidden,
        lax.all_gather(w_down, "req", axis=1, tiled=True),
        preferred_element_type=jnp.float32,
    )
    mlp_share = scatter_sum(down_terms.astype(jnp.bfloat16), "mlp")
    return (resid_mine + mlp_share).astype(jnp.bfloat16)


def solution(mesh):
    placed = (
        P(("req", "mlp"), None),
        P(),
        P(),
        P(None, "mlp"),
        P(None, "mlp"),
        P(None, "mlp"),
        P(None, "mlp"),
        P(None, "mlp"),
        P(None, "mlp"),
        P("mlp"),
        P("mlp"),
        P(None, "mlp"),
        P(None, "mlp"),
        P(None, "mlp"),
        P(),
        P("mlp", None),
        P(),
        P("req", "mlp"),
        P("req", "mlp"),
        P("mlp", "req"),
    )
    return jax.shard_map(
        per_device, mesh=mesh, in_specs=placed, out_specs=P(("req", "mlp"), None), check_vma=False
    )
```

```python
import jax
import jax.numpy as jnp
from jax import lax
from jax.sharding import PartitionSpec as P

GROUP = 64


maximal_matmul_accuracy = lax.Precision.HIGH


def shifted(value, axis, steps):
    count = lax.axis_size(axis)
    first, last = (max(0, -steps), min(count, count - steps))
    return lax.ppermute(value, axis, [(source, source + steps) for source in range(first, last)])


def carried_in(shard, axis, combine, identity):
    length, index = (lax.axis_size(axis), lax.axis_index(axis))
    everything = jax.tree.map(
        lambda part, kind: lax.all_gather(part.astype(kind), axis),
        shard,
        jax.tree.map(lambda a: jnp.bfloat16 if a.dtype == jnp.float32 else a.dtype, shard),
    )
    start = jax.tree.map(
        lambda part, zero: jnp.broadcast_to(jnp.asarray(zero, part.dtype), part.shape),
        shard,
        identity,
    )

    def step(k, before):
        reached = k < index
        new = combine(
            before, jax.tree.map(lambda part, own: part[k].astype(own.dtype), everything, shard)
        )
        return jax.tree.map(lambda a, b: jnp.where(reached, a, b), new, before)

    return lax.fori_loop(0, length, step, start)


def prefix_state(piece_map, eye_block):
    index, count = lax.axis_index("req"), lax.axis_size("req")
    core, across, down = index % 2, (index // 2) % 4, index // 8
    ident = (eye_block, jnp.zeros_like(piece_map[1]))

    def pick(flag, a, b):
        return jax.tree.map(lambda u, v: jnp.where(flag, u, v), a, b)

    def sent(value, pairs, kind):
        got = lax.ppermute(jax.tree.map(lambda a: a.astype(kind), value), "req", pairs)
        return jax.tree.map(lambda a: a.astype(jnp.float32), got)

    other = sent(piece_map, [(r, r ^ 1) for r in range(count)], jnp.float32)
    first = core == 0
    chip_total = pick(first, combine_maps(piece_map, other), combine_maps(other, piece_map))
    in_chip = pick(first, ident, other)

    def row_of(r):
        return (r // 8, (r // 2) % 4, r % 2)

    row_got = [chip_total]
    for s in range(1, 4):
        pairs = []
        for r in range(count):
            z, x, c = row_of(r)
            pairs.append((r, z * 8 + ((x + s) % 4) * 2 + c))
        row_got.append(sent(chip_total, pairs, jnp.bfloat16))
    row_total = None
    in_row = ident
    for place in range(4):
        value = jax.tree.map(
            lambda *parts: jnp.stack(parts)[(across - place) % 4], *row_got
        )
        row_total = value if row_total is None else combine_maps(row_total, value)
        if place < 3:
            in_row = pick(place < across, combine_maps(in_row, value), in_row)

    below = ident
    for s in (3, 2, 1):
        pairs = []
        for r in range(count):
            z, x, c = row_of(r)
            if z + s < count // 8:
                pairs.append((r, r + 8 * s))
        value = sent(row_total, pairs, jnp.bfloat16)
        below = pick(down >= s, combine_maps(below, value), below)

    linear, additive = combine_maps(below, in_row)
    return (
        jnp.einsum("baf,bfu->bau", in_chip[0], additive, precision=maximal_matmul_accuracy)
        + in_chip[1]
    )


def gather_rows(share, axis):
    count, index = lax.axis_size(axis), lax.axis_index(axis)
    pieces = [share] + [
        lax.ppermute(share, axis, [(j, (j - s) % count) for j in range(count)])
        for s in range(1, count)
    ]
    return jnp.roll(jnp.stack(pieces), index, axis=0).reshape((-1,) + share.shape[1:])


def scatter_sum(full, axis):
    count, index = lax.axis_size(axis), lax.axis_index(axis)
    rows = full.shape[0] // count
    total = lax.dynamic_slice_in_dim(full, index * rows, rows, 0).astype(jnp.float32)
    for s in range(1, count):
        part = lax.dynamic_slice_in_dim(full, ((index + s) % count) * rows, rows, 0)
        got = lax.ppermute(part, axis, [(j, (j + s) % count) for j in range(count)])
        total = total + got.astype(jnp.float32)
    return total


def rms_scale(values, gain):
    mean_square = jnp.mean(values * values, axis=-1, keepdims=True)
    return values / jnp.sqrt(mean_square + 1e-06) * gain


def unit_norm(values):
    return values / jnp.sqrt(jnp.sum(values * values, axis=-1, keepdims=True) + 1e-06)


def segment_of(positions, lengths):
    bounds = jnp.cumsum(lengths)[:-1]
    return jnp.sum((positions[:, None] >= bounds[None, :]).astype(jnp.int32), axis=1)


def causal_conv(projected, rim_rows, kernel, segment_ids, rim_segments):
    taps_count = kernel.shape[0]
    row_count = projected.shape[0]
    extended = jnp.concatenate([rim_rows, projected], axis=0).astype(jnp.float32)
    extended_ids = jnp.concatenate([rim_segments, segment_ids], axis=0)
    accumulated = jnp.zeros(projected.shape, jnp.float32)
    for offset in range(taps_count):
        window = lax.slice_in_dim(extended, offset, offset + row_count, axis=0)
        window_ids = lax.slice_in_dim(extended_ids, offset, offset + row_count, axis=0)
        same_doc = (window_ids == segment_ids)[:, None]
        accumulated = accumulated + kernel[offset][None, :] * jnp.where(same_doc, window, 0.0)
    return accumulated


def unit_lower_inverse(system):
    size = system.shape[-1]
    rows = jnp.arange(size)[:, None]
    cols = jnp.arange(size)[None, :]
    inverse = jnp.broadcast_to(jnp.eye(size, dtype=system.dtype), system.shape)
    block = 1
    while block < size:
        lower_left = (
            (rows // (2 * block) == cols // (2 * block))
            & ((rows // block) % 2 == 1)
            & ((cols // block) % 2 == 0)
        )
        coupling = jnp.where(lower_left, system, 0.0)
        joined = jnp.einsum(
            "hij,hjk->hik",
            jnp.einsum("hij,hjk->hik", inverse, coupling, precision=maximal_matmul_accuracy),
            inverse,
            precision=maximal_matmul_accuracy,
        )
        inverse = inverse - joined
        block *= 2
    return inverse


def group_parts(query_vecs, key_vecs, value_vecs, beta_vals, log_decay, segment_ids, prior_segment):
    group_rows = query_vecs.shape[0]
    value_dim = value_vecs.shape[-1]
    cumulative = jnp.cumsum(log_decay, axis=0)
    row_index = jnp.arange(group_rows)[:, None]
    col_index = jnp.arange(group_rows)[None, :]
    same_doc = segment_ids[:, None] == segment_ids[None, :]
    keep_mask = ((row_index >= col_index) & same_doc)[None, :, :]
    strict_mask = (row_index > col_index)[None, :, :]
    head_cumul = jnp.transpose(cumulative)
    gaps = head_cumul[:, :, None] - head_cumul[:, None, :]
    weights = jnp.where(keep_mask, jnp.exp(jnp.where(keep_mask, gaps, 0.0)), 0.0)
    open_mask = (segment_ids == prior_segment).astype(query_vecs.dtype)
    start_decay = jnp.exp(cumulative) * open_mask[:, None]
    key_dots = jnp.einsum("ihd,jhd->hij", key_vecs, key_vecs, precision=maximal_matmul_accuracy)
    coupling = jnp.where(
        strict_mask, jnp.transpose(beta_vals)[:, :, None] * weights * key_dots, 0.0
    )
    system = coupling + jnp.eye(group_rows, dtype=query_vecs.dtype)[None]
    targets = jnp.concatenate(
        [beta_vals[:, :, None] * value_vecs, (beta_vals * start_decay)[:, :, None] * key_vecs],
        axis=-1,
    )
    solved = jnp.einsum(
        "hij,hjc->hic",
        unit_lower_inverse(system),
        jnp.transpose(targets, (1, 0, 2)),
        precision=maximal_matmul_accuracy,
    )
    starting_value_rows = solved[:, :, :value_dim]
    delta_correction = solved[:, :, value_dim:]
    query_dots = weights * jnp.einsum(
        "ihd,jhd->hij", query_vecs, key_vecs, precision=maximal_matmul_accuracy
    )
    query_begin_offset = query_vecs * start_decay[:, :, None]
    final_key_rows = key_vecs * jnp.transpose(weights[:, -1, :])[:, :, None]
    carried_decay_factor = start_decay[-1]
    return (
        starting_value_rows,
        delta_correction,
        query_dots,
        query_begin_offset,
        final_key_rows,
        carried_decay_factor,
    )


def group_step(running_state, parts):
    (
        starting_value_rows,
        delta_correction,
        query_dots,
        query_begin_offset,
        final_key_rows,
        carried_decay_factor,
    ) = parts
    fresh_state_update = starting_value_rows - jnp.einsum(
        "mxf,mft->mxt", delta_correction, running_state, precision=maximal_matmul_accuracy
    )
    output_rows = jnp.einsum(
        "fob,obt->fot", query_begin_offset, running_state, precision=maximal_matmul_accuracy
    )
    output_rows = output_rows + jnp.einsum(
        "hij,hjv->ihv", query_dots, fresh_state_update, precision=maximal_matmul_accuracy
    )
    updated_state = carried_decay_factor[:, None, None] * running_state + jnp.einsum(
        "new,enr->ewr", final_key_rows, fresh_state_update, precision=maximal_matmul_accuracy
    )
    return (updated_state, output_rows)


def combine_maps(earlier, later):
    earlier_map, preceding_additive = earlier
    following_linear_map, following_additive = later
    joined_map = jnp.einsum(
        "hkl,hlm->hkm", following_linear_map, earlier_map, precision=maximal_matmul_accuracy
    )
    joined_add = (
        jnp.einsum(
            "baf,bfu->bau",
            following_linear_map,
            preceding_additive,
            precision=maximal_matmul_accuracy,
        )
        + following_additive
    )
    return (joined_map, joined_add)


def per_device(
    tokens,
    lengths,
    in_gain,
    w_query,
    w_key,
    w_value,
    w_gate,
    w_beta,
    w_decay,
    decay_log,
    decay_bias,
    conv_query,
    conv_key,
    conv_value,
    head_gain,
    w_out,
    mlp_gain,
    w_up_gate,
    w_up,
    w_down,
):
    share_rows = tokens.shape[0]
    gathered = gather_rows(tokens, "mlp")
    piece_len = gathered.shape[0]
    head_count = w_beta.shape[1]
    key_dim = w_query.shape[1] // head_count
    value_dim = w_value.shape[1] // head_count
    taps_count = conv_query.shape[0]
    group_count = piece_len // GROUP
    piece_start = lax.axis_index("req") * piece_len
    positions = piece_start + jnp.arange(piece_len, dtype=jnp.int32)
    segment_ids = segment_of(positions, lengths)
    rim_segments = segment_of(
        piece_start - (taps_count - 1) + jnp.arange(taps_count - 1, dtype=jnp.int32), lengths
    )
    token_rows = gathered.astype(jnp.float32)
    normed = rms_scale(token_rows, in_gain).astype(jnp.bfloat16)
    proj_query = jnp.dot(normed, w_query, preferred_element_type=jnp.float32).astype(jnp.bfloat16)
    proj_key = jnp.dot(normed, w_key, preferred_element_type=jnp.float32).astype(jnp.bfloat16)
    proj_value = jnp.dot(normed, w_value, preferred_element_type=jnp.float32).astype(jnp.bfloat16)
    edge_rows = jnp.concatenate(
        [
            proj_query[piece_len - taps_count + 1 :],
            proj_key[piece_len - taps_count + 1 :],
            proj_value[piece_len - taps_count + 1 :],
        ],
        axis=1,
    )
    rim_all = shifted(edge_rows, "req", 1)
    query_width = proj_query.shape[1]
    key_width = proj_key.shape[1]
    rim_query = rim_all[:, :query_width]
    rim_key = rim_all[:, query_width : query_width + key_width]
    rim_value = rim_all[:, query_width + key_width :]
    conv_q = jax.nn.silu(causal_conv(proj_query, rim_query, conv_query, segment_ids, rim_segments))
    conv_k = jax.nn.silu(causal_conv(proj_key, rim_key, conv_key, segment_ids, rim_segments))
    conv_v = jax.nn.silu(causal_conv(proj_value, rim_value, conv_value, segment_ids, rim_segments))
    query_vecs = unit_norm(conv_q.reshape(piece_len, head_count, key_dim)) * key_dim ** (-0.5)
    key_vecs = unit_norm(conv_k.reshape(piece_len, head_count, key_dim))
    value_vecs = conv_v.reshape(piece_len, head_count, value_dim)
    gate_lin = jnp.dot(normed, w_gate, preferred_element_type=jnp.float32).astype(jnp.bfloat16)
    beta_vals = jax.nn.sigmoid(jnp.dot(normed, w_beta, preferred_element_type=jnp.float32))
    log_decay = -jnp.exp(decay_log) * jax.nn.softplus(
        jnp.dot(normed, w_decay, preferred_element_type=jnp.float32) + decay_bias
    )

    def shaped(values):
        return values.reshape((group_count, GROUP) + values.shape[1:])

    prior_ids = segment_of(
        piece_start + jnp.arange(group_count, dtype=jnp.int32) * GROUP - 1, lengths
    )
    parts = jax.vmap(group_parts)(
        shaped(query_vecs),
        shaped(key_vecs),
        shaped(value_vecs),
        shaped(beta_vals),
        shaped(log_decay),
        shaped(segment_ids),
        prior_ids,
    )
    eye_block = jnp.broadcast_to(
        jnp.eye(key_dim, dtype=jnp.float32), (head_count, key_dim, key_dim)
    )
    zero_state = jnp.zeros((head_count, key_dim, value_dim), jnp.float32)

    (
        starting_value_rows,
        delta_correction,
        query_dots,
        query_begin_offset,
        final_key_rows,
        carried_decay_factor,
    ) = parts
    local_maps = carried_decay_factor[:, :, None, None] * eye_block - jnp.einsum(
        "gchk,ghcl->ghkl", final_key_rows, delta_correction, precision=maximal_matmul_accuracy
    )
    local_adds = jnp.einsum(
        "gnew,genr->gewr", final_key_rows, starting_value_rows, precision=maximal_matmul_accuracy
    )
    before = [(eye_block, zero_state)]
    for g in range(group_count):
        before.append(combine_maps(before[-1], (local_maps[g], local_adds[g])))
    start_linear = jnp.stack([m[0] for m in before[:-1]])
    start_additive = jnp.stack([m[1] for m in before[:-1]])
    state_query = query_begin_offset - jnp.einsum(
        "ghij,ghjk->gihk", query_dots, delta_correction, precision=maximal_matmul_accuracy
    )
    inner_rows = jnp.einsum(
        "ghij,ghjv->gihv", query_dots, starting_value_rows, precision=maximal_matmul_accuracy
    ) + jnp.einsum(
        "gihk,ghkv->gihv", state_query, start_additive, precision=maximal_matmul_accuracy
    )
    entry_query = jnp.einsum(
        "gihk,ghkl->gihl", state_query, start_linear, precision=maximal_matmul_accuracy
    )
    incoming = prefix_state(before[-1], eye_block)
    w_down, incoming = lax.optimization_barrier((w_down, incoming))
    output_rows = inner_rows + jnp.einsum(
        "gihk,hkv->gihv", entry_query, incoming, precision=maximal_matmul_accuracy
    )
    output_rows = output_rows.reshape(piece_len, head_count, value_dim)
    gate_vals = jax.nn.silu(gate_lin.astype(jnp.float32)).reshape(piece_len, head_count, value_dim)
    head_out = (
        (rms_scale(output_rows, head_gain) * gate_vals)
        .reshape(piece_len, head_count * value_dim)
        .astype(jnp.bfloat16)
    )
    head_out = lax.optimization_barrier(head_out)
    partial_out = jnp.dot(head_out, w_out, preferred_element_type=jnp.float32)
    attn_mine = scatter_sum(partial_out.astype(jnp.bfloat16), "mlp")
    resid_mine = tokens.astype(jnp.float32) + attn_mine
    mlp_in = gather_rows(rms_scale(resid_mine, mlp_gain).astype(jnp.bfloat16), "mlp")

    def add_rows(piece):
        return jnp.dot(mlp_in, piece, preferred_element_type=jnp.float32)

    gate_acc = add_rows(lax.all_gather(w_up_gate, "req", axis=0, tiled=True))
    up_acc = add_rows(lax.all_gather(w_up, "req", axis=0, tiled=True))
    hidden = (jax.nn.silu(gate_acc) * up_acc).astype(jnp.bfloat16)
    down_terms = jnp.dot(
        hidden,
        lax.all_gather(w_down, "req", axis=1, tiled=True),
        preferred_element_type=jnp.float32,
    )
    mlp_share = scatter_sum(down_terms.astype(jnp.bfloat16), "mlp")
    return (resid_mine + mlp_share).astype(jnp.bfloat16)


def solution(mesh):
    placed = (
        P(("req", "mlp"), None),
        P(),
        P(),
        P(None, "mlp"),
        P(None, "mlp"),
        P(None, "mlp"),
        P(None, "mlp"),
        P(None, "mlp"),
        P(None, "mlp"),
        P("mlp"),
        P("mlp"),
        P(None, "mlp"),
        P(None, "mlp"),
        P(None, "mlp"),
        P(),
        P("mlp", None),
        P(),
        P("req", "mlp"),
        P("req", "mlp"),
        P("mlp", "req"),
    )
    return jax.shard_map(
        per_device, mesh=mesh, in_specs=placed, out_specs=P(("req", "mlp"), None), check_vma=False
    )
```

```python
import jax
import jax.numpy as jnp
from jax import lax
from jax.sharding import PartitionSpec as P

GROUP = 64


maximal_matmul_accuracy = lax.Precision.HIGH


def shifted(value, axis, steps):
    count = lax.axis_size(axis)
    first, last = (max(0, -steps), min(count, count - steps))
    return lax.ppermute(value, axis, [(source, source + steps) for source in range(first, last)])


def carried_in(shard, axis, combine, identity):
    length, index = (lax.axis_size(axis), lax.axis_index(axis))
    everything = jax.tree.map(
        lambda part, kind: lax.all_gather(part.astype(kind), axis),
        shard,
        jax.tree.map(lambda a: jnp.bfloat16 if a.dtype == jnp.float32 else a.dtype, shard),
    )
    start = jax.tree.map(
        lambda part, zero: jnp.broadcast_to(jnp.asarray(zero, part.dtype), part.shape),
        shard,
        identity,
    )

    def step(k, before):
        reached = k < index
        new = combine(
            before, jax.tree.map(lambda part, own: part[k].astype(own.dtype), everything, shard)
        )
        return jax.tree.map(lambda a, b: jnp.where(reached, a, b), new, before)

    return lax.fori_loop(0, length, step, start)


def prefix_state(piece_map, eye_block):
    index, count = lax.axis_index("req"), lax.axis_size("req")
    core, across, down = index % 2, (index // 2) % 4, index // 8
    ident = (eye_block, jnp.zeros_like(piece_map[1]))

    def pick(flag, a, b):
        return jax.tree.map(lambda u, v: jnp.where(flag, u, v), a, b)

    def sent(value, pairs, kind):
        got = lax.ppermute(jax.tree.map(lambda a: a.astype(kind), value), "req", pairs)
        return jax.tree.map(lambda a: a.astype(jnp.float32), got)

    other = sent(piece_map, [(r, r ^ 1) for r in range(count)], jnp.float32)
    first = core == 0
    chip_total = pick(first, combine_maps(piece_map, other), combine_maps(other, piece_map))
    in_chip = pick(first, ident, other)

    def row_of(r):
        return (r // 8, (r // 2) % 4, r % 2)

    row_got = [chip_total]
    for s in range(1, 4):
        pairs = []
        for r in range(count):
            z, x, c = row_of(r)
            pairs.append((r, z * 8 + ((x + s) % 4) * 2 + c))
        row_got.append(sent(chip_total, pairs, jnp.bfloat16))
    row_total = None
    in_row = ident
    for place in range(4):
        value = jax.tree.map(
            lambda *parts: jnp.stack(parts)[(across - place) % 4], *row_got
        )
        row_total = value if row_total is None else combine_maps(row_total, value)
        if place < 3:
            in_row = pick(place < across, combine_maps(in_row, value), in_row)

    below = ident
    for s in (3, 2, 1):
        pairs = []
        for r in range(count):
            z, x, c = row_of(r)
            if z + s < count // 8:
                pairs.append((r, r + 8 * s))
        value = sent(row_total, pairs, jnp.bfloat16)
        below = pick(down >= s, combine_maps(below, value), below)

    linear, additive = combine_maps(below, in_row)
    return (
        jnp.einsum("baf,bfu->bau", in_chip[0], additive, precision=maximal_matmul_accuracy)
        + in_chip[1]
    )


def gather_rows(share, axis):
    count, index = lax.axis_size(axis), lax.axis_index(axis)
    pieces = [share] + [
        lax.ppermute(share, axis, [(j, (j - s) % count) for j in range(count)])
        for s in range(1, count)
    ]
    return jnp.roll(jnp.stack(pieces), index, axis=0).reshape((-1,) + share.shape[1:])


def scatter_sum(full, axis):
    count, index = lax.axis_size(axis), lax.axis_index(axis)
    rows = full.shape[0] // count
    total = lax.dynamic_slice_in_dim(full, index * rows, rows, 0).astype(jnp.float32)
    for s in range(1, count):
        part = lax.dynamic_slice_in_dim(full, ((index + s) % count) * rows, rows, 0)
        got = lax.ppermute(part, axis, [(j, (j + s) % count) for j in range(count)])
        total = total + got.astype(jnp.float32)
    return total


def rms_scale(values, gain):
    mean_square = jnp.mean(values * values, axis=-1, keepdims=True)
    return values / jnp.sqrt(mean_square + 1e-06) * gain


def unit_norm(values):
    return values / jnp.sqrt(jnp.sum(values * values, axis=-1, keepdims=True) + 1e-06)


def segment_of(positions, lengths):
    bounds = jnp.cumsum(lengths)[:-1]
    return jnp.sum((positions[:, None] >= bounds[None, :]).astype(jnp.int32), axis=1)


def causal_conv(projected, rim_rows, kernel, segment_ids, rim_segments):
    taps_count = kernel.shape[0]
    row_count = projected.shape[0]
    extended = jnp.concatenate([rim_rows, projected], axis=0).astype(jnp.float32)
    extended_ids = jnp.concatenate([rim_segments, segment_ids], axis=0)
    accumulated = jnp.zeros(projected.shape, jnp.float32)
    for offset in range(taps_count):
        window = lax.slice_in_dim(extended, offset, offset + row_count, axis=0)
        window_ids = lax.slice_in_dim(extended_ids, offset, offset + row_count, axis=0)
        same_doc = (window_ids == segment_ids)[:, None]
        accumulated = accumulated + kernel[offset][None, :] * jnp.where(same_doc, window, 0.0)
    return accumulated


def unit_lower_inverse(system):
    size = system.shape[-1]
    rows = jnp.arange(size)[:, None]
    cols = jnp.arange(size)[None, :]
    inverse = jnp.broadcast_to(jnp.eye(size, dtype=system.dtype), system.shape)
    block = 1
    while block < size:
        lower_left = (
            (rows // (2 * block) == cols // (2 * block))
            & ((rows // block) % 2 == 1)
            & ((cols // block) % 2 == 0)
        )
        coupling = jnp.where(lower_left, system, 0.0)
        joined = jnp.einsum(
            "hij,hjk->hik",
            jnp.einsum("hij,hjk->hik", inverse, coupling, precision=maximal_matmul_accuracy),
            inverse,
            precision=maximal_matmul_accuracy,
        )
        inverse = inverse - joined
        block *= 2
    return inverse


def group_parts(query_vecs, key_vecs, value_vecs, beta_vals, log_decay, segment_ids, prior_segment):
    group_rows = query_vecs.shape[0]
    value_dim = value_vecs.shape[-1]
    cumulative = jnp.cumsum(log_decay, axis=0)
    row_index = jnp.arange(group_rows)[:, None]
    col_index = jnp.arange(group_rows)[None, :]
    same_doc = segment_ids[:, None] == segment_ids[None, :]
    keep_mask = ((row_index >= col_index) & same_doc)[None, :, :]
    strict_mask = (row_index > col_index)[None, :, :]
    head_cumul = jnp.transpose(cumulative)
    gaps = head_cumul[:, :, None] - head_cumul[:, None, :]
    weights = jnp.where(keep_mask, jnp.exp(jnp.where(keep_mask, gaps, 0.0)), 0.0)
    open_mask = (segment_ids == prior_segment).astype(query_vecs.dtype)
    start_decay = jnp.exp(cumulative) * open_mask[:, None]
    key_dots = jnp.einsum("ihd,jhd->hij", key_vecs, key_vecs, precision=maximal_matmul_accuracy)
    coupling = jnp.where(
        strict_mask, jnp.transpose(beta_vals)[:, :, None] * weights * key_dots, 0.0
    )
    system = coupling + jnp.eye(group_rows, dtype=query_vecs.dtype)[None]
    targets = jnp.concatenate(
        [beta_vals[:, :, None] * value_vecs, (beta_vals * start_decay)[:, :, None] * key_vecs],
        axis=-1,
    )
    solved = jnp.einsum(
        "hij,hjc->hic",
        unit_lower_inverse(system),
        jnp.transpose(targets, (1, 0, 2)),
        precision=maximal_matmul_accuracy,
    )
    starting_value_rows = solved[:, :, :value_dim]
    delta_correction = solved[:, :, value_dim:]
    query_dots = weights * jnp.einsum(
        "ihd,jhd->hij", query_vecs, key_vecs, precision=maximal_matmul_accuracy
    )
    query_begin_offset = query_vecs * start_decay[:, :, None]
    final_key_rows = key_vecs * jnp.transpose(weights[:, -1, :])[:, :, None]
    carried_decay_factor = start_decay[-1]
    return (
        starting_value_rows,
        delta_correction,
        query_dots,
        query_begin_offset,
        final_key_rows,
        carried_decay_factor,
    )


def group_step(running_state, parts):
    (
        starting_value_rows,
        delta_correction,
        query_dots,
        query_begin_offset,
        final_key_rows,
        carried_decay_factor,
    ) = parts
    fresh_state_update = starting_value_rows - jnp.einsum(
        "mxf,mft->mxt", delta_correction, running_state, precision=maximal_matmul_accuracy
    )
    output_rows = jnp.einsum(
        "fob,obt->fot", query_begin_offset, running_state, precision=maximal_matmul_accuracy
    )
    output_rows = output_rows + jnp.einsum(
        "hij,hjv->ihv", query_dots, fresh_state_update, precision=maximal_matmul_accuracy
    )
    updated_state = carried_decay_factor[:, None, None] * running_state + jnp.einsum(
        "new,enr->ewr", final_key_rows, fresh_state_update, precision=maximal_matmul_accuracy
    )
    return (updated_state, output_rows)


def combine_maps(earlier, later):
    earlier_map, preceding_additive = earlier
    following_linear_map, following_additive = later
    joined_map = jnp.einsum(
        "hkl,hlm->hkm", following_linear_map, earlier_map, precision=maximal_matmul_accuracy
    )
    joined_add = (
        jnp.einsum(
            "baf,bfu->bau",
            following_linear_map,
            preceding_additive,
            precision=maximal_matmul_accuracy,
        )
        + following_additive
    )
    return (joined_map, joined_add)


def per_device(
    tokens,
    lengths,
    in_gain,
    w_query,
    w_key,
    w_value,
    w_gate,
    w_beta,
    w_decay,
    decay_log,
    decay_bias,
    conv_query,
    conv_key,
    conv_value,
    head_gain,
    w_out,
    mlp_gain,
    w_up_gate,
    w_up,
    w_down,
):
    share_rows = tokens.shape[0]
    gathered = gather_rows(tokens, "mlp")
    piece_len = gathered.shape[0]
    head_count = w_beta.shape[1]
    key_dim = w_query.shape[1] // head_count
    value_dim = w_value.shape[1] // head_count
    taps_count = conv_query.shape[0]
    group_count = piece_len // GROUP
    piece_start = lax.axis_index("req") * piece_len
    positions = piece_start + jnp.arange(piece_len, dtype=jnp.int32)
    segment_ids = segment_of(positions, lengths)
    rim_segments = segment_of(
        piece_start - (taps_count - 1) + jnp.arange(taps_count - 1, dtype=jnp.int32), lengths
    )
    token_rows = gathered.astype(jnp.float32)
    normed = lax.optimization_barrier(rms_scale(token_rows, in_gain).astype(jnp.bfloat16))
    proj_query = jnp.dot(normed, w_query, preferred_element_type=jnp.float32).astype(jnp.bfloat16)
    proj_key = jnp.dot(normed, w_key, preferred_element_type=jnp.float32).astype(jnp.bfloat16)
    proj_value = jnp.dot(normed, w_value, preferred_element_type=jnp.float32).astype(jnp.bfloat16)
    edge_rows = jnp.concatenate(
        [
            proj_query[piece_len - taps_count + 1 :],
            proj_key[piece_len - taps_count + 1 :],
            proj_value[piece_len - taps_count + 1 :],
        ],
        axis=1,
    )
    rim_all = shifted(edge_rows, "req", 1)
    query_width = proj_query.shape[1]
    key_width = proj_key.shape[1]
    rim_query = rim_all[:, :query_width]
    rim_key = rim_all[:, query_width : query_width + key_width]
    rim_value = rim_all[:, query_width + key_width :]
    conv_q = jax.nn.silu(causal_conv(proj_query, rim_query, conv_query, segment_ids, rim_segments))
    conv_k = jax.nn.silu(causal_conv(proj_key, rim_key, conv_key, segment_ids, rim_segments))
    conv_v = jax.nn.silu(causal_conv(proj_value, rim_value, conv_value, segment_ids, rim_segments))
    query_vecs = unit_norm(conv_q.reshape(piece_len, head_count, key_dim)) * key_dim ** (-0.5)
    key_vecs = unit_norm(conv_k.reshape(piece_len, head_count, key_dim))
    value_vecs = conv_v.reshape(piece_len, head_count, value_dim)
    gate_lin = jnp.dot(normed, w_gate, preferred_element_type=jnp.float32).astype(jnp.bfloat16)
    beta_vals = jax.nn.sigmoid(jnp.dot(normed, w_beta, preferred_element_type=jnp.float32))
    log_decay = -jnp.exp(decay_log) * jax.nn.softplus(
        jnp.dot(normed, w_decay, preferred_element_type=jnp.float32) + decay_bias
    )

    def shaped(values):
        return values.reshape((group_count, GROUP) + values.shape[1:])

    prior_ids = segment_of(
        piece_start + jnp.arange(group_count, dtype=jnp.int32) * GROUP - 1, lengths
    )
    parts = jax.vmap(group_parts)(
        shaped(query_vecs),
        shaped(key_vecs),
        shaped(value_vecs),
        shaped(beta_vals),
        shaped(log_decay),
        shaped(segment_ids),
        prior_ids,
    )
    eye_block = jnp.broadcast_to(
        jnp.eye(key_dim, dtype=jnp.float32), (head_count, key_dim, key_dim)
    )
    zero_state = jnp.zeros((head_count, key_dim, value_dim), jnp.float32)

    (
        starting_value_rows,
        delta_correction,
        query_dots,
        query_begin_offset,
        final_key_rows,
        carried_decay_factor,
    ) = parts
    local_maps = carried_decay_factor[:, :, None, None] * eye_block - jnp.einsum(
        "gchk,ghcl->ghkl", final_key_rows, delta_correction, precision=maximal_matmul_accuracy
    )
    local_adds = jnp.einsum(
        "gnew,genr->gewr", final_key_rows, starting_value_rows, precision=maximal_matmul_accuracy
    )
    before = [(eye_block, zero_state)]
    for g in range(group_count):
        before.append(combine_maps(before[-1], (local_maps[g], local_adds[g])))
    start_linear = jnp.stack([m[0] for m in before[:-1]])
    start_additive = jnp.stack([m[1] for m in before[:-1]])
    state_query = query_begin_offset - jnp.einsum(
        "ghij,ghjk->gihk", query_dots, delta_correction, precision=maximal_matmul_accuracy
    )
    inner_rows = jnp.einsum(
        "ghij,ghjv->gihv", query_dots, starting_value_rows, precision=maximal_matmul_accuracy
    ) + jnp.einsum(
        "gihk,ghkv->gihv", state_query, start_additive, precision=maximal_matmul_accuracy
    )
    entry_query = jnp.einsum(
        "gihk,ghkl->gihl", state_query, start_linear, precision=maximal_matmul_accuracy
    )
    incoming = prefix_state(before[-1], eye_block)
    w_down, incoming = lax.optimization_barrier((w_down, incoming))
    output_rows = inner_rows + jnp.einsum(
        "gihk,hkv->gihv", entry_query, incoming, precision=maximal_matmul_accuracy
    )
    output_rows = output_rows.reshape(piece_len, head_count, value_dim)
    gate_vals = jax.nn.silu(gate_lin.astype(jnp.float32)).reshape(piece_len, head_count, value_dim)
    head_out = (
        (rms_scale(output_rows, head_gain) * gate_vals)
        .reshape(piece_len, head_count * value_dim)
        .astype(jnp.bfloat16)
    )
    head_out = lax.optimization_barrier(head_out)
    partial_out = jnp.dot(head_out, w_out, preferred_element_type=jnp.float32)
    attn_mine = scatter_sum(partial_out.astype(jnp.bfloat16), "mlp")
    resid_mine = tokens.astype(jnp.float32) + attn_mine
    mlp_in = gather_rows(rms_scale(resid_mine, mlp_gain).astype(jnp.bfloat16), "mlp")

    def add_rows(piece):
        return jnp.dot(mlp_in, piece, preferred_element_type=jnp.float32)

    gate_acc = add_rows(lax.all_gather(w_up_gate, "req", axis=0, tiled=True))
    up_acc = add_rows(lax.all_gather(w_up, "req", axis=0, tiled=True))
    hidden = (jax.nn.silu(gate_acc) * up_acc).astype(jnp.bfloat16)
    down_terms = jnp.dot(
        hidden,
        lax.all_gather(w_down, "req", axis=1, tiled=True),
        preferred_element_type=jnp.float32,
    )
    mlp_share = scatter_sum(down_terms.astype(jnp.bfloat16), "mlp")
    return (resid_mine + mlp_share).astype(jnp.bfloat16)


def solution(mesh):
    placed = (
        P(("req", "mlp"), None),
        P(),
        P(),
        P(None, "mlp"),
        P(None, "mlp"),
        P(None, "mlp"),
        P(None, "mlp"),
        P(None, "mlp"),
        P(None, "mlp"),
        P("mlp"),
        P("mlp"),
        P(None, "mlp"),
        P(None, "mlp"),
        P(None, "mlp"),
        P(),
        P("mlp", None),
        P(),
        P("req", "mlp"),
        P("req", "mlp"),
        P("mlp", "req"),
    )
    return jax.shard_map(
        per_device, mesh=mesh, in_specs=placed, out_specs=P(("req", "mlp"), None), check_vma=False
    )
```

```python
import jax
import jax.numpy as jnp
from jax import lax
from jax.sharding import PartitionSpec as P

GROUP = 64


maximal_matmul_accuracy = lax.Precision.HIGH


def shifted(value, axis, steps):
    count = lax.axis_size(axis)
    first, last = (max(0, -steps), min(count, count - steps))
    return lax.ppermute(value, axis, [(source, source + steps) for source in range(first, last)])


def carried_in(shard, axis, combine, identity):
    length, index = (lax.axis_size(axis), lax.axis_index(axis))
    everything = jax.tree.map(
        lambda part, kind: lax.all_gather(part.astype(kind), axis),
        shard,
        jax.tree.map(lambda a: jnp.bfloat16 if a.dtype == jnp.float32 else a.dtype, shard),
    )
    start = jax.tree.map(
        lambda part, zero: jnp.broadcast_to(jnp.asarray(zero, part.dtype), part.shape),
        shard,
        identity,
    )

    def step(k, before):
        reached = k < index
        new = combine(
            before, jax.tree.map(lambda part, own: part[k].astype(own.dtype), everything, shard)
        )
        return jax.tree.map(lambda a, b: jnp.where(reached, a, b), new, before)

    return lax.fori_loop(0, length, step, start)


def prefix_state(piece_map, eye_block):
    index, count = lax.axis_index("req"), lax.axis_size("req")
    core, across, down = index % 2, (index // 2) % 4, index // 8
    ident = (eye_block, jnp.zeros_like(piece_map[1]))

    def pick(flag, a, b):
        return jax.tree.map(lambda u, v: jnp.where(flag, u, v), a, b)

    def sent(value, pairs, kind):
        got = lax.ppermute(jax.tree.map(lambda a: a.astype(kind), value), "req", pairs)
        return jax.tree.map(lambda a: a.astype(jnp.float32), got)

    other = sent(piece_map, [(r, r ^ 1) for r in range(count)], jnp.float32)
    first = core == 0
    chip_total = pick(first, combine_maps(piece_map, other), combine_maps(other, piece_map))
    in_chip = pick(first, ident, other)

    def row_of(r):
        return (r // 8, (r // 2) % 4, r % 2)

    row_got = [chip_total]
    for s in range(1, 4):
        pairs = []
        for r in range(count):
            z, x, c = row_of(r)
            pairs.append((r, z * 8 + ((x + s) % 4) * 2 + c))
        row_got.append(sent(chip_total, pairs, jnp.bfloat16))
    row_total = None
    in_row = ident
    for place in range(4):
        value = jax.tree.map(
            lambda *parts: jnp.stack(parts)[(across - place) % 4], *row_got
        )
        row_total = value if row_total is None else combine_maps(row_total, value)
        if place < 3:
            in_row = pick(place < across, combine_maps(in_row, value), in_row)

    below = ident
    for s in (3, 2, 1):
        pairs = []
        for r in range(count):
            z, x, c = row_of(r)
            if z + s < count // 8:
                pairs.append((r, r + 8 * s))
        value = sent(row_total, pairs, jnp.bfloat16)
        below = pick(down >= s, combine_maps(below, value), below)

    linear, additive = combine_maps(below, in_row)
    return (
        jnp.einsum("baf,bfu->bau", in_chip[0], additive, precision=maximal_matmul_accuracy)
        + in_chip[1]
    )


def gather_rows(share, axis):
    count, index = lax.axis_size(axis), lax.axis_index(axis)
    pieces = [share] + [
        lax.ppermute(share, axis, [(j, (j - s) % count) for j in range(count)])
        for s in range(1, count)
    ]
    return jnp.roll(jnp.stack(pieces), index, axis=0).reshape((-1,) + share.shape[1:])


def scatter_sum(full, axis):
    count, index = lax.axis_size(axis), lax.axis_index(axis)
    rows = full.shape[0] // count
    total = lax.dynamic_slice_in_dim(full, index * rows, rows, 0).astype(jnp.float32)
    for s in range(1, count):
        part = lax.dynamic_slice_in_dim(full, ((index + s) % count) * rows, rows, 0)
        got = lax.ppermute(part, axis, [(j, (j + s) % count) for j in range(count)])
        total = total + got.astype(jnp.float32)
    return total


def rms_scale(values, gain):
    mean_square = jnp.mean(values * values, axis=-1, keepdims=True)
    return values / jnp.sqrt(mean_square + 1e-06) * gain


def unit_norm(values):
    return values / jnp.sqrt(jnp.sum(values * values, axis=-1, keepdims=True) + 1e-06)


def segment_of(positions, lengths):
    bounds = jnp.cumsum(lengths)[:-1]
    return jnp.sum((positions[:, None] >= bounds[None, :]).astype(jnp.int32), axis=1)


def causal_conv(projected, rim_rows, kernel, segment_ids, rim_segments):
    taps_count = kernel.shape[0]
    row_count = projected.shape[0]
    extended = jnp.concatenate([rim_rows, projected], axis=0).astype(jnp.float32)
    extended_ids = jnp.concatenate([rim_segments, segment_ids], axis=0)
    accumulated = jnp.zeros(projected.shape, jnp.float32)
    for offset in range(taps_count):
        window = lax.slice_in_dim(extended, offset, offset + row_count, axis=0)
        window_ids = lax.slice_in_dim(extended_ids, offset, offset + row_count, axis=0)
        same_doc = (window_ids == segment_ids)[:, None]
        accumulated = accumulated + kernel[offset][None, :] * jnp.where(same_doc, window, 0.0)
    return accumulated


def unit_lower_inverse(system):
    size = system.shape[-1]
    rows = jnp.arange(size)[:, None]
    cols = jnp.arange(size)[None, :]
    inverse = jnp.broadcast_to(jnp.eye(size, dtype=system.dtype), system.shape)
    block = 1
    while block < size:
        lower_left = (
            (rows // (2 * block) == cols // (2 * block))
            & ((rows // block) % 2 == 1)
            & ((cols // block) % 2 == 0)
        )
        coupling = jnp.where(lower_left, system, 0.0)
        joined = jnp.einsum(
            "hij,hjk->hik",
            jnp.einsum("hij,hjk->hik", inverse, coupling, precision=maximal_matmul_accuracy),
            inverse,
            precision=maximal_matmul_accuracy,
        )
        inverse = inverse - joined
        block *= 2
    return inverse


def group_parts(query_vecs, key_vecs, value_vecs, beta_vals, log_decay, segment_ids, prior_segment):
    group_rows = query_vecs.shape[0]
    value_dim = value_vecs.shape[-1]
    cumulative = jnp.cumsum(log_decay, axis=0)
    row_index = jnp.arange(group_rows)[:, None]
    col_index = jnp.arange(group_rows)[None, :]
    same_doc = segment_ids[:, None] == segment_ids[None, :]
    keep_mask = ((row_index >= col_index) & same_doc)[None, :, :]
    strict_mask = (row_index > col_index)[None, :, :]
    head_cumul = jnp.transpose(cumulative)
    gaps = head_cumul[:, :, None] - head_cumul[:, None, :]
    weights = jnp.where(keep_mask, jnp.exp(jnp.where(keep_mask, gaps, 0.0)), 0.0)
    open_mask = (segment_ids == prior_segment).astype(query_vecs.dtype)
    start_decay = jnp.exp(cumulative) * open_mask[:, None]
    key_dots = jnp.einsum("ihd,jhd->hij", key_vecs, key_vecs, precision=maximal_matmul_accuracy)
    coupling = jnp.where(
        strict_mask, jnp.transpose(beta_vals)[:, :, None] * weights * key_dots, 0.0
    )
    system = coupling + jnp.eye(group_rows, dtype=query_vecs.dtype)[None]
    targets = jnp.concatenate(
        [beta_vals[:, :, None] * value_vecs, (beta_vals * start_decay)[:, :, None] * key_vecs],
        axis=-1,
    )
    solved = jnp.einsum(
        "hij,hjc->hic",
        unit_lower_inverse(system),
        jnp.transpose(targets, (1, 0, 2)),
        precision=maximal_matmul_accuracy,
    )
    starting_value_rows = solved[:, :, :value_dim]
    delta_correction = solved[:, :, value_dim:]
    query_dots = weights * jnp.einsum(
        "ihd,jhd->hij", query_vecs, key_vecs, precision=maximal_matmul_accuracy
    )
    query_begin_offset = query_vecs * start_decay[:, :, None]
    final_key_rows = key_vecs * jnp.transpose(weights[:, -1, :])[:, :, None]
    carried_decay_factor = start_decay[-1]
    return (
        starting_value_rows,
        delta_correction,
        query_dots,
        query_begin_offset,
        final_key_rows,
        carried_decay_factor,
    )


def group_step(running_state, parts):
    (
        starting_value_rows,
        delta_correction,
        query_dots,
        query_begin_offset,
        final_key_rows,
        carried_decay_factor,
    ) = parts
    fresh_state_update = starting_value_rows - jnp.einsum(
        "mxf,mft->mxt", delta_correction, running_state, precision=maximal_matmul_accuracy
    )
    output_rows = jnp.einsum(
        "fob,obt->fot", query_begin_offset, running_state, precision=maximal_matmul_accuracy
    )
    output_rows = output_rows + jnp.einsum(
        "hij,hjv->ihv", query_dots, fresh_state_update, precision=maximal_matmul_accuracy
    )
    updated_state = carried_decay_factor[:, None, None] * running_state + jnp.einsum(
        "new,enr->ewr", final_key_rows, fresh_state_update, precision=maximal_matmul_accuracy
    )
    return (updated_state, output_rows)


def combine_maps(earlier, later):
    earlier_map, preceding_additive = earlier
    following_linear_map, following_additive = later
    joined_map = jnp.einsum(
        "hkl,hlm->hkm", following_linear_map, earlier_map, precision=maximal_matmul_accuracy
    )
    joined_add = (
        jnp.einsum(
            "baf,bfu->bau",
            following_linear_map,
            preceding_additive,
            precision=maximal_matmul_accuracy,
        )
        + following_additive
    )
    return (joined_map, joined_add)


def per_device(
    tokens,
    lengths,
    in_gain,
    w_query,
    w_key,
    w_value,
    w_gate,
    w_beta,
    w_decay,
    decay_log,
    decay_bias,
    conv_query,
    conv_key,
    conv_value,
    head_gain,
    w_out,
    mlp_gain,
    w_up_gate,
    w_up,
    w_down,
):
    share_rows = tokens.shape[0]
    gathered = gather_rows(tokens, "mlp")
    piece_len = gathered.shape[0]
    head_count = w_beta.shape[1]
    key_dim = w_query.shape[1] // head_count
    value_dim = w_value.shape[1] // head_count
    taps_count = conv_query.shape[0]
    group_count = piece_len // GROUP
    piece_start = lax.axis_index("req") * piece_len
    positions = piece_start + jnp.arange(piece_len, dtype=jnp.int32)
    segment_ids = segment_of(positions, lengths)
    rim_segments = segment_of(
        piece_start - (taps_count - 1) + jnp.arange(taps_count - 1, dtype=jnp.int32), lengths
    )
    token_rows = gathered.astype(jnp.float32)
    normed = rms_scale(token_rows, in_gain).astype(jnp.bfloat16)
    proj_query = jnp.dot(normed, w_query, preferred_element_type=jnp.float32).astype(jnp.bfloat16)
    proj_key = jnp.dot(normed, w_key, preferred_element_type=jnp.float32).astype(jnp.bfloat16)
    proj_value = jnp.dot(normed, w_value, preferred_element_type=jnp.float32).astype(jnp.bfloat16)
    edge_rows = jnp.concatenate(
        [
            proj_query[piece_len - taps_count + 1 :],
            proj_key[piece_len - taps_count + 1 :],
            proj_value[piece_len - taps_count + 1 :],
        ],
        axis=1,
    )
    rim_all = shifted(edge_rows, "req", 1)
    query_width = proj_query.shape[1]
    key_width = proj_key.shape[1]
    rim_query = rim_all[:, :query_width]
    rim_key = rim_all[:, query_width : query_width + key_width]
    rim_value = rim_all[:, query_width + key_width :]
    conv_q = jax.nn.silu(causal_conv(proj_query, rim_query, conv_query, segment_ids, rim_segments))
    conv_k = jax.nn.silu(causal_conv(proj_key, rim_key, conv_key, segment_ids, rim_segments))
    conv_v = jax.nn.silu(causal_conv(proj_value, rim_value, conv_value, segment_ids, rim_segments))
    query_vecs = unit_norm(conv_q.reshape(piece_len, head_count, key_dim)) * key_dim ** (-0.5)
    key_vecs = unit_norm(conv_k.reshape(piece_len, head_count, key_dim))
    value_vecs = conv_v.reshape(piece_len, head_count, value_dim)
    query_vecs, key_vecs, value_vecs = lax.optimization_barrier((query_vecs, key_vecs, value_vecs))
    gate_lin = jnp.dot(normed, w_gate, preferred_element_type=jnp.float32).astype(jnp.bfloat16)
    beta_vals = jax.nn.sigmoid(jnp.dot(normed, w_beta, preferred_element_type=jnp.float32))
    log_decay = -jnp.exp(decay_log) * jax.nn.softplus(
        jnp.dot(normed, w_decay, preferred_element_type=jnp.float32) + decay_bias
    )

    def shaped(values):
        return values.reshape((group_count, GROUP) + values.shape[1:])

    prior_ids = segment_of(
        piece_start + jnp.arange(group_count, dtype=jnp.int32) * GROUP - 1, lengths
    )
    parts = jax.vmap(group_parts)(
        shaped(query_vecs),
        shaped(key_vecs),
        shaped(value_vecs),
        shaped(beta_vals),
        shaped(log_decay),
        shaped(segment_ids),
        prior_ids,
    )
    eye_block = jnp.broadcast_to(
        jnp.eye(key_dim, dtype=jnp.float32), (head_count, key_dim, key_dim)
    )
    zero_state = jnp.zeros((head_count, key_dim, value_dim), jnp.float32)

    (
        starting_value_rows,
        delta_correction,
        query_dots,
        query_begin_offset,
        final_key_rows,
        carried_decay_factor,
    ) = parts
    local_maps = carried_decay_factor[:, :, None, None] * eye_block - jnp.einsum(
        "gchk,ghcl->ghkl", final_key_rows, delta_correction, precision=maximal_matmul_accuracy
    )
    local_adds = jnp.einsum(
        "gnew,genr->gewr", final_key_rows, starting_value_rows, precision=maximal_matmul_accuracy
    )
    before = [(eye_block, zero_state)]
    for g in range(group_count):
        before.append(combine_maps(before[-1], (local_maps[g], local_adds[g])))
    start_linear = jnp.stack([m[0] for m in before[:-1]])
    start_additive = jnp.stack([m[1] for m in before[:-1]])
    state_query = query_begin_offset - jnp.einsum(
        "ghij,ghjk->gihk", query_dots, delta_correction, precision=maximal_matmul_accuracy
    )
    inner_rows = jnp.einsum(
        "ghij,ghjv->gihv", query_dots, starting_value_rows, precision=maximal_matmul_accuracy
    ) + jnp.einsum(
        "gihk,ghkv->gihv", state_query, start_additive, precision=maximal_matmul_accuracy
    )
    entry_query = jnp.einsum(
        "gihk,ghkl->gihl", state_query, start_linear, precision=maximal_matmul_accuracy
    )
    incoming = prefix_state(before[-1], eye_block)
    w_down, incoming = lax.optimization_barrier((w_down, incoming))
    output_rows = inner_rows + jnp.einsum(
        "gihk,hkv->gihv", entry_query, incoming, precision=maximal_matmul_accuracy
    )
    output_rows = output_rows.reshape(piece_len, head_count, value_dim)
    gate_vals = jax.nn.silu(gate_lin.astype(jnp.float32)).reshape(piece_len, head_count, value_dim)
    head_out = (
        (rms_scale(output_rows, head_gain) * gate_vals)
        .reshape(piece_len, head_count * value_dim)
        .astype(jnp.bfloat16)
    )
    head_out = lax.optimization_barrier(head_out)
    partial_out = jnp.dot(head_out, w_out, preferred_element_type=jnp.float32)
    attn_mine = scatter_sum(partial_out.astype(jnp.bfloat16), "mlp")
    resid_mine = tokens.astype(jnp.float32) + attn_mine
    mlp_in = gather_rows(rms_scale(resid_mine, mlp_gain).astype(jnp.bfloat16), "mlp")

    def add_rows(piece):
        return jnp.dot(mlp_in, piece, preferred_element_type=jnp.float32)

    gate_acc = add_rows(lax.all_gather(w_up_gate, "req", axis=0, tiled=True))
    up_acc = add_rows(lax.all_gather(w_up, "req", axis=0, tiled=True))
    hidden = (jax.nn.silu(gate_acc) * up_acc).astype(jnp.bfloat16)
    down_terms = jnp.dot(
        hidden,
        lax.all_gather(w_down, "req", axis=1, tiled=True),
        preferred_element_type=jnp.float32,
    )
    mlp_share = scatter_sum(down_terms.astype(jnp.bfloat16), "mlp")
    return (resid_mine + mlp_share).astype(jnp.bfloat16)


def solution(mesh):
    placed = (
        P(("req", "mlp"), None),
        P(),
        P(),
        P(None, "mlp"),
        P(None, "mlp"),
        P(None, "mlp"),
        P(None, "mlp"),
        P(None, "mlp"),
        P(None, "mlp"),
        P("mlp"),
        P("mlp"),
        P(None, "mlp"),
        P(None, "mlp"),
        P(None, "mlp"),
        P(),
        P("mlp", None),
        P(),
        P("req", "mlp"),
        P("req", "mlp"),
        P("mlp", "req"),
    )
    return jax.shard_map(
        per_device, mesh=mesh, in_specs=placed, out_specs=P(("req", "mlp"), None), check_vma=False
    )
```
